32 devices in a mesh: ctx: 8 (over z, x), tp: 4 (over y, core).
Axes of the slice: x: 2, y: 2, z: 4, core: 2. Of those that a mesh axis runs over, the one named last changes fastest.
Arguments:
- queries: bfloat16 [8192, 5120], P('ctx', 'tp'), may hold values from -6 to 6
- keys: bfloat16 [8192, 5120], P('ctx', 'tp'), may hold values from -6 to 6
- values: bfloat16 [8192, 5120], P('ctx', 'tp'), may hold values from -6 to 6
- gates: bfloat16 [8192, 5120], P('ctx', 'tp'), may hold values from -6 to 6
- gain: float32 [5120], P('tp'), may hold values from 0.1 to 1.9
- out_weight: bfloat16 [5120, 6144], P('tp'), may hold values from -0.078125 to 0.078125
Outputs:
- layer_out: bfloat16 [8192, 6144], P(('ctx', 'tp'))
The draws below stay inside these ranges and needn't reach their ends.
All inputs are finite; a program needn't handle non-finite values.
Results may differ from the reference program's by a relative error of at most 0.014.
Values may be sent and summed in bfloat16 or wider, within the bound.
No kernel may reach another device: no remote copies, remote signals or barrier semaphores. Data moves between devices by JAX's collectives and lax.ppermute only.
A program may use at most 128 MiB of HBM per device.

```python
import jax
import jax.numpy as jnp
from jax import lax

D = 6144
H = 40
HD = 128
TOK_DEV = 1024
SEQ = 8192
N_TP = 4


def level_of(rng, extent, split, least, top_value):
    factor_of = 1.0
    for position, shards_of in split:
        steps = jax.random.uniform(jax.random.fold_in(jax.random.fold_in(rng, 6), position), (shards_of,), jnp.float32, least / len(split), top_value / len(split))
        factor_of = factor_of * jnp.repeat(jnp.exp(steps), extent[position] // shards_of).reshape((-1,) + (1,) * (len(extent) - 1 - position))
    return factor_of


def scatter_about(own_key, dims, scale, bound, shards=(), kind=jnp.bfloat16):
    values = scale * jax.random.normal(own_key, dims, jnp.float32)
    if shards:
        values = values * level_of(own_key, dims, shards, -0.22, 0.18)
    return jnp.clip(values, -bound, bound).astype(kind)


def setup_inputs(seed: int = 0) -> dict:
    key_list = jax.random.split(jax.random.key(seed), 7)
    queries = scatter_about(key_list[0], (SEQ, H * HD), 1.0, 6.0, ((0, 8), (1, 4)))
    keys = scatter_about(key_list[1], (SEQ, H * HD), 1.0, 6.0, ((0, 8), (1, 4)))
    values = scatter_about(key_list[2], (SEQ, H * HD), 1.0, 6.0, ((0, 8), (1, 4)))
    gates = scatter_about(key_list[3], (SEQ, H * HD), 1.5, 6.0, ((0, 8), (1, 4)))
    gain = jnp.clip(1.0 + 0.18 * jax.random.normal(key_list[4], (H * HD,), jnp.float32), 0.1, 1.9)
    out_weight = scatter_about(key_list[5], (H * HD, D), (H * HD) ** -0.5, 0.078125, ((0, 4),))
    return dict(queries=queries, keys=keys, values=values, gates=gates, gain=gain, out_weight=out_weight)


epsilon = 1e-05

def reference(queries, keys, values, gates, gain, out_weight):
    length = queries.shape[0]
    blocks = length // TOK_DEV
    query_act = jax.nn.silu(queries.astype(jnp.float32)).astype(jnp.bfloat16)
    key_act = jax.nn.silu(keys.astype(jnp.float32)).astype(jnp.bfloat16)
    query_blocks = query_act.astype(jnp.float32).reshape(blocks, TOK_DEV, H, HD)
    key_blocks = key_act.astype(jnp.float32).reshape(blocks, TOK_DEV, H, HD)
    value_blocks = values.astype(jnp.float32).reshape(blocks, TOK_DEV, H, HD)
    causal = jnp.tril(jnp.ones((TOK_DEV, TOK_DEV), dtype=bool))
    highest = lax.Precision.HIGHEST

    def block_step(carried, pieces):
        query_rows, key_rows, value_rows = pieces
        scores = jnp.einsum('thd,shd->hts', query_rows, key_rows, precision=highest)
        scores = jnp.where(causal[None], scores, jnp.float32(0.0))
        scores = lax.optimization_barrier(scores.astype(jnp.bfloat16)).astype(jnp.float32)
        local_part = jnp.einsum('hts,she->the', scores, value_rows, precision=highest)
        remote_part = jnp.einsum('thd,hde->the', query_rows, carried, precision=highest)
        own_state = jnp.einsum('thd,the->hde', key_rows, value_rows, precision=highest)
        return (carried + own_state, remote_part + local_part)
    zero_state = jnp.zeros((H, HD, HD), jnp.float32)
    final_state, attention = lax.scan(block_step, zero_state, (query_blocks, key_blocks, value_blocks))
    attention = attention.reshape(length, H, HD)
    mean_sq = lax.optimization_barrier(jnp.mean(attention * attention, axis=-1, keepdims=True))
    normed = attention * lax.rsqrt(mean_sq + epsilon) * gain.reshape(H, HD)
    gate_open = jax.nn.sigmoid(gates.astype(jnp.float32)).reshape(length, H, HD)
    mixed = (normed * gate_open).astype(jnp.bfloat16).reshape(length, H * HD)
    group_cols = H * HD // N_TP
    total_out = jnp.zeros((length, D), jnp.float32)
    for group in range(N_TP):
        partial_value = jnp.dot(mixed[:, group * group_cols:(group + 1) * group_cols], out_weight[group * group_cols:(group + 1) * group_cols, :], preferred_element_type=jnp.float32)
        total_out = total_out + lax.optimization_barrier(partial_value.astype(jnp.bfloat16)).astype(jnp.float32)
    return total_out.astype(jnp.bfloat16)
```

```python
import jax
import jax.numpy as jnp
import numpy as np
from jax import lax
from jax.sharding import Mesh
from jax.sharding import PartitionSpec as P

HD = 128
COLUMN_CHUNKS = 3


epsilon = 1e-05


def split_bf16(x):
    hi = x.astype(jnp.bfloat16)
    lo = (x - hi.astype(jnp.float32)).astype(jnp.bfloat16)
    return hi, lo


def on_device(queries, keys, values, gates, gain, out_weight):
    tokens = queries.shape[0]
    columns = queries.shape[1]
    head_count = columns // HD
    ctx_size = lax.axis_size("ctx")
    ty_size = lax.axis_size("ty")
    tc_size = lax.axis_size("tc")
    query_act = (
        jax.nn.silu(queries.astype(jnp.float32))
        .astype(jnp.bfloat16)
        .reshape(tokens, head_count, HD)
    )
    key_act = (
        jax.nn.silu(keys.astype(jnp.float32)).astype(jnp.bfloat16).reshape(tokens, head_count, HD)
    )
    value_rows = values.reshape(tokens, head_count, HD)
    own_state = jnp.einsum("thd,the->hde", key_act, value_rows, preferred_element_type=jnp.float32)

    states = lax.all_gather(own_state.astype(jnp.bfloat16), "ctx", axis=0, tiled=False)
    earlier = jnp.arange(ctx_size) < lax.axis_index("ctx")
    prefix = jnp.sum(
        jnp.where(earlier[:, None, None, None], states.astype(jnp.float32), 0.0), axis=0
    )

    scores = jnp.einsum("thd,shd->hts", query_act, key_act, preferred_element_type=jnp.float32)
    causal = jnp.tril(jnp.ones((tokens, tokens), dtype=bool))
    scores = jnp.where(causal[None], scores, jnp.float32(0.0)).astype(jnp.bfloat16)
    local_part = jnp.einsum("hts,she->the", scores, value_rows, preferred_element_type=jnp.float32)
    prefix_hi, prefix_lo = split_bf16(prefix)
    remote_part = jnp.einsum(
        "thd,hde->the", query_act, prefix_hi, preferred_element_type=jnp.float32
    ) + jnp.einsum("thd,hde->the", query_act, prefix_lo, preferred_element_type=jnp.float32)
    attention = remote_part + local_part
    mean_sq = jnp.mean(attention * attention, axis=-1, keepdims=True)
    normed = attention * lax.rsqrt(mean_sq + epsilon) * gain.reshape(head_count, HD)
    gate_open = jax.nn.sigmoid(gates.astype(jnp.float32)).reshape(tokens, head_count, HD)
    mixed_rows = (normed * gate_open).astype(jnp.bfloat16).reshape(tokens, columns)

    block = tokens // (ty_size * tc_size)
    mixed_rows = (
        mixed_rows.reshape(ty_size, tc_size, block, columns)
        .transpose(1, 0, 2, 3)
        .reshape(tokens, columns)
    )
    width = out_weight.shape[1]
    chunk = width // COLUMN_CHUNKS
    pieces = []
    for c in range(COLUMN_CHUNKS):
        part = jnp.dot(
            mixed_rows, out_weight[:, c * chunk:(c + 1) * chunk], preferred_element_type=jnp.float32
        ).astype(jnp.bfloat16)
        part = lax.psum_scatter(part, "tc", scatter_dimension=0, tiled=True)
        part = lax.psum_scatter(part, "ty", scatter_dimension=0, tiled=True)
        pieces.append(part)
    return jnp.concatenate(pieces, axis=1)


def solution(mesh):
    ctx_size, tp_size = mesh.devices.shape
    split = Mesh(
        np.asarray(mesh.devices).reshape(ctx_size, tp_size // 2, 2), ("ctx", "ty", "tc")
    )
    tp = ("ty", "tc")
    return jax.shard_map(
        on_device,
        mesh=split,
        in_specs=(
            P("ctx", tp),
            P("ctx", tp),
            P("ctx", tp),
            P("ctx", tp),
            P(tp),
            P(tp, None),
        ),
        out_specs=P(("ctx",) + tp, None),
        check_vma=False,
    )
```

```python
import jax
import jax.numpy as jnp
import numpy as np
from jax import lax
from jax.sharding import Mesh
from jax.sharding import PartitionSpec as P

HD = 128
COLUMN_CHUNKS = 3


epsilon = 1e-05


def split_bf16(x):
    hi = x.astype(jnp.bfloat16)
    lo = (x - hi.astype(jnp.float32)).astype(jnp.bfloat16)
    return hi, lo


def shift(block, axis, distance):
    size = lax.axis_size(axis)
    return lax.ppermute(block, axis, [(i, i + distance) for i in range(size) if i + distance < size])


def swap(block, axis):
    return lax.ppermute(block, axis, [(0, 1), (1, 0)])


def exclusive_prefix(state, axis):
    inclusive = state
    exclusive = jnp.zeros_like(state)
    distance = 1
    while distance < lax.axis_size(axis):
        arrived = shift(inclusive.astype(jnp.bfloat16), axis, distance).astype(jnp.float32)
        exclusive = exclusive + arrived
        inclusive = inclusive + arrived
        distance *= 2
    return exclusive


def project_and_reduce(mixed_rows, out_weight):
    tokens, columns = mixed_rows.shape
    ty_size = lax.axis_size("ty")
    tc_size = lax.axis_size("tc")
    block = tokens // (ty_size * tc_size)
    width = out_weight.shape[1]

    def product(rows):
        return jnp.dot(rows, out_weight, preferred_element_type=jnp.float32).astype(jnp.bfloat16)

    if ty_size != 2 or tc_size != 2:
        ordered = (
            mixed_rows.reshape(ty_size, tc_size, block, columns)
            .transpose(1, 0, 2, 3)
            .reshape(tokens, columns)
        )
        part = product(ordered)
        part = lax.psum_scatter(part, "tc", scatter_dimension=0, tiled=True)
        return lax.psum_scatter(part, "ty", scatter_dimension=0, tiled=True)

    ty = lax.axis_index("ty")
    tc = lax.axis_index("tc")

    def rows_of(owner_ty, owner_tc):
        start = (owner_ty * tc_size + owner_tc) * block
        return lax.dynamic_slice_in_dim(mixed_rows, start, block, axis=0)

    chunk = width // COLUMN_CHUNKS
    across = []
    for c in range(COLUMN_CHUNKS):
        weight = out_weight[:, c * chunk:(c + 1) * chunk]
        partner_part = jnp.dot(
            rows_of(1 - ty, 1 - tc), weight, preferred_element_type=jnp.float32
        ).astype(jnp.bfloat16)
        from_partner = swap(partner_part, "tc")
        own_part = jnp.dot(rows_of(1 - ty, tc), weight, preferred_element_type=jnp.float32)
        chip_sum = (own_part.astype(jnp.bfloat16).astype(jnp.float32) + from_partner.astype(jnp.float32))
        across.append(swap(chip_sum.astype(jnp.bfloat16), "ty"))
    near = swap(product(rows_of(ty, 1 - tc)), "tc")
    mine = product(rows_of(ty, tc))
    far = jnp.concatenate(across, axis=1)
    total = mine.astype(jnp.float32) + near.astype(jnp.float32) + far.astype(jnp.float32)
    return total.astype(jnp.bfloat16)


def on_device(queries, keys, values, gates, gain, out_weight):
    tokens = queries.shape[0]
    columns = queries.shape[1]
    head_count = columns // HD
    key_act = (
        jax.nn.silu(keys.astype(jnp.float32)).astype(jnp.bfloat16).reshape(tokens, head_count, HD)
    )
    value_rows = values.reshape(tokens, head_count, HD)
    own_state = jnp.einsum("thd,the->hde", key_act, value_rows, preferred_element_type=jnp.float32)
    prefix = exclusive_prefix(own_state, "ctx")

    query_act = (
        jax.nn.silu(queries.astype(jnp.float32))
        .astype(jnp.bfloat16)
        .reshape(tokens, head_count, HD)
    )
    scores = jnp.einsum("thd,shd->hts", query_act, key_act, preferred_element_type=jnp.float32)
    causal = jnp.tril(jnp.ones((tokens, tokens), dtype=bool))
    scores = jnp.where(causal[None], scores, jnp.float32(0.0)).astype(jnp.bfloat16)
    local_part = jnp.einsum("hts,she->the", scores, value_rows, preferred_element_type=jnp.float32)
    prefix_hi, prefix_lo = split_bf16(prefix)
    remote_part = jnp.einsum(
        "thd,hde->the", query_act, prefix_hi, preferred_element_type=jnp.float32
    ) + jnp.einsum("thd,hde->the", query_act, prefix_lo, preferred_element_type=jnp.float32)
    attention = remote_part + local_part
    mean_sq = jnp.mean(attention * attention, axis=-1, keepdims=True)
    normed = attention * lax.rsqrt(mean_sq + epsilon) * gain.reshape(head_count, HD)
    gate_open = jax.nn.sigmoid(gates.astype(jnp.float32)).reshape(tokens, head_count, HD)
    mixed_rows = (normed * gate_open).astype(jnp.bfloat16).reshape(tokens, columns)
    return project_and_reduce(mixed_rows, out_weight)


def solution(mesh):
    ctx_size, tp_size = mesh.devices.shape
    split = Mesh(
        np.asarray(mesh.devices).reshape(ctx_size, tp_size // 2, 2), ("ctx", "ty", "tc")
    )
    tp = ("ty", "tc")
    return jax.shard_map(
        on_device,
        mesh=split,
        in_specs=(
            P("ctx", tp),
            P("ctx", tp),
            P("ctx", tp),
            P("ctx", tp),
            P(tp),
            P(tp, None),
        ),
        out_specs=P(("ctx",) + tp, None),
        check_vma=False,
    )
```

```python
import jax
import jax.numpy as jnp
import numpy as np
from jax import lax
from jax.sharding import Mesh
from jax.sharding import PartitionSpec as P

HD = 128
COLUMN_CHUNKS = 3


epsilon = 1e-05


def split_bf16(x):
    hi = x.astype(jnp.bfloat16)
    lo = (x - hi.astype(jnp.float32)).astype(jnp.bfloat16)
    return hi, lo


def shift(block, axis, distance):
    size = lax.axis_size(axis)
    return lax.ppermute(block, axis, [(i, i + distance) for i in range(size) if i + distance < size])


def swap(block, axis):
    return lax.ppermute(block, axis, [(0, 1), (1, 0)])


def exclusive_prefix(state, axis):
    inclusive = state
    exclusive = jnp.zeros_like(state)
    distance = 1
    while distance < lax.axis_size(axis):
        arrived = shift(inclusive.astype(jnp.bfloat16), axis, distance).astype(jnp.float32)
        exclusive = exclusive + arrived
        inclusive = inclusive + arrived
        distance *= 2
    return exclusive


def project_and_reduce(mixed_rows, out_weight):
    tokens, columns = mixed_rows.shape
    ty_size = lax.axis_size("ty")
    tc_size = lax.axis_size("tc")
    block = tokens // (ty_size * tc_size)
    width = out_weight.shape[1]

    def product(rows):
        return jnp.dot(rows, out_weight, preferred_element_type=jnp.float32).astype(jnp.bfloat16)

    if ty_size != 2 or tc_size != 2:
        ordered = (
            mixed_rows.reshape(ty_size, tc_size, block, columns)
            .transpose(1, 0, 2, 3)
            .reshape(tokens, columns)
        )
        part = product(ordered)
        part = lax.psum_scatter(part, "tc", scatter_dimension=0, tiled=True)
        return lax.psum_scatter(part, "ty", scatter_dimension=0, tiled=True)

    ty = lax.axis_index("ty")
    tc = lax.axis_index("tc")

    def rows_of(owner_ty, owner_tc):
        start = (owner_ty * tc_size + owner_tc) * block
        return lax.dynamic_slice_in_dim(mixed_rows, start, block, axis=0)

    chunk = width // COLUMN_CHUNKS
    across = []
    for c in range(COLUMN_CHUNKS):
        weight = out_weight[:, c * chunk:(c + 1) * chunk]
        partner_part = jnp.dot(
            rows_of(1 - ty, 1 - tc), weight, preferred_element_type=jnp.float32
        ).astype(jnp.bfloat16)
        from_partner = swap(partner_part, "tc")
        own_part = jnp.dot(rows_of(1 - ty, tc), weight, preferred_element_type=jnp.float32)
        chip_sum = (own_part.astype(jnp.bfloat16).astype(jnp.float32) + from_partner.astype(jnp.float32))
        across.append(swap(chip_sum.astype(jnp.bfloat16), "ty"))
    near = swap(product(rows_of(ty, 1 - tc)), "tc")
    mine = lax.optimization_barrier(product(rows_of(ty, tc)))
    far = jnp.concatenate(across, axis=1)
    total = mine.astype(jnp.float32) + near.astype(jnp.float32) + far.astype(jnp.float32)
    return total.astype(jnp.bfloat16)


def on_device(queries, keys, values, gates, gain, out_weight):
    tokens = queries.shape[0]
    columns = queries.shape[1]
    head_count = columns // HD
    key_act = (
        jax.nn.silu(keys.astype(jnp.float32)).astype(jnp.bfloat16).reshape(tokens, head_count, HD)
    )
    value_rows = values.reshape(tokens, head_count, HD)
    own_state = jnp.einsum("thd,the->hde", key_act, value_rows, preferred_element_type=jnp.float32)
    prefix = exclusive_prefix(own_state, "ctx")

    query_act = (
        jax.nn.silu(queries.astype(jnp.float32))
        .astype(jnp.bfloat16)
        .reshape(tokens, head_count, HD)
    )
    scores = jnp.einsum("thd,shd->hts", query_act, key_act, preferred_element_type=jnp.float32)
    causal = jnp.tril(jnp.ones((tokens, tokens), dtype=bool))
    scores = jnp.where(causal[None], scores, jnp.float32(0.0)).astype(jnp.bfloat16)
    local_part = jnp.einsum("hts,she->the", scores, value_rows, preferred_element_type=jnp.float32)
    prefix_hi, prefix_lo = split_bf16(prefix)
    remote_part = jnp.einsum(
        "thd,hde->the", query_act, prefix_hi, preferred_element_type=jnp.float32
    ) + jnp.einsum("thd,hde->the", query_act, prefix_lo, preferred_element_type=jnp.float32)
    attention = remote_part + local_part
    mean_sq = jnp.mean(attention * attention, axis=-1, keepdims=True)
    normed = attention * lax.rsqrt(mean_sq + epsilon) * gain.reshape(head_count, HD)
    gate_open = jax.nn.sigmoid(gates.astype(jnp.float32)).reshape(tokens, head_count, HD)
    mixed_rows = (normed * gate_open).astype(jnp.bfloat16).reshape(tokens, columns)
    return project_and_reduce(mixed_rows, out_weight)


def solution(mesh):
    ctx_size, tp_size = mesh.devices.shape
    split = Mesh(
        np.asarray(mesh.devices).reshape(ctx_size, tp_size // 2, 2), ("ctx", "ty", "tc")
    )
    tp = ("ty", "tc")
    return jax.shard_map(
        on_device,
        mesh=split,
        in_specs=(
            P("ctx", tp),
            P("ctx", tp),
            P("ctx", tp),
            P("ctx", tp),
            P(tp),
            P(tp, None),
        ),
        out_specs=P(("ctx",) + tp, None),
        check_vma=False,
    )
```

```python
import jax
import jax.numpy as jnp
import numpy as np
from jax import lax
from jax.experimental import pallas as pl
from jax.experimental.pallas import tpu as pltpu
from jax.sharding import Mesh
from jax.sharding import PartitionSpec as P

HD = 128
COLUMN_CHUNKS = 3
QUERY_TILE = 256


epsilon = 1e-05


def silu(x):
    x = x.astype(jnp.float32)
    return (x / (1.0 + jnp.exp(-x))).astype(jnp.bfloat16)


def head_block(tokens):
    return pl.BlockSpec((tokens, HD), lambda h: (0, h))


def state_kernel(k_ref, v_ref, state_ref):
    key_act = silu(k_ref[...])
    state_ref[0] = lax.dot_general(
        key_act, v_ref[...], (((0,), (0,)), ((), ())), preferred_element_type=jnp.float32
    )


def key_value_states(keys, values):
    tokens, columns = keys.shape
    heads = columns // HD
    return pl.pallas_call(
        state_kernel,
        grid=(heads,),
        in_specs=[head_block(tokens), head_block(tokens)],
        out_specs=pl.BlockSpec((1, HD, HD), lambda h: (h, 0, 0)),
        out_shape=jax.ShapeDtypeStruct((heads, HD, HD), jnp.float32),
        cost_estimate=pl.CostEstimate(
            flops=2 * tokens * HD * HD * heads,
            transcendentals=tokens * columns,
            bytes_accessed=4 * tokens * columns + 4 * heads * HD * HD,
        ),
    )(keys, values)


def local_kernel(q_ref, k_ref, v_ref, out_ref):
    tokens = q_ref.shape[0]
    query_act = silu(q_ref[...])
    key_act = silu(k_ref[...])
    value_rows = v_ref[...]
    for tile in range(tokens // QUERY_TILE):
        seen = (tile + 1) * QUERY_TILE
        scores = lax.dot_general(
            query_act[tile * QUERY_TILE:seen],
            key_act[:seen],
            (((1,), (1,)), ((), ())),
            preferred_element_type=jnp.float32,
        )
        row = lax.broadcasted_iota(jnp.int32, scores.shape, 0) + tile * QUERY_TILE
        col = lax.broadcasted_iota(jnp.int32, scores.shape, 1)
        scores = jnp.where(row >= col, scores, 0.0).astype(jnp.bfloat16)
        out_ref[tile * QUERY_TILE:seen, :] = jnp.dot(
            scores, value_rows[:seen], preferred_element_type=jnp.float32
        )


def local_attention(queries, keys, values):
    tokens, columns = queries.shape
    heads = columns // HD
    tiles = tokens // QUERY_TILE
    pairs = QUERY_TILE * QUERY_TILE * tiles * (tiles + 1) // 2
    return pl.pallas_call(
        local_kernel,
        grid=(heads,),
        in_specs=[head_block(tokens)] * 3,
        out_specs=head_block(tokens),
        out_shape=jax.ShapeDtypeStruct((tokens, columns), jnp.float32),
        cost_estimate=pl.CostEstimate(
            flops=4 * pairs * HD * heads,
            transcendentals=2 * tokens * columns,
            bytes_accessed=10 * tokens * columns,
        ),
    )(queries, keys, values)


def mix_kernel(local_ref, q_ref, g_ref, hi_ref, lo_ref, gain_ref, out_ref):
    query_act = silu(q_ref[...])
    remote = jnp.dot(query_act, hi_ref[0], preferred_element_type=jnp.float32) + jnp.dot(
        query_act, lo_ref[0], preferred_element_type=jnp.float32
    )
    attention = local_ref[...] + remote
    mean_sq = jnp.mean(attention * attention, axis=-1, keepdims=True)
    normed = attention * lax.rsqrt(mean_sq + epsilon) * gain_ref[...]
    gates = g_ref[...].astype(jnp.float32)
    gate_open = 1.0 / (1.0 + jnp.exp(-gates))
    out_ref[...] = (normed * gate_open).astype(out_ref.dtype)


def mix(local_part, queries, gates, prefix_hi, prefix_lo, gain):
    tokens, columns = queries.shape
    heads = columns // HD
    state_block = pl.BlockSpec((1, HD, HD), lambda h: (h, 0, 0))
    return pl.pallas_call(
        mix_kernel,
        grid=(heads,),
        in_specs=[
            head_block(tokens),
            head_block(tokens),
            head_block(tokens),
            state_block,
            state_block,
            pl.BlockSpec((1, HD), lambda h: (0, h)),
        ],
        out_specs=head_block(tokens),
        out_shape=jax.ShapeDtypeStruct((tokens, columns), jnp.bfloat16),
        cost_estimate=pl.CostEstimate(
            flops=4 * tokens * HD * HD * heads,
            transcendentals=2 * tokens * columns,
            bytes_accessed=10 * tokens * columns,
        ),
    )(local_part, queries, gates, prefix_hi, prefix_lo, gain.reshape(1, columns))


def split_bf16(x):
    hi = x.astype(jnp.bfloat16)
    lo = (x - hi.astype(jnp.float32)).astype(jnp.bfloat16)
    return hi, lo


def shift(block, axis, distance):
    size = lax.axis_size(axis)
    return lax.ppermute(block, axis, [(i, i + distance) for i in range(size) if i + distance < size])


def swap(block, axis):
    return lax.ppermute(block, axis, [(0, 1), (1, 0)])


def exclusive_prefix(state, axis):
    inclusive = state
    exclusive = jnp.zeros_like(state)
    distance = 1
    while distance < lax.axis_size(axis):
        arrived = shift(inclusive.astype(jnp.bfloat16), axis, distance).astype(jnp.float32)
        exclusive = exclusive + arrived
        inclusive = inclusive + arrived
        distance *= 2
    return exclusive


def project_and_reduce(mixed_rows, out_weight):
    tokens, columns = mixed_rows.shape
    ty_size = lax.axis_size("ty")
    tc_size = lax.axis_size("tc")
    block = tokens // (ty_size * tc_size)
    width = out_weight.shape[1]

    def product(rows):
        return jnp.dot(rows, out_weight, preferred_element_type=jnp.float32).astype(jnp.bfloat16)

    if ty_size != 2 or tc_size != 2:
        ordered = (
            mixed_rows.reshape(ty_size, tc_size, block, columns)
            .transpose(1, 0, 2, 3)
            .reshape(tokens, columns)
        )
        part = product(ordered)
        part = lax.psum_scatter(part, "tc", scatter_dimension=0, tiled=True)
        return lax.psum_scatter(part, "ty", scatter_dimension=0, tiled=True)

    ty = lax.axis_index("ty")
    tc = lax.axis_index("tc")

    def rows_of(owner_ty, owner_tc):
        start = (owner_ty * tc_size + owner_tc) * block
        return lax.dynamic_slice_in_dim(mixed_rows, start, block, axis=0)

    chunk = width // COLUMN_CHUNKS
    across = []
    for c in range(COLUMN_CHUNKS):
        weight = out_weight[:, c * chunk:(c + 1) * chunk]
        partner_part = jnp.dot(
            rows_of(1 - ty, 1 - tc), weight, preferred_element_type=jnp.float32
        ).astype(jnp.bfloat16)
        from_partner = swap(partner_part, "tc")
        own_part = jnp.dot(rows_of(1 - ty, tc), weight, preferred_element_type=jnp.float32)
        chip_sum = (own_part.astype(jnp.bfloat16).astype(jnp.float32) + from_partner.astype(jnp.float32))
        across.append(swap(chip_sum.astype(jnp.bfloat16), "ty"))
    near = swap(product(rows_of(ty, 1 - tc)), "tc")
    mine = lax.optimization_barrier(product(rows_of(ty, tc)))
    far = jnp.concatenate(across, axis=1)
    total = mine.astype(jnp.float32) + near.astype(jnp.float32) + far.astype(jnp.float32)
    return total.astype(jnp.bfloat16)


def on_device(queries, keys, values, gates, gain, out_weight):
    own_state = key_value_states(keys, values)
    prefix = exclusive_prefix(own_state, "ctx")
    local_part = local_attention(queries, keys, values)
    prefix_hi, prefix_lo = split_bf16(prefix)
    mixed_rows = mix(local_part, queries, gates, prefix_hi, prefix_lo, gain)
    return project_and_reduce(mixed_rows, out_weight)


def solution(mesh):
    ctx_size, tp_size = mesh.devices.shape
    split = Mesh(
        np.asarray(mesh.devices).reshape(ctx_size, tp_size // 2, 2), ("ctx", "ty", "tc")
    )
    tp = ("ty", "tc")
    return jax.shard_map(
        on_device,
        mesh=split,
        in_specs=(
            P("ctx", tp),
            P("ctx", tp),
            P("ctx", tp),
            P("ctx", tp),
            P(tp),
            P(tp, None),
        ),
        out_specs=P(("ctx",) + tp, None),
        check_vma=False,
    )
```

```python
import jax
import jax.numpy as jnp
import numpy as np
from jax import lax
from jax.experimental import pallas as pl
from jax.experimental.pallas import tpu as pltpu
from jax.sharding import Mesh
from jax.sharding import PartitionSpec as P

HD = 128
COLUMN_CHUNKS = 3
QUERY_TILE = 256
ROW_TILE = 256


epsilon = 1e-05


def silu(x):
    x = x.astype(jnp.float32)
    return (x / (1.0 + jnp.exp(-x))).astype(jnp.bfloat16)


def head_block(tokens):
    return pl.BlockSpec((tokens, HD), lambda h: (0, h))


def state_kernel(k_ref, v_ref, state_ref):
    @pl.when(pl.program_id(0) == 0)
    def _():
        state_ref[...] = jnp.zeros_like(state_ref)

    key_act = silu(k_ref[...])
    value_rows = v_ref[...]
    for h in range(state_ref.shape[0]):
        heads = slice(h * HD, (h + 1) * HD)
        state_ref[h] += lax.dot_general(
            key_act[:, heads], value_rows[:, heads], (((0,), (0,)), ((), ())),
            preferred_element_type=jnp.float32,
        )


def row_block(columns):
    return pl.BlockSpec((ROW_TILE, columns), lambda i: (i, 0))


def key_value_states(keys, values):
    tokens, columns = keys.shape
    heads = columns // HD
    return pl.pallas_call(
        state_kernel,
        grid=(tokens // ROW_TILE,),
        in_specs=[row_block(columns), row_block(columns)],
        out_specs=pl.BlockSpec((heads, HD, HD), lambda i: (0, 0, 0)),
        out_shape=jax.ShapeDtypeStruct((heads, HD, HD), jnp.float32),
        cost_estimate=pl.CostEstimate(
            flops=2 * tokens * HD * HD * heads,
            transcendentals=tokens * columns,
            bytes_accessed=4 * tokens * columns + 4 * heads * HD * HD,
        ),
    )(keys, values)


def local_kernel(q_ref, k_ref, v_ref, out_ref):
    tokens = q_ref.shape[0]
    query_act = silu(q_ref[...])
    key_act = silu(k_ref[...])
    value_rows = v_ref[...]
    for tile in range(tokens // QUERY_TILE):
        seen = (tile + 1) * QUERY_TILE
        scores = lax.dot_general(
            query_act[tile * QUERY_TILE:seen],
            key_act[:seen],
            (((1,), (1,)), ((), ())),
            preferred_element_type=jnp.float32,
        )
        row = lax.broadcasted_iota(jnp.int32, scores.shape, 0) + tile * QUERY_TILE
        col = lax.broadcasted_iota(jnp.int32, scores.shape, 1)
        scores = jnp.where(row >= col, scores, 0.0).astype(jnp.bfloat16)
        out_ref[tile * QUERY_TILE:seen, :] = jnp.dot(
            scores, value_rows[:seen], preferred_element_type=jnp.float32
        )


def local_attention(queries, keys, values):
    tokens, columns = queries.shape
    heads = columns // HD
    tiles = tokens // QUERY_TILE
    pairs = QUERY_TILE * QUERY_TILE * tiles * (tiles + 1) // 2
    return pl.pallas_call(
        local_kernel,
        grid=(heads,),
        in_specs=[head_block(tokens)] * 3,
        out_specs=head_block(tokens),
        out_shape=jax.ShapeDtypeStruct((tokens, columns), jnp.float32),
        cost_estimate=pl.CostEstimate(
            flops=4 * pairs * HD * heads,
            transcendentals=2 * tokens * columns,
            bytes_accessed=10 * tokens * columns,
        ),
    )(queries, keys, values)


def mix_kernel(local_ref, q_ref, g_ref, hi_ref, lo_ref, gain_ref, out_ref):
    query_act = silu(q_ref[...])
    gates = g_ref[...].astype(jnp.float32)
    gate_open = 1.0 / (1.0 + jnp.exp(-gates))
    for h in range(hi_ref.shape[0]):
        heads = slice(h * HD, (h + 1) * HD)
        remote = jnp.dot(query_act[:, heads], hi_ref[h], preferred_element_type=jnp.float32) + jnp.dot(
            query_act[:, heads], lo_ref[h], preferred_element_type=jnp.float32
        )
        attention = local_ref[:, heads] + remote
        mean_sq = jnp.mean(attention * attention, axis=-1, keepdims=True)
        normed = attention * lax.rsqrt(mean_sq + epsilon) * gain_ref[:, heads]
        out_ref[:, heads] = (normed * gate_open[:, heads]).astype(out_ref.dtype)


def mix(local_part, queries, gates, prefix_hi, prefix_lo, gain):
    tokens, columns = queries.shape
    heads = columns // HD
    whole_state = pl.BlockSpec((heads, HD, HD), lambda i: (0, 0, 0))
    return pl.pallas_call(
        mix_kernel,
        grid=(tokens // ROW_TILE,),
        in_specs=[
            row_block(columns),
            row_block(columns),
            row_block(columns),
            whole_state,
            whole_state,
            pl.BlockSpec((1, columns), lambda i: (0, 0)),
        ],
        out_specs=row_block(columns),
        out_shape=jax.ShapeDtypeStruct((tokens, columns), jnp.bfloat16),
        cost_estimate=pl.CostEstimate(
            flops=4 * tokens * HD * HD * heads,
            transcendentals=2 * tokens * columns,
            bytes_accessed=10 * tokens * columns,
        ),
    )(local_part, queries, gates, prefix_hi, prefix_lo, gain.reshape(1, columns))


def split_bf16(x):
    hi = x.astype(jnp.bfloat16)
    lo = (x - hi.astype(jnp.float32)).astype(jnp.bfloat16)
    return hi, lo


def shift(block, axis, distance):
    size = lax.axis_size(axis)
    return lax.ppermute(block, axis, [(i, i + distance) for i in range(size) if i + distance < size])


def swap(block, axis):
    return lax.ppermute(block, axis, [(0, 1), (1, 0)])


def exclusive_prefix(state, axis):
    inclusive = state
    exclusive = jnp.zeros_like(state)
    distance = 1
    while distance < lax.axis_size(axis):
        arrived = shift(inclusive.astype(jnp.bfloat16), axis, distance).astype(jnp.float32)
        exclusive = exclusive + arrived
        inclusive = inclusive + arrived
        distance *= 2
    return exclusive


def project_and_reduce(mixed_rows, out_weight):
    tokens, columns = mixed_rows.shape
    ty_size = lax.axis_size("ty")
    tc_size = lax.axis_size("tc")
    block = tokens // (ty_size * tc_size)
    width = out_weight.shape[1]

    def product(rows):
        return jnp.dot(rows, out_weight, preferred_element_type=jnp.float32).astype(jnp.bfloat16)

    if ty_size != 2 or tc_size != 2:
        ordered = (
            mixed_rows.reshape(ty_size, tc_size, block, columns)
            .transpose(1, 0, 2, 3)
            .reshape(tokens, columns)
        )
        part = product(ordered)
        part = lax.psum_scatter(part, "tc", scatter_dimension=0, tiled=True)
        return lax.psum_scatter(part, "ty", scatter_dimension=0, tiled=True)

    ty = lax.axis_index("ty")
    tc = lax.axis_index("tc")

    def rows_of(owner_ty, owner_tc):
        start = (owner_ty * tc_size + owner_tc) * block
        return lax.dynamic_slice_in_dim(mixed_rows, start, block, axis=0)

    chunk = width // COLUMN_CHUNKS
    chip_sums = []
    near_parts = []
    for c in range(COLUMN_CHUNKS):
        weight = out_weight[:, c * chunk:(c + 1) * chunk]
        partner_part = jnp.dot(
            rows_of(1 - ty, 1 - tc), weight, preferred_element_type=jnp.float32
        ).astype(jnp.bfloat16)
        from_partner = swap(partner_part, "tc")
        own_part = jnp.dot(rows_of(1 - ty, tc), weight, preferred_element_type=jnp.float32)
        chip_sum = (own_part.astype(jnp.bfloat16).astype(jnp.float32) + from_partner.astype(jnp.float32))
        chip_sums.append(chip_sum.astype(jnp.bfloat16))
        near_parts.append(jnp.dot(
            rows_of(ty, 1 - tc), weight, preferred_element_type=jnp.float32
        ).astype(jnp.bfloat16))
    chip_sums, near_parts, mixed_rows = lax.optimization_barrier((chip_sums, near_parts, mixed_rows))
    across = [swap(chip_sum, "ty") for chip_sum in chip_sums]
    near = [swap(part, "tc") for part in near_parts]
    mine = lax.optimization_barrier(product(rows_of(ty, tc)))
    far = jnp.concatenate(across, axis=1)
    near = jnp.concatenate(near, axis=1)
    total = mine.astype(jnp.float32) + near.astype(jnp.float32) + far.astype(jnp.float32)
    return total.astype(jnp.bfloat16)


def on_device(queries, keys, values, gates, gain, out_weight):
    own_state = key_value_states(keys, values)
    prefix = exclusive_prefix(own_state, "ctx")
    local_part = local_attention(queries, keys, values)
    prefix_hi, prefix_lo = split_bf16(prefix)
    mixed_rows = mix(local_part, queries, gates, prefix_hi, prefix_lo, gain)
    return project_and_reduce(mixed_rows, out_weight)


def solution(mesh):
    ctx_size, tp_size = mesh.devices.shape
    split = Mesh(
        np.asarray(mesh.devices).reshape(ctx_size, tp_size // 2, 2), ("ctx", "ty", "tc")
    )
    tp = ("ty", "tc")
    return jax.shard_map(
        on_device,
        mesh=split,
        in_specs=(
            P("ctx", tp),
            P("ctx", tp),
            P("ctx", tp),
            P("ctx", tp),
            P(tp),
            P(tp, None),
        ),
        out_specs=P(("ctx",) + tp, None),
        check_vma=False,
    )
```

```python
import jax
import jax.numpy as jnp
import numpy as np
from jax import lax
from jax.experimental import pallas as pl
from jax.experimental.pallas import tpu as pltpu
from jax.sharding import Mesh
from jax.sharding import PartitionSpec as P

HD = 128
COLUMN_CHUNKS = 3
QUERY_TILE = 256
ROW_TILE = 256


epsilon = 1e-05


def silu(x):
    x = x.astype(jnp.float32)
    return (x / (1.0 + jnp.exp(-x))).astype(jnp.bfloat16)


def head_block(tokens):
    return pl.BlockSpec((tokens, HD), lambda h: (0, h))


def state_kernel(k_ref, v_ref, state_ref):
    @pl.when(pl.program_id(0) == 0)
    def _():
        state_ref[...] = jnp.zeros_like(state_ref)

    key_act = silu(k_ref[...])
    value_rows = v_ref[...]
    for h in range(state_ref.shape[0]):
        heads = slice(h * HD, (h + 1) * HD)
        state_ref[h] += lax.dot_general(
            key_act[:, heads], value_rows[:, heads], (((0,), (0,)), ((), ())),
            preferred_element_type=jnp.float32,
        )


def row_block(columns):
    return pl.BlockSpec((ROW_TILE, columns), lambda i: (i, 0))


def key_value_states(keys, values):
    tokens, columns = keys.shape
    heads = columns // HD
    return pl.pallas_call(
        state_kernel,
        grid=(tokens // ROW_TILE,),
        in_specs=[row_block(columns), row_block(columns)],
        out_specs=pl.BlockSpec((heads, HD, HD), lambda i: (0, 0, 0)),
        out_shape=jax.ShapeDtypeStruct((heads, HD, HD), jnp.float32),
        cost_estimate=pl.CostEstimate(
            flops=2 * tokens * HD * HD * heads,
            transcendentals=tokens * columns,
            bytes_accessed=4 * tokens * columns + 4 * heads * HD * HD,
        ),
    )(keys, values)


def local_kernel(q_ref, k_ref, v_ref, out_ref):
    tokens = q_ref.shape[0]
    query_act = silu(q_ref[...])
    key_act = silu(k_ref[...])
    value_rows = v_ref[...]
    for tile in range(tokens // QUERY_TILE):
        seen = (tile + 1) * QUERY_TILE
        scores = lax.dot_general(
            query_act[tile * QUERY_TILE:seen],
            key_act[:seen],
            (((1,), (1,)), ((), ())),
            preferred_element_type=jnp.float32,
        )
        row = lax.broadcasted_iota(jnp.int32, scores.shape, 0) + tile * QUERY_TILE
        col = lax.broadcasted_iota(jnp.int32, scores.shape, 1)
        scores = jnp.where(row >= col, scores, 0.0).astype(jnp.bfloat16)
        out_ref[tile * QUERY_TILE:seen, :] = jnp.dot(
            scores, value_rows[:seen], preferred_element_type=jnp.float32
        )


def local_attention(queries, keys, values):
    tokens, columns = queries.shape
    heads = columns // HD
    tiles = tokens // QUERY_TILE
    pairs = QUERY_TILE * QUERY_TILE * tiles * (tiles + 1) // 2
    return pl.pallas_call(
        local_kernel,
        grid=(heads,),
        in_specs=[head_block(tokens)] * 3,
        out_specs=head_block(tokens),
        out_shape=jax.ShapeDtypeStruct((tokens, columns), jnp.float32),
        cost_estimate=pl.CostEstimate(
            flops=4 * pairs * HD * heads,
            transcendentals=2 * tokens * columns,
            bytes_accessed=10 * tokens * columns,
        ),
    )(queries, keys, values)


def mix_kernel(local_ref, q_ref, g_ref, hi_ref, lo_ref, gain_ref, out_ref):
    query_act = silu(q_ref[...])
    gates = g_ref[...].astype(jnp.float32)
    gate_open = 1.0 / (1.0 + jnp.exp(-gates))
    for h in range(hi_ref.shape[0]):
        heads = slice(h * HD, (h + 1) * HD)
        remote = jnp.dot(query_act[:, heads], hi_ref[h], preferred_element_type=jnp.float32) + jnp.dot(
            query_act[:, heads], lo_ref[h], preferred_element_type=jnp.float32
        )
        attention = local_ref[:, heads] + remote
        mean_sq = jnp.mean(attention * attention, axis=-1, keepdims=True)
        normed = attention * lax.rsqrt(mean_sq + epsilon) * gain_ref[:, heads]
        out_ref[:, heads] = (normed * gate_open[:, heads]).astype(out_ref.dtype)


def mix(local_part, queries, gates, prefix_hi, prefix_lo, gain):
    tokens, columns = queries.shape
    heads = columns // HD
    whole_state = pl.BlockSpec((heads, HD, HD), lambda i: (0, 0, 0))
    return pl.pallas_call(
        mix_kernel,
        grid=(tokens // ROW_TILE,),
        in_specs=[
            row_block(columns),
            row_block(columns),
            row_block(columns),
            whole_state,
            whole_state,
            pl.BlockSpec((1, columns), lambda i: (0, 0)),
        ],
        out_specs=row_block(columns),
        out_shape=jax.ShapeDtypeStruct((tokens, columns), jnp.bfloat16),
        cost_estimate=pl.CostEstimate(
            flops=4 * tokens * HD * HD * heads,
            transcendentals=2 * tokens * columns,
            bytes_accessed=10 * tokens * columns,
        ),
    )(local_part, queries, gates, prefix_hi, prefix_lo, gain.reshape(1, columns))


def split_bf16(x):
    hi = x.astype(jnp.bfloat16)
    lo = (x - hi.astype(jnp.float32)).astype(jnp.bfloat16)
    return hi, lo


def shift(block, axis, distance):
    size = lax.axis_size(axis)
    return lax.ppermute(block, axis, [(i, i + distance) for i in range(size) if i + distance < size])


def swap(block, axis):
    return lax.ppermute(block, axis, [(0, 1), (1, 0)])


def exclusive_prefix(state, axis):
    inclusive = state
    exclusive = jnp.zeros_like(state)
    distance = 1
    while distance < lax.axis_size(axis):
        arrived = shift(inclusive.astype(jnp.bfloat16), axis, distance).astype(jnp.float32)
        exclusive = exclusive + arrived
        inclusive = inclusive + arrived
        distance *= 2
    return exclusive


def project_and_reduce(mixed_rows, out_weight):
    tokens, columns = mixed_rows.shape
    ty_size = lax.axis_size("ty")
    tc_size = lax.axis_size("tc")
    block = tokens // (ty_size * tc_size)
    width = out_weight.shape[1]

    def product(rows):
        return jnp.dot(rows, out_weight, preferred_element_type=jnp.float32).astype(jnp.bfloat16)

    if ty_size != 2 or tc_size != 2:
        ordered = (
            mixed_rows.reshape(ty_size, tc_size, block, columns)
            .transpose(1, 0, 2, 3)
            .reshape(tokens, columns)
        )
        part = product(ordered)
        part = lax.psum_scatter(part, "tc", scatter_dimension=0, tiled=True)
        return lax.psum_scatter(part, "ty", scatter_dimension=0, tiled=True)

    ty = lax.axis_index("ty")
    tc = lax.axis_index("tc")
    pair = tc_size * block
    far_rows = lax.dynamic_slice_in_dim(mixed_rows, (1 - ty) * pair, pair, axis=0)
    near_rows = lax.dynamic_slice_in_dim(mixed_rows, ty * pair, pair, axis=0)

    def block_of(part, owner_tc):
        return lax.dynamic_slice_in_dim(part, owner_tc * block, block, axis=0)

    chunk = width // COLUMN_CHUNKS
    chip_sums = []
    for c in range(COLUMN_CHUNKS):
        far_part = jnp.dot(
            far_rows, out_weight[:, c * chunk:(c + 1) * chunk], preferred_element_type=jnp.float32
        ).astype(jnp.bfloat16)
        from_partner = swap(block_of(far_part, 1 - tc), "tc")
        chip_sum = block_of(far_part, tc).astype(jnp.float32) + from_partner.astype(jnp.float32)
        chip_sums.append(chip_sum.astype(jnp.bfloat16))
    chip_sums, near_rows = lax.optimization_barrier((chip_sums, near_rows))
    across = [swap(chip_sum, "ty") for chip_sum in chip_sums]
    near = swap(product(block_of(near_rows, 1 - tc)), "tc")
    mine = lax.optimization_barrier(product(block_of(near_rows, tc)))
    far = jnp.concatenate(across, axis=1)
    total = mine.astype(jnp.float32) + near.astype(jnp.float32) + far.astype(jnp.float32)
    return total.astype(jnp.bfloat16)


def on_device(queries, keys, values, gates, gain, out_weight):
    own_state = key_value_states(keys, values)
    prefix = exclusive_prefix(own_state, "ctx")
    local_part = local_attention(queries, keys, values)
    prefix_hi, prefix_lo = split_bf16(prefix)
    mixed_rows = mix(local_part, queries, gates, prefix_hi, prefix_lo, gain)
    return project_and_reduce(mixed_rows, out_weight)


def solution(mesh):
    ctx_size, tp_size = mesh.devices.shape
    split = Mesh(
        np.asarray(mesh.devices).reshape(ctx_size, tp_size // 2, 2), ("ctx", "ty", "tc")
    )
    tp = ("ty", "tc")
    return jax.shard_map(
        on_device,
        mesh=split,
        in_specs=(
            P("ctx", tp),
            P("ctx", tp),
            P("ctx", tp),
            P("ctx", tp),
            P(tp),
            P(tp, None),
        ),
        out_specs=P(("ctx",) + tp, None),
        check_vma=False,
    )
```

```python
import jax
import jax.numpy as jnp
import numpy as np
from jax import lax
from jax.experimental import pallas as pl
from jax.experimental.pallas import tpu as pltpu
from jax.sharding import Mesh
from jax.sharding import PartitionSpec as P

HD = 128
COLUMN_CHUNKS = 3
QUERY_TILE = 256
ROW_TILE = 256


epsilon = 1e-05


def silu(x):
    x = x.astype(jnp.float32)
    return (x / (1.0 + jnp.exp(-x))).astype(jnp.bfloat16)


def head_block(tokens):
    return pl.BlockSpec((tokens, HD), lambda h: (0, h))


def state_kernel(k_ref, v_ref, state_ref):
    @pl.when(pl.program_id(0) == 0)
    def _():
        state_ref[...] = jnp.zeros_like(state_ref)

    key_act = silu(k_ref[...])
    value_rows = v_ref[...]
    for h in range(state_ref.shape[0]):
        heads = slice(h * HD, (h + 1) * HD)
        state_ref[h] += lax.dot_general(
            key_act[:, heads], value_rows[:, heads], (((0,), (0,)), ((), ())),
            preferred_element_type=jnp.float32,
        )


def row_block(columns):
    return pl.BlockSpec((ROW_TILE, columns), lambda i: (i, 0))


def key_value_states(keys, values):
    tokens, columns = keys.shape
    heads = columns // HD
    return pl.pallas_call(
        state_kernel,
        grid=(tokens // ROW_TILE,),
        in_specs=[row_block(columns), row_block(columns)],
        out_specs=pl.BlockSpec((heads, HD, HD), lambda i: (0, 0, 0)),
        out_shape=jax.ShapeDtypeStruct((heads, HD, HD), jnp.float32),
        cost_estimate=pl.CostEstimate(
            flops=2 * tokens * HD * HD * heads,
            transcendentals=tokens * columns,
            bytes_accessed=4 * tokens * columns + 4 * heads * HD * HD,
        ),
    )(keys, values)


def local_kernel(q_ref, k_ref, v_ref, out_ref):
    tokens = q_ref.shape[0]
    query_act = silu(q_ref[...])
    key_act = silu(k_ref[...])
    value_rows = v_ref[...]
    for tile in range(tokens // QUERY_TILE):
        seen = (tile + 1) * QUERY_TILE
        scores = lax.dot_general(
            query_act[tile * QUERY_TILE:seen],
            key_act[:seen],
            (((1,), (1,)), ((), ())),
            preferred_element_type=jnp.float32,
        )
        row = lax.broadcasted_iota(jnp.int32, scores.shape, 0) + tile * QUERY_TILE
        col = lax.broadcasted_iota(jnp.int32, scores.shape, 1)
        scores = jnp.where(row >= col, scores, 0.0).astype(jnp.bfloat16)
        out_ref[tile * QUERY_TILE:seen, :] = jnp.dot(
            scores, value_rows[:seen], preferred_element_type=jnp.float32
        )


def local_attention(queries, keys, values):
    tokens, columns = queries.shape
    heads = columns // HD
    tiles = tokens // QUERY_TILE
    pairs = QUERY_TILE * QUERY_TILE * tiles * (tiles + 1) // 2
    return pl.pallas_call(
        local_kernel,
        grid=(heads,),
        in_specs=[head_block(tokens)] * 3,
        out_specs=head_block(tokens),
        out_shape=jax.ShapeDtypeStruct((tokens, columns), jnp.float32),
        cost_estimate=pl.CostEstimate(
            flops=4 * pairs * HD * heads,
            transcendentals=2 * tokens * columns,
            bytes_accessed=10 * tokens * columns,
        ),
    )(queries, keys, values)


def mix_kernel(order_ref, local_ref, q_ref, g_ref, prefix_ref, gain_ref, out_ref):
    query_act = silu(q_ref[...])
    gates = g_ref[...].astype(jnp.float32)
    gate_open = 1.0 / (1.0 + jnp.exp(-gates))
    for h in range(prefix_ref.shape[0]):
        heads = slice(h * HD, (h + 1) * HD)
        prefix_hi, prefix_lo = split_bf16(prefix_ref[h])
        remote = jnp.dot(query_act[:, heads], prefix_hi, preferred_element_type=jnp.float32) + jnp.dot(
            query_act[:, heads], prefix_lo, preferred_element_type=jnp.float32
        )
        attention = local_ref[:, heads] + remote
        mean_sq = jnp.mean(attention * attention, axis=-1, keepdims=True)
        normed = attention * lax.rsqrt(mean_sq + epsilon) * gain_ref[:, heads]
        out_ref[:, heads] = (normed * gate_open[:, heads]).astype(out_ref.dtype)


def mix(order, local_part, queries, gates, prefix, gain):
    tokens, columns = queries.shape
    heads = columns // HD
    picked = pl.BlockSpec((ROW_TILE, columns), lambda i, order: (order[i], 0))
    return pl.pallas_call(
        mix_kernel,
        grid_spec=pltpu.PrefetchScalarGridSpec(
            num_scalar_prefetch=1,
            grid=(tokens // ROW_TILE,),
            in_specs=[
                picked,
                picked,
                picked,
                pl.BlockSpec((heads, HD, HD), lambda i, order: (0, 0, 0)),
                pl.BlockSpec((1, columns), lambda i, order: (0, 0)),
            ],
            out_specs=pl.BlockSpec((ROW_TILE, columns), lambda i, order: (i, 0)),
        ),
        out_shape=jax.ShapeDtypeStruct((tokens, columns), jnp.bfloat16),
        cost_estimate=pl.CostEstimate(
            flops=4 * tokens * HD * HD * heads,
            transcendentals=2 * tokens * columns,
            bytes_accessed=10 * tokens * columns,
        ),
    )(order, local_part, queries, gates, prefix, gain.reshape(1, columns))


def split_bf16(x):
    hi = x.astype(jnp.bfloat16)
    lo = (x - hi.astype(jnp.float32)).astype(jnp.bfloat16)
    return hi, lo


def shift(block, axis, distance):
    size = lax.axis_size(axis)
    return lax.ppermute(block, axis, [(i, i + distance) for i in range(size) if i + distance < size])


def swap(block, axis):
    return lax.ppermute(block, axis, [(0, 1), (1, 0)])


def exclusive_prefix(state, axis):
    inclusive = state
    exclusive = jnp.zeros_like(state)
    distance = 1
    while distance < lax.axis_size(axis):
        arrived = shift(inclusive.astype(jnp.bfloat16), axis, distance).astype(jnp.float32)
        exclusive = exclusive + arrived
        inclusive = inclusive + arrived
        distance *= 2
    return exclusive


def reduce_order(tokens):
    ty_size = lax.axis_size("ty")
    tc_size = lax.axis_size("tc")
    tiles = tokens // ROW_TILE
    if ty_size != 2 or tc_size != 2 or tiles != 4:
        return jnp.arange(tiles, dtype=jnp.int32)
    ty = lax.axis_index("ty")
    tc = lax.axis_index("tc")
    return jnp.stack(
        [(1 - ty) * 2 + 1 - tc, ty * 2 + 1 - tc, (1 - ty) * 2 + tc, ty * 2 + tc]
    ).astype(jnp.int32)


def project_and_reduce(mixed_rows, out_weight):
    tokens, columns = mixed_rows.shape
    ty_size = lax.axis_size("ty")
    tc_size = lax.axis_size("tc")
    block = tokens // (ty_size * tc_size)
    width = out_weight.shape[1]

    def product(rows):
        return jnp.dot(rows, out_weight, preferred_element_type=jnp.float32).astype(jnp.bfloat16)

    if ty_size != 2 or tc_size != 2 or block != ROW_TILE:
        ordered = (
            mixed_rows.reshape(ty_size, tc_size, block, columns)
            .transpose(1, 0, 2, 3)
            .reshape(tokens, columns)
        )
        part = product(ordered)
        part = lax.psum_scatter(part, "tc", scatter_dimension=0, tiled=True)
        return lax.psum_scatter(part, "ty", scatter_dimension=0, tiled=True)

    early_rows = mixed_rows[:3 * block]
    own_rows = mixed_rows[3 * block:]
    chunk = width // COLUMN_CHUNKS
    chip_sums = []
    near_parts = []
    for c in range(COLUMN_CHUNKS):
        part = jnp.dot(
            early_rows, out_weight[:, c * chunk:(c + 1) * chunk], preferred_element_type=jnp.float32
        ).astype(jnp.bfloat16)
        from_partner = swap(part[:2 * block], "tc")
        chip_sum = part[2 * block:].astype(jnp.float32) + from_partner[:block].astype(jnp.float32)
        chip_sums.append(chip_sum.astype(jnp.bfloat16))
        near_parts.append(from_partner[block:])
    chip_sums, own_rows = lax.optimization_barrier((chip_sums, own_rows))
    across = [swap(chip_sum, "ty") for chip_sum in chip_sums]
    mine = lax.optimization_barrier(product(own_rows))
    far = jnp.concatenate(across, axis=1)
    near = jnp.concatenate(near_parts, axis=1)
    total = mine.astype(jnp.float32) + near.astype(jnp.float32) + far.astype(jnp.float32)
    return total.astype(jnp.bfloat16)


def on_device(queries, keys, values, gates, gain, out_weight):
    own_state = key_value_states(keys, values)
    prefix = exclusive_prefix(own_state, "ctx")
    local_part = local_attention(queries, keys, values)
    mixed_rows = mix(reduce_order(queries.shape[0]), local_part, queries, gates, prefix, gain)
    return project_and_reduce(mixed_rows, out_weight)


def solution(mesh):
    ctx_size, tp_size = mesh.devices.shape
    split = Mesh(
        np.asarray(mesh.devices).reshape(ctx_size, tp_size // 2, 2), ("ctx", "ty", "tc")
    )
    tp = ("ty", "tc")
    return jax.shard_map(
        on_device,
        mesh=split,
        in_specs=(
            P("ctx", tp),
            P("ctx", tp),
            P("ctx", tp),
            P("ctx", tp),
            P(tp),
            P(tp, None),
        ),
        out_specs=P(("ctx",) + tp, None),
        check_vma=False,
    )
```

```python
import jax
import jax.numpy as jnp
import numpy as np
from jax import lax
from jax.experimental import pallas as pl
from jax.experimental.pallas import tpu as pltpu
from jax.sharding import Mesh
from jax.sharding import PartitionSpec as P

HD = 128
COLUMN_CHUNKS = 3
QUERY_TILE = 256
ROW_TILE = 256


epsilon = 1e-05


def silu(x):
    x = x.astype(jnp.float32)
    return (x / (1.0 + jnp.exp(-x))).astype(jnp.bfloat16)


def head_block(tokens):
    return pl.BlockSpec((tokens, HD), lambda h: (0, h))


def state_kernel(k_ref, v_ref, state_ref):
    @pl.when(pl.program_id(0) == 0)
    def _():
        state_ref[...] = jnp.zeros_like(state_ref)

    key_act = silu(k_ref[...])
    value_rows = v_ref[...]
    for h in range(state_ref.shape[0]):
        heads = slice(h * HD, (h + 1) * HD)
        state_ref[h] += lax.dot_general(
            key_act[:, heads], value_rows[:, heads], (((0,), (0,)), ((), ())),
            preferred_element_type=jnp.float32,
        )


def row_block(columns):
    return pl.BlockSpec((ROW_TILE, columns), lambda i: (i, 0))


def key_value_states(keys, values):
    tokens, columns = keys.shape
    heads = columns // HD
    return pl.pallas_call(
        state_kernel,
        grid=(tokens // ROW_TILE,),
        in_specs=[row_block(columns), row_block(columns)],
        out_specs=pl.BlockSpec((heads, HD, HD), lambda i: (0, 0, 0)),
        out_shape=jax.ShapeDtypeStruct((heads, HD, HD), jnp.float32),
        cost_estimate=pl.CostEstimate(
            flops=2 * tokens * HD * HD * heads,
            transcendentals=tokens * columns,
            bytes_accessed=4 * tokens * columns + 4 * heads * HD * HD,
        ),
    )(keys, values)


def local_kernel(q_ref, k_ref, v_ref, out_ref):
    tokens = q_ref.shape[0]
    query_act = silu(q_ref[...])
    key_act = silu(k_ref[...])
    value_rows = v_ref[...]
    for tile in range(tokens // QUERY_TILE):
        seen = (tile + 1) * QUERY_TILE
        scores = lax.dot_general(
            query_act[tile * QUERY_TILE:seen],
            key_act[:seen],
            (((1,), (1,)), ((), ())),
            preferred_element_type=jnp.float32,
        )
        row = lax.broadcasted_iota(jnp.int32, scores.shape, 0) + tile * QUERY_TILE
        col = lax.broadcasted_iota(jnp.int32, scores.shape, 1)
        scores = jnp.where(row >= col, scores, 0.0).astype(jnp.bfloat16)
        out_ref[tile * QUERY_TILE:seen, :] = jnp.dot(
            scores, value_rows[:seen], preferred_element_type=jnp.float32
        )


def local_attention(queries, keys, values, first_head, heads):
    tokens, columns = queries.shape
    tiles = tokens // QUERY_TILE
    pairs = QUERY_TILE * QUERY_TILE * tiles * (tiles + 1) // 2
    picked = pl.BlockSpec((tokens, HD), lambda h: (0, h + first_head))
    return pl.pallas_call(
        local_kernel,
        grid=(heads,),
        in_specs=[picked] * 3,
        out_specs=head_block(tokens),
        out_shape=jax.ShapeDtypeStruct((tokens, heads * HD), jnp.float32),
        cost_estimate=pl.CostEstimate(
            flops=4 * pairs * HD * heads,
            transcendentals=2 * tokens * heads * HD,
            bytes_accessed=10 * tokens * heads * HD,
        ),
    )(queries, keys, values)


def mix_kernel(local_a_ref, local_b_ref, q_ref, g_ref, hi_ref, lo_ref, gain_ref, out_ref):
    query_act = silu(q_ref[...])
    gates = g_ref[...].astype(jnp.float32)
    gate_open = 1.0 / (1.0 + jnp.exp(-gates))
    first = local_a_ref.shape[1] // HD
    for h in range(hi_ref.shape[0]):
        heads = slice(h * HD, (h + 1) * HD)
        if h < first:
            local = local_a_ref[:, heads]
        else:
            local = local_b_ref[:, (h - first) * HD:(h - first + 1) * HD]
        remote = jnp.dot(query_act[:, heads], hi_ref[h], preferred_element_type=jnp.float32) + jnp.dot(
            query_act[:, heads], lo_ref[h], preferred_element_type=jnp.float32
        )
        attention = local + remote
        mean_sq = jnp.mean(attention * attention, axis=-1, keepdims=True)
        normed = attention * lax.rsqrt(mean_sq + epsilon) * gain_ref[:, heads]
        out_ref[:, heads] = (normed * gate_open[:, heads]).astype(out_ref.dtype)


def mix(local_a, local_b, queries, gates, prefix_hi, prefix_lo, gain):
    tokens, columns = queries.shape
    heads = columns // HD
    whole_state = pl.BlockSpec((heads, HD, HD), lambda i: (0, 0, 0))
    return pl.pallas_call(
        mix_kernel,
        grid=(tokens // ROW_TILE,),
        in_specs=[
            row_block(local_a.shape[1]),
            row_block(local_b.shape[1]),
            row_block(columns),
            row_block(columns),
            whole_state,
            whole_state,
            pl.BlockSpec((1, columns), lambda i: (0, 0)),
        ],
        out_specs=row_block(columns),
        out_shape=jax.ShapeDtypeStruct((tokens, columns), jnp.bfloat16),
        cost_estimate=pl.CostEstimate(
            flops=4 * tokens * HD * HD * heads,
            transcendentals=2 * tokens * columns,
            bytes_accessed=10 * tokens * columns,
        ),
    )(local_a, local_b, queries, gates, prefix_hi, prefix_lo, gain.reshape(1, columns))


def split_bf16(x):
    hi = x.astype(jnp.bfloat16)
    lo = (x - hi.astype(jnp.float32)).astype(jnp.bfloat16)
    return hi, lo


def shift(block, axis, distance):
    size = lax.axis_size(axis)
    return lax.ppermute(block, axis, [(i, i + distance) for i in range(size) if i + distance < size])


def swap(block, axis):
    return lax.ppermute(block, axis, [(0, 1), (1, 0)])


def exclusive_prefix(state, axis, fillers=()):
    inclusive = state
    exclusive = jnp.zeros_like(state)
    distance = 1
    results = []
    while distance < lax.axis_size(axis):
        sent = inclusive.astype(jnp.bfloat16)
        arrived = shift(sent, axis, distance)
        if len(results) < len(fillers):
            function, operands = fillers[len(results)]
            _, operands = lax.optimization_barrier((sent, operands))
            result = function(*operands)
            arrived, result = lax.optimization_barrier((arrived, result))
            results.append(result)
        arrived = arrived.astype(jnp.float32)
        exclusive = exclusive + arrived
        inclusive = inclusive + arrived
        distance *= 2
    for function, operands in fillers[len(results):]:
        results.append(function(*operands))
    return exclusive, results


def project_and_reduce(mixed_rows, out_weight):
    tokens, columns = mixed_rows.shape
    ty_size = lax.axis_size("ty")
    tc_size = lax.axis_size("tc")
    block = tokens // (ty_size * tc_size)
    width = out_weight.shape[1]

    def product(rows):
        return jnp.dot(rows, out_weight, preferred_element_type=jnp.float32).astype(jnp.bfloat16)

    if ty_size != 2 or tc_size != 2:
        ordered = (
            mixed_rows.reshape(ty_size, tc_size, block, columns)
            .transpose(1, 0, 2, 3)
            .reshape(tokens, columns)
        )
        part = product(ordered)
        part = lax.psum_scatter(part, "tc", scatter_dimension=0, tiled=True)
        return lax.psum_scatter(part, "ty", scatter_dimension=0, tiled=True)

    ty = lax.axis_index("ty")
    tc = lax.axis_index("tc")
    pair = tc_size * block
    far_rows = lax.dynamic_slice_in_dim(mixed_rows, (1 - ty) * pair, pair, axis=0)
    near_rows = lax.dynamic_slice_in_dim(mixed_rows, ty * pair, pair, axis=0)

    def block_of(part, owner_tc):
        return lax.dynamic_slice_in_dim(part, owner_tc * block, block, axis=0)

    chunk = width // COLUMN_CHUNKS
    chip_sums = []
    for c in range(COLUMN_CHUNKS):
        far_part = jnp.dot(
            far_rows, out_weight[:, c * chunk:(c + 1) * chunk], preferred_element_type=jnp.float32
        ).astype(jnp.bfloat16)
        from_partner = swap(block_of(far_part, 1 - tc), "tc")
        chip_sum = block_of(far_part, tc).astype(jnp.float32) + from_partner.astype(jnp.float32)
        chip_sums.append(chip_sum.astype(jnp.bfloat16))
    chip_sums, near_rows = lax.optimization_barrier((chip_sums, near_rows))
    across = [swap(chip_sum, "ty") for chip_sum in chip_sums]
    near = swap(product(block_of(near_rows, 1 - tc)), "tc")
    mine = lax.optimization_barrier(product(block_of(near_rows, tc)))
    far = jnp.concatenate(across, axis=1)
    total = mine.astype(jnp.float32) + near.astype(jnp.float32) + far.astype(jnp.float32)
    return total.astype(jnp.bfloat16)


def on_device(queries, keys, values, gates, gain, out_weight):
    own_state = key_value_states(keys, values)
    head_count = queries.shape[1] // HD
    first = (head_count + 1) // 2
    fillers = (
        (lambda q, k, v: local_attention(q, k, v, 0, first), (queries, keys, values)),
        (lambda q, k, v: local_attention(q, k, v, first, head_count - first), (queries, keys, values)),
    )
    prefix, (local_a, local_b) = exclusive_prefix(own_state, "ctx", fillers)
    prefix_hi, prefix_lo = split_bf16(prefix)
    mixed_rows = mix(local_a, local_b, queries, gates, prefix_hi, prefix_lo, gain)
    return project_and_reduce(mixed_rows, out_weight)


def solution(mesh):
    ctx_size, tp_size = mesh.devices.shape
    split = Mesh(
        np.asarray(mesh.devices).reshape(ctx_size, tp_size // 2, 2), ("ctx", "ty", "tc")
    )
    tp = ("ty", "tc")
    return jax.shard_map(
        on_device,
        mesh=split,
        in_specs=(
            P("ctx", tp),
            P("ctx", tp),
            P("ctx", tp),
            P("ctx", tp),
            P(tp),
            P(tp, None),
        ),
        out_specs=P(("ctx",) + tp, None),
        check_vma=False,
    )
```

```python
import jax
import jax.numpy as jnp
import numpy as np
from jax import lax
from jax.experimental import pallas as pl
from jax.experimental.pallas import tpu as pltpu
from jax.sharding import Mesh
from jax.sharding import PartitionSpec as P

HD = 128
COLUMN_CHUNKS = 3
QUERY_TILE = 256
ROW_TILE = 256


epsilon = 1e-05


def silu(x):
    x = x.astype(jnp.float32)
    return (x / (1.0 + jnp.exp(-x))).astype(jnp.bfloat16)


def head_block(tokens):
    return pl.BlockSpec((tokens, HD), lambda h: (0, h))


def state_kernel(k_ref, v_ref, state_ref):
    @pl.when(pl.program_id(0) == 0)
    def _():
        state_ref[...] = jnp.zeros_like(state_ref)

    key_act = silu(k_ref[...])
    value_rows = v_ref[...]
    for h in range(state_ref.shape[0]):
        heads = slice(h * HD, (h + 1) * HD)
        state_ref[h] += lax.dot_general(
            key_act[:, heads], value_rows[:, heads], (((0,), (0,)), ((), ())),
            preferred_element_type=jnp.float32,
        )


def row_block(columns):
    return pl.BlockSpec((ROW_TILE, columns), lambda i: (i, 0))


def key_value_states(keys, values):
    tokens, columns = keys.shape
    heads = columns // HD
    return pl.pallas_call(
        state_kernel,
        grid=(tokens // ROW_TILE,),
        in_specs=[row_block(columns), row_block(columns)],
        out_specs=pl.BlockSpec((heads, HD, HD), lambda i: (0, 0, 0)),
        out_shape=jax.ShapeDtypeStruct((heads, HD, HD), jnp.float32),
        cost_estimate=pl.CostEstimate(
            flops=2 * tokens * HD * HD * heads,
            transcendentals=tokens * columns,
            bytes_accessed=4 * tokens * columns + 4 * heads * HD * HD,
        ),
    )(keys, values)


def local_kernel(q_ref, k_ref, v_ref, out_ref):
    tokens = q_ref.shape[0]
    query_act = silu(q_ref[...])
    key_act = silu(k_ref[...])
    value_rows = v_ref[...]
    for tile in range(tokens // QUERY_TILE):
        seen = (tile + 1) * QUERY_TILE
        scores = lax.dot_general(
            query_act[tile * QUERY_TILE:seen],
            key_act[:seen],
            (((1,), (1,)), ((), ())),
            preferred_element_type=jnp.float32,
        )
        row = lax.broadcasted_iota(jnp.int32, scores.shape, 0) + tile * QUERY_TILE
        col = lax.broadcasted_iota(jnp.int32, scores.shape, 1)
        scores = jnp.where(row >= col, scores, 0.0).astype(jnp.bfloat16)
        out_ref[tile * QUERY_TILE:seen, :] = jnp.dot(
            scores, value_rows[:seen], preferred_element_type=jnp.float32
        )


def local_attention(queries, keys, values, first_head, heads):
    tokens, columns = queries.shape
    tiles = tokens // QUERY_TILE
    pairs = QUERY_TILE * QUERY_TILE * tiles * (tiles + 1) // 2
    picked = pl.BlockSpec((tokens, HD), lambda h: (0, h + first_head))
    return pl.pallas_call(
        local_kernel,
        grid=(heads,),
        in_specs=[picked] * 3,
        out_specs=head_block(tokens),
        out_shape=jax.ShapeDtypeStruct((tokens, heads * HD), jnp.float32),
        cost_estimate=pl.CostEstimate(
            flops=4 * pairs * HD * heads,
            transcendentals=2 * tokens * heads * HD,
            bytes_accessed=10 * tokens * heads * HD,
        ),
    )(queries, keys, values)


def mix_kernel(order_ref, local_a_ref, local_b_ref, q_ref, g_ref, prefix_ref, gain_ref, out_ref):
    query_act = silu(q_ref[...])
    gates = g_ref[...].astype(jnp.float32)
    gate_open = 1.0 / (1.0 + jnp.exp(-gates))
    first = local_a_ref.shape[1] // HD
    for h in range(prefix_ref.shape[0]):
        heads = slice(h * HD, (h + 1) * HD)
        if h < first:
            local = local_a_ref[:, heads]
        else:
            local = local_b_ref[:, (h - first) * HD:(h - first + 1) * HD]
        prefix_hi, prefix_lo = split_bf16(prefix_ref[h])
        remote = jnp.dot(query_act[:, heads], prefix_hi, preferred_element_type=jnp.float32) + jnp.dot(
            query_act[:, heads], prefix_lo, preferred_element_type=jnp.float32
        )
        attention = local + remote
        mean_sq = jnp.mean(attention * attention, axis=-1, keepdims=True)
        normed = attention * lax.rsqrt(mean_sq + epsilon) * gain_ref[:, heads]
        out_ref[:, heads] = (normed * gate_open[:, heads]).astype(out_ref.dtype)


def mix(order, local_a, local_b, queries, gates, prefix, gain):
    tokens, columns = queries.shape
    heads = columns // HD

    def picked(width):
        return pl.BlockSpec((ROW_TILE, width), lambda i, order: (order[i], 0))

    return pl.pallas_call(
        mix_kernel,
        grid_spec=pltpu.PrefetchScalarGridSpec(
            num_scalar_prefetch=1,
            grid=(tokens // ROW_TILE,),
            in_specs=[
                picked(local_a.shape[1]),
                picked(local_b.shape[1]),
                picked(columns),
                picked(columns),
                pl.BlockSpec((heads, HD, HD), lambda i, order: (0, 0, 0)),
                pl.BlockSpec((1, columns), lambda i, order: (0, 0)),
            ],
            out_specs=pl.BlockSpec((ROW_TILE, columns), lambda i, order: (i, 0)),
        ),
        out_shape=jax.ShapeDtypeStruct((tokens, columns), jnp.bfloat16),
        cost_estimate=pl.CostEstimate(
            flops=4 * tokens * HD * HD * heads,
            transcendentals=2 * tokens * columns,
            bytes_accessed=10 * tokens * columns,
        ),
    )(order, local_a, local_b, queries, gates, prefix, gain.reshape(1, columns))


def split_bf16(x):
    hi = x.astype(jnp.bfloat16)
    lo = (x - hi.astype(jnp.float32)).astype(jnp.bfloat16)
    return hi, lo


def shift(block, axis, distance):
    size = lax.axis_size(axis)
    return lax.ppermute(block, axis, [(i, i + distance) for i in range(size) if i + distance < size])


def swap(block, axis):
    return lax.ppermute(block, axis, [(0, 1), (1, 0)])


def exclusive_prefix(state, axis, fillers=()):
    inclusive = state
    exclusive = jnp.zeros_like(state)
    distance = 1
    results = []
    while distance < lax.axis_size(axis):
        sent = inclusive.astype(jnp.bfloat16)
        arrived = shift(sent, axis, distance)
        if len(results) < len(fillers):
            function, operands = fillers[len(results)]
            _, operands = lax.optimization_barrier((sent, operands))
            result = function(*operands)
            arrived, result = lax.optimization_barrier((arrived, result))
            results.append(result)
        arrived = arrived.astype(jnp.float32)
        exclusive = exclusive + arrived
        inclusive = inclusive + arrived
        distance *= 2
    for function, operands in fillers[len(results):]:
        results.append(function(*operands))
    return exclusive, results


def reduce_order(tokens):
    ty_size = lax.axis_size("ty")
    tc_size = lax.axis_size("tc")
    tiles = tokens // ROW_TILE
    if ty_size != 2 or tc_size != 2 or tiles != 4:
        return jnp.arange(tiles, dtype=jnp.int32)
    ty = lax.axis_index("ty")
    tc = lax.axis_index("tc")
    return jnp.stack(
        [(1 - ty) * 2 + 1 - tc, (1 - ty) * 2 + tc, ty * 2 + 1 - tc, ty * 2 + tc]
    ).astype(jnp.int32)


def project_and_reduce(mixed_rows, out_weight):
    tokens, columns = mixed_rows.shape
    ty_size = lax.axis_size("ty")
    tc_size = lax.axis_size("tc")
    block = tokens // (ty_size * tc_size)
    width = out_weight.shape[1]

    def product(rows):
        return jnp.dot(rows, out_weight, preferred_element_type=jnp.float32).astype(jnp.bfloat16)

    if ty_size != 2 or tc_size != 2 or block != ROW_TILE:
        ordered = (
            mixed_rows.reshape(ty_size, tc_size, block, columns)
            .transpose(1, 0, 2, 3)
            .reshape(tokens, columns)
        )
        part = product(ordered)
        part = lax.psum_scatter(part, "tc", scatter_dimension=0, tiled=True)
        return lax.psum_scatter(part, "ty", scatter_dimension=0, tiled=True)

    far_rows = mixed_rows[:2 * block]
    partner_rows = mixed_rows[2 * block:3 * block]
    own_rows = mixed_rows[3 * block:]
    chunk = width // COLUMN_CHUNKS
    chip_sums = []
    for c in range(COLUMN_CHUNKS):
        far_part = jnp.dot(
            far_rows, out_weight[:, c * chunk:(c + 1) * chunk], preferred_element_type=jnp.float32
        ).astype(jnp.bfloat16)
        from_partner = swap(far_part[:block], "tc")
        chip_sum = far_part[block:].astype(jnp.float32) + from_partner.astype(jnp.float32)
        chip_sums.append(chip_sum.astype(jnp.bfloat16))
    chip_sums, partner_rows, own_rows = lax.optimization_barrier((chip_sums, partner_rows, own_rows))
    across = [swap(chip_sum, "ty") for chip_sum in chip_sums]
    near = swap(product(partner_rows), "tc")
    mine = lax.optimization_barrier(product(own_rows))
    far = jnp.concatenate(across, axis=1)
    total = mine.astype(jnp.float32) + near.astype(jnp.float32) + far.astype(jnp.float32)
    return total.astype(jnp.bfloat16)


def on_device(queries, keys, values, gates, gain, out_weight):
    own_state = key_value_states(keys, values)
    head_count = queries.shape[1] // HD
    first = (head_count + 1) // 2
    fillers = (
        (lambda q, k, v: local_attention(q, k, v, 0, first), (queries, keys, values)),
        (lambda q, k, v: local_attention(q, k, v, first, head_count - first), (queries, keys, values)),
    )
    prefix, (local_a, local_b) = exclusive_prefix(own_state, "ctx", fillers)
    mixed_rows = mix(reduce_order(queries.shape[0]), local_a, local_b, queries, gates, prefix, gain)
    return project_and_reduce(mixed_rows, out_weight)


def solution(mesh):
    ctx_size, tp_size = mesh.devices.shape
    split = Mesh(
        np.asarray(mesh.devices).reshape(ctx_size, tp_size // 2, 2), ("ctx", "ty", "tc")
    )
    tp = ("ty", "tc")
    return jax.shard_map(
        on_device,
        mesh=split,
        in_specs=(
            P("ctx", tp),
            P("ctx", tp),
            P("ctx", tp),
            P("ctx", tp),
            P(tp),
            P(tp, None),
        ),
        out_specs=P(("ctx",) + tp, None),
        check_vma=False,
    )
```

```python
import jax
import jax.numpy as jnp
import numpy as np
from jax import lax
from jax.experimental import pallas as pl
from jax.experimental.pallas import tpu as pltpu
from jax.sharding import Mesh
from jax.sharding import PartitionSpec as P

HD = 128
COLUMN_CHUNKS = 3
QUERY_TILE = 256
ROW_TILE = 256


epsilon = 1e-05


def silu(x):
    x = x.astype(jnp.float32)
    return (x / (1.0 + jnp.exp(-x))).astype(jnp.bfloat16)


def head_block(tokens):
    return pl.BlockSpec((tokens, HD), lambda h: (0, h))


def state_kernel(k_ref, v_ref, state_ref):
    @pl.when(pl.program_id(0) == 0)
    def _():
        state_ref[...] = jnp.zeros_like(state_ref)

    key_act = silu(k_ref[...])
    value_rows = v_ref[...]
    for h in range(state_ref.shape[0]):
        heads = slice(h * HD, (h + 1) * HD)
        state_ref[h] += lax.dot_general(
            key_act[:, heads], value_rows[:, heads], (((0,), (0,)), ((), ())),
            preferred_element_type=jnp.float32,
        )


def row_block(columns):
    return pl.BlockSpec((ROW_TILE, columns), lambda i: (i, 0))


def key_value_states(keys, values):
    tokens, columns = keys.shape
    heads = columns // HD
    return pl.pallas_call(
        state_kernel,
        grid=(tokens // ROW_TILE,),
        in_specs=[row_block(columns), row_block(columns)],
        out_specs=pl.BlockSpec((heads, HD, HD), lambda i: (0, 0, 0)),
        out_shape=jax.ShapeDtypeStruct((heads, HD, HD), jnp.float32),
        cost_estimate=pl.CostEstimate(
            flops=2 * tokens * HD * HD * heads,
            transcendentals=tokens * columns,
            bytes_accessed=4 * tokens * columns + 4 * heads * HD * HD,
        ),
    )(keys, values)


def local_kernel(q_ref, k_ref, v_ref, out_ref):
    tokens = q_ref.shape[0]
    query_act = silu(q_ref[...])
    key_act = silu(k_ref[...])
    value_rows = v_ref[...]
    for tile in range(tokens // QUERY_TILE):
        seen = (tile + 1) * QUERY_TILE
        scores = lax.dot_general(
            query_act[tile * QUERY_TILE:seen],
            key_act[:seen],
            (((1,), (1,)), ((), ())),
            preferred_element_type=jnp.float32,
        )
        row = lax.broadcasted_iota(jnp.int32, scores.shape, 0) + tile * QUERY_TILE
        col = lax.broadcasted_iota(jnp.int32, scores.shape, 1)
        scores = jnp.where(row >= col, scores, 0.0).astype(jnp.bfloat16)
        out_ref[tile * QUERY_TILE:seen, :] = jnp.dot(
            scores, value_rows[:seen], preferred_element_type=jnp.float32
        )


def local_attention(queries, keys, values, first_head, heads):
    tokens, columns = queries.shape
    tiles = tokens // QUERY_TILE
    pairs = QUERY_TILE * QUERY_TILE * tiles * (tiles + 1) // 2
    picked = pl.BlockSpec((tokens, HD), lambda h: (0, h + first_head))
    return pl.pallas_call(
        local_kernel,
        grid=(heads,),
        in_specs=[picked] * 3,
        out_specs=head_block(tokens),
        out_shape=jax.ShapeDtypeStruct((tokens, heads * HD), jnp.float32),
        cost_estimate=pl.CostEstimate(
            flops=4 * pairs * HD * heads,
            transcendentals=2 * tokens * heads * HD,
            bytes_accessed=10 * tokens * heads * HD,
        ),
    )(queries, keys, values)


def mix_kernel(order_ref, local_a_ref, local_b_ref, q_ref, g_ref, prefix_ref, gain_ref, out_ref):
    query_act = silu(q_ref[...])
    gates = g_ref[...].astype(jnp.float32)
    gate_open = 1.0 / (1.0 + jnp.exp(-gates))
    first = local_a_ref.shape[1] // HD
    for h in range(prefix_ref.shape[0]):
        heads = slice(h * HD, (h + 1) * HD)
        if h < first:
            local = local_a_ref[:, heads]
        else:
            local = local_b_ref[:, (h - first) * HD:(h - first + 1) * HD]
        prefix_hi, prefix_lo = split_bf16(prefix_ref[h])
        remote = jnp.dot(query_act[:, heads], prefix_hi, preferred_element_type=jnp.float32) + jnp.dot(
            query_act[:, heads], prefix_lo, preferred_element_type=jnp.float32
        )
        attention = local + remote
        mean_sq = jnp.mean(attention * attention, axis=-1, keepdims=True)
        normed = attention * lax.rsqrt(mean_sq + epsilon) * gain_ref[:, heads]
        out_ref[:, heads] = (normed * gate_open[:, heads]).astype(out_ref.dtype)


def mix(order, local_a, local_b, queries, gates, prefix, gain):
    tokens, columns = queries.shape
    heads = columns // HD

    def picked(width):
        return pl.BlockSpec((ROW_TILE, width), lambda i, order: (order[i], 0))

    return pl.pallas_call(
        mix_kernel,
        grid_spec=pltpu.PrefetchScalarGridSpec(
            num_scalar_prefetch=1,
            grid=(tokens // ROW_TILE,),
            in_specs=[
                picked(local_a.shape[1]),
                picked(local_b.shape[1]),
                picked(columns),
                picked(columns),
                pl.BlockSpec((heads, HD, HD), lambda i, order: (0, 0, 0)),
                pl.BlockSpec((1, columns), lambda i, order: (0, 0)),
            ],
            out_specs=pl.BlockSpec((ROW_TILE, columns), lambda i, order: (i, 0)),
        ),
        out_shape=jax.ShapeDtypeStruct((tokens, columns), jnp.bfloat16),
        cost_estimate=pl.CostEstimate(
            flops=4 * tokens * HD * HD * heads,
            transcendentals=2 * tokens * columns,
            bytes_accessed=10 * tokens * columns,
        ),
    )(order, local_a, local_b, queries, gates, prefix, gain.reshape(1, columns))


def split_bf16(x):
    hi = x.astype(jnp.bfloat16)
    lo = (x - hi.astype(jnp.float32)).astype(jnp.bfloat16)
    return hi, lo


def shift(block, axis, distance):
    size = lax.axis_size(axis)
    return lax.ppermute(block, axis, [(i, i + distance) for i in range(size) if i + distance < size])


def swap(block, axis):
    return lax.ppermute(block, axis, [(0, 1), (1, 0)])


def exclusive_prefix(state, axis, fillers=()):
    inclusive = state
    exclusive = jnp.zeros_like(state)
    distance = 1
    results = []
    while distance < lax.axis_size(axis):
        sent = inclusive.astype(jnp.bfloat16)
        arrived = shift(sent, axis, distance)
        if len(results) < len(fillers):
            function, operands = fillers[len(results)]
            _, operands = lax.optimization_barrier((sent, operands))
            result = function(*operands)
            arrived, result = lax.optimization_barrier((arrived, result))
            results.append(result)
        arrived = arrived.astype(jnp.float32)
        exclusive = exclusive + arrived
        inclusive = inclusive + arrived
        distance *= 2
    for function, operands in fillers[len(results):]:
        results.append(function(*operands))
    return exclusive, results


def reduce_order(tokens):
    ty_size = lax.axis_size("ty")
    tc_size = lax.axis_size("tc")
    tiles = tokens // ROW_TILE
    if ty_size != 2 or tc_size != 2 or tiles != 4:
        return jnp.arange(tiles, dtype=jnp.int32)
    ty = lax.axis_index("ty")
    tc = lax.axis_index("tc")
    return jnp.stack(
        [(1 - ty) * 2 + 1 - tc, (1 - ty) * 2 + tc, ty * 2 + 1 - tc, ty * 2 + tc]
    ).astype(jnp.int32)


PRODUCT_TILE = 512


def early_product_kernel(far_ref, near_ref, w_ref, far_out_ref, near_out_ref):
    weight = w_ref[...]
    far_out_ref[...] = jnp.dot(far_ref[...], weight, preferred_element_type=jnp.float32).astype(
        far_out_ref.dtype
    )
    near_out_ref[...] = jnp.dot(near_ref[...], weight, preferred_element_type=jnp.float32).astype(
        near_out_ref.dtype
    )


def early_products(mixed_rows, out_weight, block, first_column, width):
    columns = mixed_rows.shape[1]
    tiles = width // PRODUCT_TILE
    offset = first_column // PRODUCT_TILE
    return pl.pallas_call(
        early_product_kernel,
        grid=(tiles,),
        in_specs=[
            pl.BlockSpec((2 * block, columns), lambda j: (0, 0)),
            pl.BlockSpec((block, columns), lambda j: (2, 0)),
            pl.BlockSpec((columns, PRODUCT_TILE), lambda j: (0, j + offset)),
        ],
        out_specs=[
            pl.BlockSpec((2 * block, PRODUCT_TILE), lambda j: (0, j)),
            pl.BlockSpec((block, PRODUCT_TILE), lambda j: (0, j)),
        ],
        out_shape=[
            jax.ShapeDtypeStruct((2 * block, width), jnp.bfloat16),
            jax.ShapeDtypeStruct((block, width), jnp.bfloat16),
        ],
        cost_estimate=pl.CostEstimate(
            flops=2 * 3 * block * columns * width,
            transcendentals=0,
            bytes_accessed=2 * (3 * block * columns + columns * width + 3 * block * width),
        ),
    )(mixed_rows, mixed_rows, out_weight)


def project_and_reduce(mixed_rows, out_weight):
    tokens, columns = mixed_rows.shape
    ty_size = lax.axis_size("ty")
    tc_size = lax.axis_size("tc")
    block = tokens // (ty_size * tc_size)
    width = out_weight.shape[1]

    def product(rows):
        return jnp.dot(rows, out_weight, preferred_element_type=jnp.float32).astype(jnp.bfloat16)

    if ty_size != 2 or tc_size != 2 or block != ROW_TILE:
        ordered = (
            mixed_rows.reshape(ty_size, tc_size, block, columns)
            .transpose(1, 0, 2, 3)
            .reshape(tokens, columns)
        )
        part = product(ordered)
        part = lax.psum_scatter(part, "tc", scatter_dimension=0, tiled=True)
        return lax.psum_scatter(part, "ty", scatter_dimension=0, tiled=True)

    own_rows = mixed_rows[3 * block:]
    chunk = width // COLUMN_CHUNKS
    chip_sums = []
    near_parts = []
    for c in range(COLUMN_CHUNKS):
        far_part, near_part = early_products(mixed_rows, out_weight, block, c * chunk, chunk)
        from_partner = swap(far_part[:block], "tc")
        chip_sum = far_part[block:].astype(jnp.float32) + from_partner.astype(jnp.float32)
        chip_sums.append(chip_sum.astype(jnp.bfloat16))
        near_parts.append(near_part)
    chip_sums, near_parts, own_rows = lax.optimization_barrier((chip_sums, near_parts, own_rows))
    across = [swap(chip_sum, "ty") for chip_sum in chip_sums]
    near = swap(jnp.concatenate(near_parts, axis=1), "tc")
    mine = lax.optimization_barrier(product(own_rows))
    far = jnp.concatenate(across, axis=1)
    total = mine.astype(jnp.float32) + near.astype(jnp.float32) + far.astype(jnp.float32)
    return total.astype(jnp.bfloat16)


def on_device(queries, keys, values, gates, gain, out_weight):
    own_state = key_value_states(keys, values)
    head_count = queries.shape[1] // HD
    first = (head_count + 1) // 2
    fillers = (
        (lambda q, k, v: local_attention(q, k, v, 0, first), (queries, keys, values)),
        (lambda q, k, v: local_attention(q, k, v, first, head_count - first), (queries, keys, values)),
    )
    prefix, (local_a, local_b) = exclusive_prefix(own_state, "ctx", fillers)
    mixed_rows = mix(reduce_order(queries.shape[0]), local_a, local_b, queries, gates, prefix, gain)
    return project_and_reduce(mixed_rows, out_weight)


def solution(mesh):
    ctx_size, tp_size = mesh.devices.shape
    split = Mesh(
        np.asarray(mesh.devices).reshape(ctx_size, tp_size // 2, 2), ("ctx", "ty", "tc")
    )
    tp = ("ty", "tc")
    return jax.shard_map(
        on_device,
        mesh=split,
        in_specs=(
            P("ctx", tp),
            P("ctx", tp),
            P("ctx", tp),
            P("ctx", tp),
            P(tp),
            P(tp, None),
        ),
        out_specs=P(("ctx",) + tp, None),
        check_vma=False,
    )
```

```python
import jax
import jax.numpy as jnp
import numpy as np
from jax import lax
from jax.experimental import pallas as pl
from jax.experimental.pallas import tpu as pltpu
from jax.sharding import Mesh
from jax.sharding import PartitionSpec as P

HD = 128
COLUMN_CHUNKS = 3
QUERY_TILE = 256
ROW_TILE = 256


epsilon = 1e-05


def silu(x):
    x = x.astype(jnp.float32)
    return (x / (1.0 + jnp.exp(-x))).astype(jnp.bfloat16)


def head_block(tokens):
    return pl.BlockSpec((tokens, HD), lambda h: (0, h))


def state_kernel(k_ref, v_ref, state_ref):
    @pl.when(pl.program_id(0) == 0)
    def _():
        state_ref[...] = jnp.zeros_like(state_ref)

    key_act = silu(k_ref[...])
    value_rows = v_ref[...]
    for h in range(state_ref.shape[0]):
        heads = slice(h * HD, (h + 1) * HD)
        state_ref[h] += lax.dot_general(
            key_act[:, heads], value_rows[:, heads], (((0,), (0,)), ((), ())),
            preferred_element_type=jnp.float32,
        )


def row_block(columns):
    return pl.BlockSpec((ROW_TILE, columns), lambda i: (i, 0))


def key_value_states(keys, values):
    tokens, columns = keys.shape
    heads = columns // HD
    return pl.pallas_call(
        state_kernel,
        grid=(tokens // ROW_TILE,),
        in_specs=[row_block(columns), row_block(columns)],
        out_specs=pl.BlockSpec((heads, HD, HD), lambda i: (0, 0, 0)),
        out_shape=jax.ShapeDtypeStruct((heads, HD, HD), jnp.float32),
        cost_estimate=pl.CostEstimate(
            flops=2 * tokens * HD * HD * heads,
            transcendentals=tokens * columns,
            bytes_accessed=4 * tokens * columns + 4 * heads * HD * HD,
        ),
    )(keys, values)


def local_kernel(q_ref, k_ref, v_ref, out_ref):
    tokens = q_ref.shape[0]
    query_act = silu(q_ref[...])
    key_act = silu(k_ref[...])
    value_rows = v_ref[...]
    for tile in range(tokens // QUERY_TILE):
        seen = (tile + 1) * QUERY_TILE
        scores = lax.dot_general(
            query_act[tile * QUERY_TILE:seen],
            key_act[:seen],
            (((1,), (1,)), ((), ())),
            preferred_element_type=jnp.float32,
        )
        row = lax.broadcasted_iota(jnp.int32, scores.shape, 0) + tile * QUERY_TILE
        col = lax.broadcasted_iota(jnp.int32, scores.shape, 1)
        scores = jnp.where(row >= col, scores, 0.0).astype(jnp.bfloat16)
        out_ref[tile * QUERY_TILE:seen, :] = jnp.dot(
            scores, value_rows[:seen], preferred_element_type=jnp.float32
        )


def local_attention(queries, keys, values, first_head, heads):
    tokens, columns = queries.shape
    tiles = tokens // QUERY_TILE
    pairs = QUERY_TILE * QUERY_TILE * tiles * (tiles + 1) // 2
    picked = pl.BlockSpec((tokens, HD), lambda h: (0, h + first_head))
    return pl.pallas_call(
        local_kernel,
        grid=(heads,),
        in_specs=[picked] * 3,
        out_specs=head_block(tokens),
        out_shape=jax.ShapeDtypeStruct((tokens, heads * HD), jnp.float32),
        cost_estimate=pl.CostEstimate(
            flops=4 * pairs * HD * heads,
            transcendentals=2 * tokens * heads * HD,
            bytes_accessed=10 * tokens * heads * HD,
        ),
    )(queries, keys, values)


def gate_kernel(q_ref, g_ref, gain_ref, query_act_ref, scale_ref):
    query_act_ref[...] = silu(q_ref[...])
    gates = g_ref[...].astype(jnp.float32)
    scale_ref[...] = gain_ref[...] * (1.0 / (1.0 + jnp.exp(-gates)))


def query_and_gate(queries, gates, gain):
    tokens, columns = queries.shape
    return pl.pallas_call(
        gate_kernel,
        grid=(tokens // ROW_TILE,),
        in_specs=[row_block(columns), row_block(columns), pl.BlockSpec((1, columns), lambda i: (0, 0))],
        out_specs=[row_block(columns), row_block(columns)],
        out_shape=[
            jax.ShapeDtypeStruct((tokens, columns), jnp.bfloat16),
            jax.ShapeDtypeStruct((tokens, columns), jnp.float32),
        ],
        cost_estimate=pl.CostEstimate(
            flops=8 * tokens * columns,
            transcendentals=2 * tokens * columns,
            bytes_accessed=10 * tokens * columns,
        ),
    )(queries, gates, gain.reshape(1, columns))


def mix_kernel(local_a_ref, local_b_ref, q_ref, scale_ref, hi_ref, lo_ref, out_ref):
    query_act = q_ref[...]
    first = local_a_ref.shape[1] // HD
    for h in range(hi_ref.shape[0]):
        heads = slice(h * HD, (h + 1) * HD)
        if h < first:
            local = local_a_ref[:, heads]
        else:
            local = local_b_ref[:, (h - first) * HD:(h - first + 1) * HD]
        remote = jnp.dot(query_act[:, heads], hi_ref[h], preferred_element_type=jnp.float32) + jnp.dot(
            query_act[:, heads], lo_ref[h], preferred_element_type=jnp.float32
        )
        attention = local + remote
        mean_sq = jnp.mean(attention * attention, axis=-1, keepdims=True)
        out_ref[:, heads] = (attention * lax.rsqrt(mean_sq + epsilon) * scale_ref[:, heads]).astype(
            out_ref.dtype
        )


def mix(local_a, local_b, query_act, scale, prefix_hi, prefix_lo):
    tokens, columns = query_act.shape
    heads = columns // HD
    whole_state = pl.BlockSpec((heads, HD, HD), lambda i: (0, 0, 0))
    return pl.pallas_call(
        mix_kernel,
        grid=(tokens // ROW_TILE,),
        in_specs=[
            row_block(local_a.shape[1]),
            row_block(local_b.shape[1]),
            row_block(columns),
            row_block(columns),
            whole_state,
            whole_state,
        ],
        out_specs=row_block(columns),
        out_shape=jax.ShapeDtypeStruct((tokens, columns), jnp.bfloat16),
        cost_estimate=pl.CostEstimate(
            flops=4 * tokens * HD * HD * heads,
            transcendentals=tokens * heads,
            bytes_accessed=12 * tokens * columns,
        ),
    )(local_a, local_b, query_act, scale, prefix_hi, prefix_lo)


def split_bf16(x):
    hi = x.astype(jnp.bfloat16)
    lo = (x - hi.astype(jnp.float32)).astype(jnp.bfloat16)
    return hi, lo


def shift(block, axis, distance):
    size = lax.axis_size(axis)
    return lax.ppermute(block, axis, [(i, i + distance) for i in range(size) if i + distance < size])


def swap(block, axis):
    return lax.ppermute(block, axis, [(0, 1), (1, 0)])


def exclusive_prefix(state, axis, fillers=()):
    inclusive = state
    exclusive = jnp.zeros_like(state)
    distance = 1
    results = []
    while distance < lax.axis_size(axis):
        sent = inclusive.astype(jnp.bfloat16)
        arrived = shift(sent, axis, distance)
        if len(results) < len(fillers):
            function, operands = fillers[len(results)]
            _, operands = lax.optimization_barrier((sent, operands))
            result = function(*operands)
            arrived, result = lax.optimization_barrier((arrived, result))
            results.append(result)
        arrived = arrived.astype(jnp.float32)
        exclusive = exclusive + arrived
        inclusive = inclusive + arrived
        distance *= 2
    for function, operands in fillers[len(results):]:
        results.append(function(*operands))
    return exclusive, results


def project_and_reduce(mixed_rows, out_weight):
    tokens, columns = mixed_rows.shape
    ty_size = lax.axis_size("ty")
    tc_size = lax.axis_size("tc")
    block = tokens // (ty_size * tc_size)
    width = out_weight.shape[1]

    def product(rows):
        return jnp.dot(rows, out_weight, preferred_element_type=jnp.float32).astype(jnp.bfloat16)

    if ty_size != 2 or tc_size != 2:
        ordered = (
            mixed_rows.reshape(ty_size, tc_size, block, columns)
            .transpose(1, 0, 2, 3)
            .reshape(tokens, columns)
        )
        part = product(ordered)
        part = lax.psum_scatter(part, "tc", scatter_dimension=0, tiled=True)
        return lax.psum_scatter(part, "ty", scatter_dimension=0, tiled=True)

    ty = lax.axis_index("ty")
    tc = lax.axis_index("tc")
    pair = tc_size * block
    far_rows = lax.dynamic_slice_in_dim(mixed_rows, (1 - ty) * pair, pair, axis=0)
    near_rows = lax.dynamic_slice_in_dim(mixed_rows, ty * pair, pair, axis=0)

    def block_of(part, owner_tc):
        return lax.dynamic_slice_in_dim(part, owner_tc * block, block, axis=0)

    chunk = width // COLUMN_CHUNKS
    chip_sums = []
    for c in range(COLUMN_CHUNKS):
        far_part = jnp.dot(
            far_rows, out_weight[:, c * chunk:(c + 1) * chunk], preferred_element_type=jnp.float32
        ).astype(jnp.bfloat16)
        from_partner = swap(block_of(far_part, 1 - tc), "tc")
        chip_sum = block_of(far_part, tc).astype(jnp.float32) + from_partner.astype(jnp.float32)
        chip_sums.append(chip_sum.astype(jnp.bfloat16))
    chip_sums, near_rows = lax.optimization_barrier((chip_sums, near_rows))
    across = [swap(chip_sum, "ty") for chip_sum in chip_sums]
    near = swap(product(block_of(near_rows, 1 - tc)), "tc")
    mine = lax.optimization_barrier(product(block_of(near_rows, tc)))
    far = jnp.concatenate(across, axis=1)
    total = mine.astype(jnp.float32) + near.astype(jnp.float32) + far.astype(jnp.float32)
    return total.astype(jnp.bfloat16)


def on_device(queries, keys, values, gates, gain, out_weight):
    own_state = key_value_states(keys, values)
    head_count = queries.shape[1] // HD
    first = (head_count + 1) // 2
    fillers = (
        (lambda q, k, v: local_attention(q, k, v, 0, first), (queries, keys, values)),
        (lambda q, k, v: local_attention(q, k, v, first, head_count - first), (queries, keys, values)),
        (query_and_gate, (queries, gates, gain)),
    )
    prefix, (local_a, local_b, (query_act, scale)) = exclusive_prefix(own_state, "ctx", fillers)
    prefix_hi, prefix_lo = split_bf16(prefix)
    mixed_rows = mix(local_a, local_b, query_act, scale, prefix_hi, prefix_lo)
    return project_and_reduce(mixed_rows, out_weight)


def solution(mesh):
    ctx_size, tp_size = mesh.devices.shape
    split = Mesh(
        np.asarray(mesh.devices).reshape(ctx_size, tp_size // 2, 2), ("ctx", "ty", "tc")
    )
    tp = ("ty", "tc")
    return jax.shard_map(
        on_device,
        mesh=split,
        in_specs=(
            P("ctx", tp),
            P("ctx", tp),
            P("ctx", tp),
            P("ctx", tp),
            P(tp),
            P(tp, None),
        ),
        out_specs=P(("ctx",) + tp, None),
        check_vma=False,
    )
```

```python
import jax
import jax.numpy as jnp
import numpy as np
from jax import lax
from jax.experimental import pallas as pl
from jax.experimental.pallas import tpu as pltpu
from jax.sharding import Mesh
from jax.sharding import PartitionSpec as P

HD = 128
COLUMN_CHUNKS = 3
QUERY_TILE = 256
ROW_TILE = 256


epsilon = 1e-05


def silu(x):
    x = x.astype(jnp.float32)
    return (x / (1.0 + jnp.exp(-x))).astype(jnp.bfloat16)


def head_block(tokens):
    return pl.BlockSpec((tokens, HD), lambda h: (0, h))


def state_kernel(k_ref, v_ref, state_ref):
    @pl.when(pl.program_id(0) == 0)
    def _():
        state_ref[...] = jnp.zeros_like(state_ref)

    key_act = silu(k_ref[...])
    value_rows = v_ref[...]
    for h in range(state_ref.shape[0]):
        heads = slice(h * HD, (h + 1) * HD)
        state_ref[h] += lax.dot_general(
            key_act[:, heads], value_rows[:, heads], (((0,), (0,)), ((), ())),
            preferred_element_type=jnp.float32,
        )


def row_block(columns):
    return pl.BlockSpec((ROW_TILE, columns), lambda i: (i, 0))


def key_value_states(keys, values):
    tokens, columns = keys.shape
    heads = columns // HD
    return pl.pallas_call(
        state_kernel,
        grid=(tokens // ROW_TILE,),
        in_specs=[row_block(columns), row_block(columns)],
        out_specs=pl.BlockSpec((heads, HD, HD), lambda i: (0, 0, 0)),
        out_shape=jax.ShapeDtypeStruct((heads, HD, HD), jnp.float32),
        cost_estimate=pl.CostEstimate(
            flops=2 * tokens * HD * HD * heads,
            transcendentals=tokens * columns,
            bytes_accessed=4 * tokens * columns + 4 * heads * HD * HD,
        ),
    )(keys, values)


def local_kernel(q_ref, k_ref, v_ref, out_ref):
    tokens = q_ref.shape[0]
    query_act = silu(q_ref[...])
    key_act = silu(k_ref[...])
    value_rows = v_ref[...]
    for tile in range(tokens // QUERY_TILE):
        seen = (tile + 1) * QUERY_TILE
        scores = lax.dot_general(
            query_act[tile * QUERY_TILE:seen],
            key_act[:seen],
            (((1,), (1,)), ((), ())),
            preferred_element_type=jnp.float32,
        )
        row = lax.broadcasted_iota(jnp.int32, scores.shape, 0) + tile * QUERY_TILE
        col = lax.broadcasted_iota(jnp.int32, scores.shape, 1)
        scores = jnp.where(row >= col, scores, 0.0).astype(jnp.bfloat16)
        out_ref[tile * QUERY_TILE:seen, :] = jnp.dot(
            scores, value_rows[:seen], preferred_element_type=jnp.float32
        ).astype(out_ref.dtype)


def local_attention(queries, keys, values, first_head, heads):
    tokens, columns = queries.shape
    tiles = tokens // QUERY_TILE
    pairs = QUERY_TILE * QUERY_TILE * tiles * (tiles + 1) // 2
    picked = pl.BlockSpec((tokens, HD), lambda h: (0, h + first_head))
    return pl.pallas_call(
        local_kernel,
        grid=(heads,),
        in_specs=[picked] * 3,
        out_specs=head_block(tokens),
        out_shape=jax.ShapeDtypeStruct((tokens, heads * HD), jnp.bfloat16),
        cost_estimate=pl.CostEstimate(
            flops=4 * pairs * HD * heads,
            transcendentals=2 * tokens * heads * HD,
            bytes_accessed=10 * tokens * heads * HD,
        ),
    )(queries, keys, values)


def gate_kernel(q_ref, g_ref, gain_ref, query_act_ref, scale_ref):
    query_act_ref[...] = silu(q_ref[...])
    gates = g_ref[...].astype(jnp.float32)
    scale_ref[...] = (gain_ref[...] * (1.0 / (1.0 + jnp.exp(-gates)))).astype(scale_ref.dtype)


def query_and_gate(queries, gates, gain):
    tokens, columns = queries.shape
    return pl.pallas_call(
        gate_kernel,
        grid=(tokens // ROW_TILE,),
        in_specs=[row_block(columns), row_block(columns), pl.BlockSpec((1, columns), lambda i: (0, 0))],
        out_specs=[row_block(columns), row_block(columns)],
        out_shape=[
            jax.ShapeDtypeStruct((tokens, columns), jnp.bfloat16),
            jax.ShapeDtypeStruct((tokens, columns), jnp.bfloat16),
        ],
        cost_estimate=pl.CostEstimate(
            flops=8 * tokens * columns,
            transcendentals=2 * tokens * columns,
            bytes_accessed=10 * tokens * columns,
        ),
    )(queries, gates, gain.reshape(1, columns))


def mix_kernel(local_a_ref, local_b_ref, q_ref, scale_ref, hi_ref, lo_ref, out_ref):
    query_act = q_ref[...]
    first = local_a_ref.shape[1] // HD
    for h in range(hi_ref.shape[0]):
        heads = slice(h * HD, (h + 1) * HD)
        if h < first:
            local = local_a_ref[:, heads]
        else:
            local = local_b_ref[:, (h - first) * HD:(h - first + 1) * HD]
        local = local.astype(jnp.float32)
        remote = jnp.dot(query_act[:, heads], hi_ref[h], preferred_element_type=jnp.float32) + jnp.dot(
            query_act[:, heads], lo_ref[h], preferred_element_type=jnp.float32
        )
        attention = local + remote
        mean_sq = jnp.mean(attention * attention, axis=-1, keepdims=True)
        scale = scale_ref[:, heads].astype(jnp.float32)
        out_ref[:, heads] = (attention * lax.rsqrt(mean_sq + epsilon) * scale).astype(
            out_ref.dtype
        )


def mix(local_a, local_b, query_act, scale, prefix_hi, prefix_lo):
    tokens, columns = query_act.shape
    heads = columns // HD
    whole_state = pl.BlockSpec((heads, HD, HD), lambda i: (0, 0, 0))
    return pl.pallas_call(
        mix_kernel,
        grid=(tokens // ROW_TILE,),
        in_specs=[
            row_block(local_a.shape[1]),
            row_block(local_b.shape[1]),
            row_block(columns),
            row_block(columns),
            whole_state,
            whole_state,
        ],
        out_specs=row_block(columns),
        out_shape=jax.ShapeDtypeStruct((tokens, columns), jnp.bfloat16),
        cost_estimate=pl.CostEstimate(
            flops=4 * tokens * HD * HD * heads,
            transcendentals=tokens * heads,
            bytes_accessed=12 * tokens * columns,
        ),
    )(local_a, local_b, query_act, scale, prefix_hi, prefix_lo)


def split_bf16(x):
    hi = x.astype(jnp.bfloat16)
    lo = (x - hi.astype(jnp.float32)).astype(jnp.bfloat16)
    return hi, lo


def shift(block, axis, distance):
    size = lax.axis_size(axis)
    return lax.ppermute(block, axis, [(i, i + distance) for i in range(size) if i + distance < size])


def swap(block, axis):
    return lax.ppermute(block, axis, [(0, 1), (1, 0)])


def exclusive_prefix(state, axis, fillers=()):
    inclusive = state
    exclusive = jnp.zeros_like(state)
    distance = 1
    results = []
    while distance < lax.axis_size(axis):
        sent = inclusive.astype(jnp.bfloat16)
        arrived = shift(sent, axis, distance)
        if len(results) < len(fillers):
            function, operands = fillers[len(results)]
            _, operands = lax.optimization_barrier((sent, operands))
            result = function(*operands)
            arrived, result = lax.optimization_barrier((arrived, result))
            results.append(result)
        arrived = arrived.astype(jnp.float32)
        exclusive = exclusive + arrived
        inclusive = inclusive + arrived
        distance *= 2
    for function, operands in fillers[len(results):]:
        results.append(function(*operands))
    return exclusive, results


def project_and_reduce(mixed_rows, out_weight):
    tokens, columns = mixed_rows.shape
    ty_size = lax.axis_size("ty")
    tc_size = lax.axis_size("tc")
    block = tokens // (ty_size * tc_size)
    width = out_weight.shape[1]

    def product(rows):
        return jnp.dot(rows, out_weight, preferred_element_type=jnp.float32).astype(jnp.bfloat16)

    if ty_size != 2 or tc_size != 2:
        ordered = (
            mixed_rows.reshape(ty_size, tc_size, block, columns)
            .transpose(1, 0, 2, 3)
            .reshape(tokens, columns)
        )
        part = product(ordered)
        part = lax.psum_scatter(part, "tc", scatter_dimension=0, tiled=True)
        return lax.psum_scatter(part, "ty", scatter_dimension=0, tiled=True)

    ty = lax.axis_index("ty")
    tc = lax.axis_index("tc")
    pair = tc_size * block
    far_rows = lax.dynamic_slice_in_dim(mixed_rows, (1 - ty) * pair, pair, axis=0)
    near_rows = lax.dynamic_slice_in_dim(mixed_rows, ty * pair, pair, axis=0)

    def block_of(part, owner_tc):
        return lax.dynamic_slice_in_dim(part, owner_tc * block, block, axis=0)

    chunk = width // COLUMN_CHUNKS
    chip_sums = []
    for c in range(COLUMN_CHUNKS):
        far_part = jnp.dot(
            far_rows, out_weight[:, c * chunk:(c + 1) * chunk], preferred_element_type=jnp.float32
        ).astype(jnp.bfloat16)
        from_partner = swap(block_of(far_part, 1 - tc), "tc")
        chip_sum = block_of(far_part, tc).astype(jnp.float32) + from_partner.astype(jnp.float32)
        chip_sums.append(chip_sum.astype(jnp.bfloat16))
    chip_sums, near_rows = lax.optimization_barrier((chip_sums, near_rows))
    across = [swap(chip_sum, "ty") for chip_sum in chip_sums]
    near = swap(product(block_of(near_rows, 1 - tc)), "tc")
    mine = lax.optimization_barrier(product(block_of(near_rows, tc)))
    far = jnp.concatenate(across, axis=1)
    total = mine.astype(jnp.float32) + near.astype(jnp.float32) + far.astype(jnp.float32)
    return total.astype(jnp.bfloat16)


def on_device(queries, keys, values, gates, gain, out_weight):
    own_state = key_value_states(keys, values)
    head_count = queries.shape[1] // HD
    first = (head_count + 1) // 2
    fillers = (
        (lambda q, k, v: local_attention(q, k, v, 0, first), (queries, keys, values)),
        (lambda q, k, v: local_attention(q, k, v, first, head_count - first), (queries, keys, values)),
        (query_and_gate, (queries, gates, gain)),
    )
    prefix, (local_a, local_b, (query_act, scale)) = exclusive_prefix(own_state, "ctx", fillers)
    prefix_hi, prefix_lo = split_bf16(prefix)
    mixed_rows = mix(local_a, local_b, query_act, scale, prefix_hi, prefix_lo)
    return project_and_reduce(mixed_rows, out_weight)


def solution(mesh):
    ctx_size, tp_size = mesh.devices.shape
    split = Mesh(
        np.asarray(mesh.devices).reshape(ctx_size, tp_size // 2, 2), ("ctx", "ty", "tc")
    )
    tp = ("ty", "tc")
    return jax.shard_map(
        on_device,
        mesh=split,
        in_specs=(
            P("ctx", tp),
            P("ctx", tp),
            P("ctx", tp),
            P("ctx", tp),
            P(tp),
            P(tp, None),
        ),
        out_specs=P(("ctx",) + tp, None),
        check_vma=False,
    )
```

```python
import jax
import jax.numpy as jnp
import numpy as np
from jax import lax
from jax.experimental import pallas as pl
from jax.experimental.pallas import tpu as pltpu
from jax.sharding import Mesh
from jax.sharding import PartitionSpec as P

HD = 128
COLUMN_CHUNKS = 3
QUERY_TILE = 256
ROW_TILE = 256


epsilon = 1e-05


def silu(x):
    x = x.astype(jnp.float32)
    return (x / (1.0 + jnp.exp(-x))).astype(jnp.bfloat16)


def head_block(tokens):
    return pl.BlockSpec((tokens, HD), lambda h: (0, h))


def state_kernel(k_ref, v_ref, state_ref, sent_ref):
    @pl.when(pl.program_id(0) == 0)
    def _():
        state_ref[...] = jnp.zeros_like(state_ref)

    key_act = silu(k_ref[...])
    value_rows = v_ref[...]
    for h in range(state_ref.shape[0]):
        heads = slice(h * HD, (h + 1) * HD)
        state_ref[h] += lax.dot_general(
            key_act[:, heads], value_rows[:, heads], (((0,), (0,)), ((), ())),
            preferred_element_type=jnp.float32,
        )

    @pl.when(pl.program_id(0) == pl.num_programs(0) - 1)
    def _():
        sent_ref[...] = state_ref[...].astype(sent_ref.dtype)


def row_block(columns):
    return pl.BlockSpec((ROW_TILE, columns), lambda i: (i, 0))


def key_value_states(keys, values):
    tokens, columns = keys.shape
    heads = columns // HD
    return pl.pallas_call(
        state_kernel,
        grid=(tokens // ROW_TILE,),
        in_specs=[row_block(columns), row_block(columns)],
        out_specs=[pl.BlockSpec((heads, HD, HD), lambda i: (0, 0, 0))] * 2,
        out_shape=[
            jax.ShapeDtypeStruct((heads, HD, HD), jnp.float32),
            jax.ShapeDtypeStruct((heads, HD, HD), jnp.bfloat16),
        ],
        cost_estimate=pl.CostEstimate(
            flops=2 * tokens * HD * HD * heads,
            transcendentals=tokens * columns,
            bytes_accessed=4 * tokens * columns + 4 * heads * HD * HD,
        ),
    )(keys, values)


def local_kernel(q_ref, k_ref, v_ref, out_ref):
    tokens = q_ref.shape[0]
    query_act = silu(q_ref[...])
    key_act = silu(k_ref[...])
    value_rows = v_ref[...]
    for tile in range(tokens // QUERY_TILE):
        seen = (tile + 1) * QUERY_TILE
        scores = lax.dot_general(
            query_act[tile * QUERY_TILE:seen],
            key_act[:seen],
            (((1,), (1,)), ((), ())),
            preferred_element_type=jnp.float32,
        )
        row = lax.broadcasted_iota(jnp.int32, scores.shape, 0) + tile * QUERY_TILE
        col = lax.broadcasted_iota(jnp.int32, scores.shape, 1)
        scores = jnp.where(row >= col, scores, 0.0).astype(jnp.bfloat16)
        out_ref[tile * QUERY_TILE:seen, :] = jnp.dot(
            scores, value_rows[:seen], preferred_element_type=jnp.float32
        ).astype(out_ref.dtype)


def local_attention(queries, keys, values, first_head, heads):
    tokens, columns = queries.shape
    tiles = tokens // QUERY_TILE
    pairs = QUERY_TILE * QUERY_TILE * tiles * (tiles + 1) // 2
    picked = pl.BlockSpec((tokens, HD), lambda h: (0, h + first_head))
    return pl.pallas_call(
        local_kernel,
        grid=(heads,),
        in_specs=[picked] * 3,
        out_specs=head_block(tokens),
        out_shape=jax.ShapeDtypeStruct((tokens, heads * HD), jnp.bfloat16),
        cost_estimate=pl.CostEstimate(
            flops=4 * pairs * HD * heads,
            transcendentals=2 * tokens * heads * HD,
            bytes_accessed=10 * tokens * heads * HD,
        ),
    )(queries, keys, values)


def gate_kernel(q_ref, g_ref, gain_ref, query_act_ref, scale_ref):
    query_act_ref[...] = silu(q_ref[...])
    gates = g_ref[...].astype(jnp.float32)
    scale_ref[...] = (gain_ref[...] * (1.0 / (1.0 + jnp.exp(-gates)))).astype(scale_ref.dtype)


def query_and_gate(queries, gates, gain):
    tokens, columns = queries.shape
    return pl.pallas_call(
        gate_kernel,
        grid=(tokens // ROW_TILE,),
        in_specs=[row_block(columns), row_block(columns), pl.BlockSpec((1, columns), lambda i: (0, 0))],
        out_specs=[row_block(columns), row_block(columns)],
        out_shape=[
            jax.ShapeDtypeStruct((tokens, columns), jnp.bfloat16),
            jax.ShapeDtypeStruct((tokens, columns), jnp.bfloat16),
        ],
        cost_estimate=pl.CostEstimate(
            flops=8 * tokens * columns,
            transcendentals=2 * tokens * columns,
            bytes_accessed=10 * tokens * columns,
        ),
    )(queries, gates, gain.reshape(1, columns))


def mix_kernel(local_a_ref, local_b_ref, q_ref, scale_ref, prefix_ref, out_ref):
    query_act = q_ref[...]
    first = local_a_ref.shape[1] // HD
    for h in range(prefix_ref.shape[0]):
        heads = slice(h * HD, (h + 1) * HD)
        prefix_hi, prefix_lo = split_bf16(prefix_ref[h])
        if h < first:
            local = local_a_ref[:, heads]
        else:
            local = local_b_ref[:, (h - first) * HD:(h - first + 1) * HD]
        local = local.astype(jnp.float32)
        remote = jnp.dot(query_act[:, heads], prefix_hi, preferred_element_type=jnp.float32) + jnp.dot(
            query_act[:, heads], prefix_lo, preferred_element_type=jnp.float32
        )
        attention = local + remote
        mean_sq = jnp.mean(attention * attention, axis=-1, keepdims=True)
        scale = scale_ref[:, heads].astype(jnp.float32)
        out_ref[:, heads] = (attention * lax.rsqrt(mean_sq + epsilon) * scale).astype(
            out_ref.dtype
        )


def mix(local_a, local_b, query_act, scale, prefix):
    tokens, columns = query_act.shape
    heads = columns // HD
    whole_state = pl.BlockSpec((heads, HD, HD), lambda i: (0, 0, 0))
    return pl.pallas_call(
        mix_kernel,
        grid=(tokens // ROW_TILE,),
        in_specs=[
            row_block(local_a.shape[1]),
            row_block(local_b.shape[1]),
            row_block(columns),
            row_block(columns),
            whole_state,
        ],
        out_specs=row_block(columns),
        out_shape=jax.ShapeDtypeStruct((tokens, columns), jnp.bfloat16),
        cost_estimate=pl.CostEstimate(
            flops=4 * tokens * HD * HD * heads,
            transcendentals=tokens * heads,
            bytes_accessed=12 * tokens * columns,
        ),
    )(local_a, local_b, query_act, scale, prefix)


def split_bf16(x):
    hi = x.astype(jnp.bfloat16)
    lo = (x - hi.astype(jnp.float32)).astype(jnp.bfloat16)
    return hi, lo


def shift(block, axis, distance):
    size = lax.axis_size(axis)
    return lax.ppermute(block, axis, [(i, i + distance) for i in range(size) if i + distance < size])


def swap(block, axis):
    return lax.ppermute(block, axis, [(0, 1), (1, 0)])


def exclusive_prefix(state, axis, fillers=(), sent_first=None):
    inclusive = state
    exclusive = jnp.zeros_like(state)
    distance = 1
    results = []
    while distance < lax.axis_size(axis):
        sent = inclusive.astype(jnp.bfloat16) if distance > 1 or sent_first is None else sent_first
        arrived = shift(sent, axis, distance)
        if len(results) < len(fillers):
            function, operands = fillers[len(results)]
            _, operands = lax.optimization_barrier((sent, operands))
            result = function(*operands)
            arrived, result = lax.optimization_barrier((arrived, result))
            results.append(result)
        arrived = arrived.astype(jnp.float32)
        exclusive = exclusive + arrived
        inclusive = inclusive + arrived
        distance *= 2
    for function, operands in fillers[len(results):]:
        results.append(function(*operands))
    return exclusive, results


def project_and_reduce(mixed_rows, out_weight):
    tokens, columns = mixed_rows.shape
    ty_size = lax.axis_size("ty")
    tc_size = lax.axis_size("tc")
    block = tokens // (ty_size * tc_size)
    width = out_weight.shape[1]

    def product(rows):
        return jnp.dot(rows, out_weight, preferred_element_type=jnp.float32).astype(jnp.bfloat16)

    if ty_size != 2 or tc_size != 2:
        ordered = (
            mixed_rows.reshape(ty_size, tc_size, block, columns)
            .transpose(1, 0, 2, 3)
            .reshape(tokens, columns)
        )
        part = product(ordered)
        part = lax.psum_scatter(part, "tc", scatter_dimension=0, tiled=True)
        return lax.psum_scatter(part, "ty", scatter_dimension=0, tiled=True)

    ty = lax.axis_index("ty")
    tc = lax.axis_index("tc")
    pair = tc_size * block
    far_rows = lax.dynamic_slice_in_dim(mixed_rows, (1 - ty) * pair, pair, axis=0)
    near_rows = lax.dynamic_slice_in_dim(mixed_rows, ty * pair, pair, axis=0)

    def block_of(part, owner_tc):
        return lax.dynamic_slice_in_dim(part, owner_tc * block, block, axis=0)

    chunk = width // COLUMN_CHUNKS
    chip_sums = []
    for c in range(COLUMN_CHUNKS):
        far_part = jnp.dot(
            far_rows, out_weight[:, c * chunk:(c + 1) * chunk], preferred_element_type=jnp.float32
        ).astype(jnp.bfloat16)
        from_partner = swap(block_of(far_part, 1 - tc), "tc")
        chip_sum = block_of(far_part, tc).astype(jnp.float32) + from_partner.astype(jnp.float32)
        chip_sums.append(chip_sum.astype(jnp.bfloat16))
    chip_sums, near_rows = lax.optimization_barrier((chip_sums, near_rows))
    across = [swap(chip_sum, "ty") for chip_sum in chip_sums]
    near = swap(product(block_of(near_rows, 1 - tc)), "tc")
    mine = lax.optimization_barrier(product(block_of(near_rows, tc)))
    far = jnp.concatenate(across, axis=1)
    total = mine.astype(jnp.float32) + near.astype(jnp.float32) + far.astype(jnp.float32)
    return total.astype(jnp.bfloat16)


def on_device(queries, keys, values, gates, gain, out_weight):
    own_state, own_sent = key_value_states(keys, values)
    head_count = queries.shape[1] // HD
    first = (head_count + 1) // 2
    fillers = (
        (lambda q, k, v: local_attention(q, k, v, 0, first), (queries, keys, values)),
        (lambda q, k, v: local_attention(q, k, v, first, head_count - first), (queries, keys, values)),
        (query_and_gate, (queries, gates, gain)),
    )
    prefix, (local_a, local_b, (query_act, scale)) = exclusive_prefix(own_state, "ctx", fillers, own_sent)
    mixed_rows = mix(local_a, local_b, query_act, scale, prefix)
    return project_and_reduce(mixed_rows, out_weight)


def solution(mesh):
    ctx_size, tp_size = mesh.devices.shape
    split = Mesh(
        np.asarray(mesh.devices).reshape(ctx_size, tp_size // 2, 2), ("ctx", "ty", "tc")
    )
    tp = ("ty", "tc")
    return jax.shard_map(
        on_device,
        mesh=split,
        in_specs=(
            P("ctx", tp),
            P("ctx", tp),
            P("ctx", tp),
            P("ctx", tp),
            P(tp),
            P(tp, None),
        ),
        out_specs=P(("ctx",) + tp, None),
        check_vma=False,
    )
```

```python
import jax
import jax.numpy as jnp
import numpy as np
from jax import lax
from jax.experimental import pallas as pl
from jax.experimental.pallas import tpu as pltpu
from jax.sharding import Mesh
from jax.sharding import PartitionSpec as P

HD = 128
COLUMN_CHUNKS = 2
QUERY_TILE = 256
ROW_TILE = 256


epsilon = 1e-05


def silu(x):
    x = x.astype(jnp.float32)
    return (x / (1.0 + jnp.exp(-x))).astype(jnp.bfloat16)


def head_block(tokens):
    return pl.BlockSpec((tokens, HD), lambda h: (0, h))


def state_kernel(k_ref, v_ref, state_ref, sent_ref):
    @pl.when(pl.program_id(0) == 0)
    def _():
        state_ref[...] = jnp.zeros_like(state_ref)

    key_act = silu(k_ref[...])
    value_rows = v_ref[...]
    for h in range(state_ref.shape[0]):
        heads = slice(h * HD, (h + 1) * HD)
        state_ref[h] += lax.dot_general(
            key_act[:, heads], value_rows[:, heads], (((0,), (0,)), ((), ())),
            preferred_element_type=jnp.float32,
        )

    @pl.when(pl.program_id(0) == pl.num_programs(0) - 1)
    def _():
        sent_ref[...] = state_ref[...].astype(sent_ref.dtype)


def row_block(columns):
    return pl.BlockSpec((ROW_TILE, columns), lambda i: (i, 0))


def key_value_states(keys, values):
    tokens, columns = keys.shape
    heads = columns // HD
    return pl.pallas_call(
        state_kernel,
        grid=(tokens // ROW_TILE,),
        in_specs=[row_block(columns), row_block(columns)],
        out_specs=[pl.BlockSpec((heads, HD, HD), lambda i: (0, 0, 0))] * 2,
        out_shape=[
            jax.ShapeDtypeStruct((heads, HD, HD), jnp.float32),
            jax.ShapeDtypeStruct((heads, HD, HD), jnp.bfloat16),
        ],
        cost_estimate=pl.CostEstimate(
            flops=2 * tokens * HD * HD * heads,
            transcendentals=tokens * columns,
            bytes_accessed=4 * tokens * columns + 4 * heads * HD * HD,
        ),
    )(keys, values)


def local_kernel(q_ref, k_ref, v_ref, out_ref):
    tokens = q_ref.shape[0]
    query_act = silu(q_ref[...])
    key_act = silu(k_ref[...])
    value_rows = v_ref[...]
    for tile in range(tokens // QUERY_TILE):
        seen = (tile + 1) * QUERY_TILE
        scores = lax.dot_general(
            query_act[tile * QUERY_TILE:seen],
            key_act[:seen],
            (((1,), (1,)), ((), ())),
            preferred_element_type=jnp.float32,
        )
        row = lax.broadcasted_iota(jnp.int32, scores.shape, 0) + tile * QUERY_TILE
        col = lax.broadcasted_iota(jnp.int32, scores.shape, 1)
        scores = jnp.where(row >= col, scores, 0.0).astype(jnp.bfloat16)
        out_ref[tile * QUERY_TILE:seen, :] = jnp.dot(
            scores, value_rows[:seen], preferred_element_type=jnp.float32
        ).astype(out_ref.dtype)


def local_attention(queries, keys, values, first_head, heads):
    tokens, columns = queries.shape
    tiles = tokens // QUERY_TILE
    pairs = QUERY_TILE * QUERY_TILE * tiles * (tiles + 1) // 2
    picked = pl.BlockSpec((tokens, HD), lambda h: (0, h + first_head))
    return pl.pallas_call(
        local_kernel,
        grid=(heads,),
        in_specs=[picked] * 3,
        out_specs=head_block(tokens),
        out_shape=jax.ShapeDtypeStruct((tokens, heads * HD), jnp.bfloat16),
        cost_estimate=pl.CostEstimate(
            flops=4 * pairs * HD * heads,
            transcendentals=2 * tokens * heads * HD,
            bytes_accessed=10 * tokens * heads * HD,
        ),
    )(queries, keys, values)


def gate_kernel(q_ref, g_ref, gain_ref, query_act_ref, scale_ref):
    query_act_ref[...] = silu(q_ref[...])
    gates = g_ref[...].astype(jnp.float32)
    scale_ref[...] = (gain_ref[...] * (1.0 / (1.0 + jnp.exp(-gates)))).astype(scale_ref.dtype)


def query_and_gate(queries, gates, gain):
    tokens, columns = queries.shape
    return pl.pallas_call(
        gate_kernel,
        grid=(tokens // ROW_TILE,),
        in_specs=[row_block(columns), row_block(columns), pl.BlockSpec((1, columns), lambda i: (0, 0))],
        out_specs=[row_block(columns), row_block(columns)],
        out_shape=[
            jax.ShapeDtypeStruct((tokens, columns), jnp.bfloat16),
            jax.ShapeDtypeStruct((tokens, columns), jnp.bfloat16),
        ],
        cost_estimate=pl.CostEstimate(
            flops=8 * tokens * columns,
            transcendentals=2 * tokens * columns,
            bytes_accessed=10 * tokens * columns,
        ),
    )(queries, gates, gain.reshape(1, columns))


def mix_kernel(local_a_ref, local_b_ref, q_ref, scale_ref, prefix_ref, out_ref):
    query_act = q_ref[...]
    first = local_a_ref.shape[1] // HD
    for h in range(prefix_ref.shape[0]):
        heads = slice(h * HD, (h + 1) * HD)
        prefix_hi, prefix_lo = split_bf16(prefix_ref[h])
        if h < first:
            local = local_a_ref[:, heads]
        else:
            local = local_b_ref[:, (h - first) * HD:(h - first + 1) * HD]
        local = local.astype(jnp.float32)
        remote = jnp.dot(query_act[:, heads], prefix_hi, preferred_element_type=jnp.float32) + jnp.dot(
            query_act[:, heads], prefix_lo, preferred_element_type=jnp.float32
        )
        attention = local + remote
        mean_sq = jnp.mean(attention * attention, axis=-1, keepdims=True)
        scale = scale_ref[:, heads].astype(jnp.float32)
        out_ref[:, heads] = (attention * lax.rsqrt(mean_sq + epsilon) * scale).astype(
            out_ref.dtype
        )


def mix(local_a, local_b, query_act, scale, prefix):
    tokens, columns = query_act.shape
    heads = columns // HD
    whole_state = pl.BlockSpec((heads, HD, HD), lambda i: (0, 0, 0))
    return pl.pallas_call(
        mix_kernel,
        grid=(tokens // ROW_TILE,),
        in_specs=[
            row_block(local_a.shape[1]),
            row_block(local_b.shape[1]),
            row_block(columns),
            row_block(columns),
            whole_state,
        ],
        out_specs=row_block(columns),
        out_shape=jax.ShapeDtypeStruct((tokens, columns), jnp.bfloat16),
        cost_estimate=pl.CostEstimate(
            flops=4 * tokens * HD * HD * heads,
            transcendentals=tokens * heads,
            bytes_accessed=12 * tokens * columns,
        ),
    )(local_a, local_b, query_act, scale, prefix)


def split_bf16(x):
    hi = x.astype(jnp.bfloat16)
    lo = (x - hi.astype(jnp.float32)).astype(jnp.bfloat16)
    return hi, lo


def shift(block, axis, distance):
    size = lax.axis_size(axis)
    return lax.ppermute(block, axis, [(i, i + distance) for i in range(size) if i + distance < size])


def swap(block, axis):
    return lax.ppermute(block, axis, [(0, 1), (1, 0)])


def exclusive_prefix(state, axis, fillers=(), sent_first=None):
    inclusive = state
    exclusive = jnp.zeros_like(state)
    distance = 1
    results = []
    while distance < lax.axis_size(axis):
        sent = inclusive.astype(jnp.bfloat16) if distance > 1 or sent_first is None else sent_first
        arrived = shift(sent, axis, distance)
        if len(results) < len(fillers):
            function, operands = fillers[len(results)]
            _, operands = lax.optimization_barrier((sent, operands))
            result = function(*operands)
            arrived, result = lax.optimization_barrier((arrived, result))
            results.append(result)
        arrived = arrived.astype(jnp.float32)
        exclusive = exclusive + arrived
        inclusive = inclusive + arrived
        distance *= 2
    for function, operands in fillers[len(results):]:
        results.append(function(*operands))
    return exclusive, results


def project_and_reduce(mixed_rows, out_weight):
    tokens, columns = mixed_rows.shape
    ty_size = lax.axis_size("ty")
    tc_size = lax.axis_size("tc")
    block = tokens // (ty_size * tc_size)
    width = out_weight.shape[1]

    def product(rows):
        return jnp.dot(rows, out_weight, preferred_element_type=jnp.float32).astype(jnp.bfloat16)

    if ty_size != 2 or tc_size != 2:
        ordered = (
            mixed_rows.reshape(ty_size, tc_size, block, columns)
            .transpose(1, 0, 2, 3)
            .reshape(tokens, columns)
        )
        part = product(ordered)
        part = lax.psum_scatter(part, "tc", scatter_dimension=0, tiled=True)
        return lax.psum_scatter(part, "ty", scatter_dimension=0, tiled=True)

    ty = lax.axis_index("ty")
    tc = lax.axis_index("tc")
    pair = tc_size * block
    far_rows = lax.dynamic_slice_in_dim(mixed_rows, (1 - ty) * pair, pair, axis=0)
    near_rows = lax.dynamic_slice_in_dim(mixed_rows, ty * pair, pair, axis=0)

    def block_of(part, owner_tc):
        return lax.dynamic_slice_in_dim(part, owner_tc * block, block, axis=0)

    chunk = width // COLUMN_CHUNKS
    chip_sums = []
    for c in range(COLUMN_CHUNKS):
        far_part = jnp.dot(
            far_rows, out_weight[:, c * chunk:(c + 1) * chunk], preferred_element_type=jnp.float32
        ).astype(jnp.bfloat16)
        from_partner = swap(block_of(far_part, 1 - tc), "tc")
        chip_sum = block_of(far_part, tc).astype(jnp.float32) + from_partner.astype(jnp.float32)
        chip_sums.append(chip_sum.astype(jnp.bfloat16))
    chip_sums, near_rows = lax.optimization_barrier((chip_sums, near_rows))
    across = [swap(chip_sum, "ty") for chip_sum in chip_sums]
    near = swap(product(block_of(near_rows, 1 - tc)), "tc")
    mine = lax.optimization_barrier(product(block_of(near_rows, tc)))
    far = jnp.concatenate(across, axis=1)
    total = mine.astype(jnp.float32) + near.astype(jnp.float32) + far.astype(jnp.float32)
    return total.astype(jnp.bfloat16)


def on_device(queries, keys, values, gates, gain, out_weight):
    own_state, own_sent = key_value_states(keys, values)
    head_count = queries.shape[1] // HD
    first = (head_count + 1) // 2
    fillers = (
        (lambda q, k, v: local_attention(q, k, v, 0, first), (queries, keys, values)),
        (lambda q, k, v: local_attention(q, k, v, first, head_count - first), (queries, keys, values)),
        (query_and_gate, (queries, gates, gain)),
    )
    prefix, (local_a, local_b, (query_act, scale)) = exclusive_prefix(own_state, "ctx", fillers, own_sent)
    mixed_rows = mix(local_a, local_b, query_act, scale, prefix)
    return project_and_reduce(mixed_rows, out_weight)


def solution(mesh):
    ctx_size, tp_size = mesh.devices.shape
    split = Mesh(
        np.asarray(mesh.devices).reshape(ctx_size, tp_size // 2, 2), ("ctx", "ty", "tc")
    )
    tp = ("ty", "tc")
    return jax.shard_map(
        on_device,
        mesh=split,
        in_specs=(
            P("ctx", tp),
            P("ctx", tp),
            P("ctx", tp),
            P("ctx", tp),
            P(tp),
            P(tp, None),
        ),
        out_specs=P(("ctx",) + tp, None),
        check_vma=False,
    )
```

```python
import jax
import jax.numpy as jnp
import numpy as np
from jax import lax
from jax.experimental import pallas as pl
from jax.experimental.pallas import tpu as pltpu
from jax.sharding import Mesh
from jax.sharding import PartitionSpec as P

HD = 128
COLUMN_CHUNKS = 4
QUERY_TILE = 256
ROW_TILE = 256


epsilon = 1e-05


def silu(x):
    x = x.astype(jnp.float32)
    return (x / (1.0 + jnp.exp(-x))).astype(jnp.bfloat16)


def head_block(tokens):
    return pl.BlockSpec((tokens, HD), lambda h: (0, h))


def state_kernel(k_ref, v_ref, state_ref, sent_ref):
    @pl.when(pl.program_id(0) == 0)
    def _():
        state_ref[...] = jnp.zeros_like(state_ref)

    key_act = silu(k_ref[...])
    value_rows = v_ref[...]
    for h in range(state_ref.shape[0]):
        heads = slice(h * HD, (h + 1) * HD)
        state_ref[h] += lax.dot_general(
            key_act[:, heads], value_rows[:, heads], (((0,), (0,)), ((), ())),
            preferred_element_type=jnp.float32,
        )

    @pl.when(pl.program_id(0) == pl.num_programs(0) - 1)
    def _():
        sent_ref[...] = state_ref[...].astype(sent_ref.dtype)


def row_block(columns):
    return pl.BlockSpec((ROW_TILE, columns), lambda i: (i, 0))


def key_value_states(keys, values):
    tokens, columns = keys.shape
    heads = columns // HD
    return pl.pallas_call(
        state_kernel,
        grid=(tokens // ROW_TILE,),
        in_specs=[row_block(columns), row_block(columns)],
        out_specs=[pl.BlockSpec((heads, HD, HD), lambda i: (0, 0, 0))] * 2,
        out_shape=[
            jax.ShapeDtypeStruct((heads, HD, HD), jnp.float32),
            jax.ShapeDtypeStruct((heads, HD, HD), jnp.bfloat16),
        ],
        cost_estimate=pl.CostEstimate(
            flops=2 * tokens * HD * HD * heads,
            transcendentals=tokens * columns,
            bytes_accessed=4 * tokens * columns + 4 * heads * HD * HD,
        ),
    )(keys, values)


def local_kernel(q_ref, k_ref, v_ref, out_ref):
    tokens = q_ref.shape[0]
    query_act = silu(q_ref[...])
    key_act = silu(k_ref[...])
    value_rows = v_ref[...]
    for tile in range(tokens // QUERY_TILE):
        seen = (tile + 1) * QUERY_TILE
        scores = lax.dot_general(
            query_act[tile * QUERY_TILE:seen],
            key_act[:seen],
            (((1,), (1,)), ((), ())),
            preferred_element_type=jnp.float32,
        )
        row = lax.broadcasted_iota(jnp.int32, scores.shape, 0) + tile * QUERY_TILE
        col = lax.broadcasted_iota(jnp.int32, scores.shape, 1)
        scores = jnp.where(row >= col, scores, 0.0).astype(jnp.bfloat16)
        out_ref[tile * QUERY_TILE:seen, :] = jnp.dot(
            scores, value_rows[:seen], preferred_element_type=jnp.float32
        ).astype(out_ref.dtype)


def local_attention(queries, keys, values, first_head, heads):
    tokens, columns = queries.shape
    tiles = tokens // QUERY_TILE
    pairs = QUERY_TILE * QUERY_TILE * tiles * (tiles + 1) // 2
    picked = pl.BlockSpec((tokens, HD), lambda h: (0, h + first_head))
    return pl.pallas_call(
        local_kernel,
        grid=(heads,),
        in_specs=[picked] * 3,
        out_specs=head_block(tokens),
        out_shape=jax.ShapeDtypeStruct((tokens, heads * HD), jnp.bfloat16),
        cost_estimate=pl.CostEstimate(
            flops=4 * pairs * HD * heads,
            transcendentals=2 * tokens * heads * HD,
            bytes_accessed=10 * tokens * heads * HD,
        ),
    )(queries, keys, values)


def gate_kernel(q_ref, g_ref, gain_ref, query_act_ref, scale_ref):
    query_act_ref[...] = silu(q_ref[...])
    gates = g_ref[...].astype(jnp.float32)
    scale_ref[...] = (gain_ref[...] * (1.0 / (1.0 + jnp.exp(-gates)))).astype(scale_ref.dtype)


def query_and_gate(queries, gates, gain):
    tokens, columns = queries.shape
    return pl.pallas_call(
        gate_kernel,
        grid=(tokens // ROW_TILE,),
        in_specs=[row_block(columns), row_block(columns), pl.BlockSpec((1, columns), lambda i: (0, 0))],
        out_specs=[row_block(columns), row_block(columns)],
        out_shape=[
            jax.ShapeDtypeStruct((tokens, columns), jnp.bfloat16),
            jax.ShapeDtypeStruct((tokens, columns), jnp.bfloat16),
        ],
        cost_estimate=pl.CostEstimate(
            flops=8 * tokens * columns,
            transcendentals=2 * tokens * columns,
            bytes_accessed=10 * tokens * columns,
        ),
    )(queries, gates, gain.reshape(1, columns))


def mix_kernel(local_a_ref, local_b_ref, q_ref, scale_ref, prefix_ref, out_ref):
    query_act = q_ref[...]
    first = local_a_ref.shape[1] // HD
    for h in range(prefix_ref.shape[0]):
        heads = slice(h * HD, (h + 1) * HD)
        prefix_hi, prefix_lo = split_bf16(prefix_ref[h])
        if h < first:
            local = local_a_ref[:, heads]
        else:
            local = local_b_ref[:, (h - first) * HD:(h - first + 1) * HD]
        local = local.astype(jnp.float32)
        remote = jnp.dot(query_act[:, heads], prefix_hi, preferred_element_type=jnp.float32) + jnp.dot(
            query_act[:, heads], prefix_lo, preferred_element_type=jnp.float32
        )
        attention = local + remote
        mean_sq = jnp.mean(attention * attention, axis=-1, keepdims=True)
        scale = scale_ref[:, heads].astype(jnp.float32)
        out_ref[:, heads] = (attention * lax.rsqrt(mean_sq + epsilon) * scale).astype(
            out_ref.dtype
        )


def mix(local_a, local_b, query_act, scale, prefix):
    tokens, columns = query_act.shape
    heads = columns // HD
    whole_state = pl.BlockSpec((heads, HD, HD), lambda i: (0, 0, 0))
    return pl.pallas_call(
        mix_kernel,
        grid=(tokens // ROW_TILE,),
        in_specs=[
            row_block(local_a.shape[1]),
            row_block(local_b.shape[1]),
            row_block(columns),
            row_block(columns),
            whole_state,
        ],
        out_specs=row_block(columns),
        out_shape=jax.ShapeDtypeStruct((tokens, columns), jnp.bfloat16),
        cost_estimate=pl.CostEstimate(
            flops=4 * tokens * HD * HD * heads,
            transcendentals=tokens * heads,
            bytes_accessed=12 * tokens * columns,
        ),
    )(local_a, local_b, query_act, scale, prefix)


def split_bf16(x):
    hi = x.astype(jnp.bfloat16)
    lo = (x - hi.astype(jnp.float32)).astype(jnp.bfloat16)
    return hi, lo


def shift(block, axis, distance):
    size = lax.axis_size(axis)
    return lax.ppermute(block, axis, [(i, i + distance) for i in range(size) if i + distance < size])


def swap(block, axis):
    return lax.ppermute(block, axis, [(0, 1), (1, 0)])


def exclusive_prefix(state, axis, fillers=(), sent_first=None):
    inclusive = state
    exclusive = jnp.zeros_like(state)
    distance = 1
    results = []
    while distance < lax.axis_size(axis):
        sent = inclusive.astype(jnp.bfloat16) if distance > 1 or sent_first is None else sent_first
        arrived = shift(sent, axis, distance)
        if len(results) < len(fillers):
            function, operands = fillers[len(results)]
            _, operands = lax.optimization_barrier((sent, operands))
            result = function(*operands)
            arrived, result = lax.optimization_barrier((arrived, result))
            results.append(result)
        arrived = arrived.astype(jnp.float32)
        exclusive = exclusive + arrived
        inclusive = inclusive + arrived
        distance *= 2
    for function, operands in fillers[len(results):]:
        results.append(function(*operands))
    return exclusive, results


def project_and_reduce(mixed_rows, out_weight):
    tokens, columns = mixed_rows.shape
    ty_size = lax.axis_size("ty")
    tc_size = lax.axis_size("tc")
    block = tokens // (ty_size * tc_size)
    width = out_weight.shape[1]

    def product(rows):
        return jnp.dot(rows, out_weight, preferred_element_type=jnp.float32).astype(jnp.bfloat16)

    if ty_size != 2 or tc_size != 2:
        ordered = (
            mixed_rows.reshape(ty_size, tc_size, block, columns)
            .transpose(1, 0, 2, 3)
            .reshape(tokens, columns)
        )
        part = product(ordered)
        part = lax.psum_scatter(part, "tc", scatter_dimension=0, tiled=True)
        return lax.psum_scatter(part, "ty", scatter_dimension=0, tiled=True)

    ty = lax.axis_index("ty")
    tc = lax.axis_index("tc")
    pair = tc_size * block
    far_rows = lax.dynamic_slice_in_dim(mixed_rows, (1 - ty) * pair, pair, axis=0)
    near_rows = lax.dynamic_slice_in_dim(mixed_rows, ty * pair, pair, axis=0)

    def block_of(part, owner_tc):
        return lax.dynamic_slice_in_dim(part, owner_tc * block, block, axis=0)

    chunk = width // COLUMN_CHUNKS
    chip_sums = []
    for c in range(COLUMN_CHUNKS):
        far_part = jnp.dot(
            far_rows, out_weight[:, c * chunk:(c + 1) * chunk], preferred_element_type=jnp.float32
        ).astype(jnp.bfloat16)
        from_partner = swap(block_of(far_part, 1 - tc), "tc")
        chip_sum = block_of(far_part, tc).astype(jnp.float32) + from_partner.astype(jnp.float32)
        chip_sums.append(chip_sum.astype(jnp.bfloat16))
    chip_sums, near_rows = lax.optimization_barrier((chip_sums, near_rows))
    across = [swap(chip_sum, "ty") for chip_sum in chip_sums]
    near = swap(product(block_of(near_rows, 1 - tc)), "tc")
    mine = lax.optimization_barrier(product(block_of(near_rows, tc)))
    far = jnp.concatenate(across, axis=1)
    total = mine.astype(jnp.float32) + near.astype(jnp.float32) + far.astype(jnp.float32)
    return total.astype(jnp.bfloat16)


def on_device(queries, keys, values, gates, gain, out_weight):
    own_state, own_sent = key_value_states(keys, values)
    head_count = queries.shape[1] // HD
    first = (head_count + 1) // 2
    fillers = (
        (lambda q, k, v: local_attention(q, k, v, 0, first), (queries, keys, values)),
        (lambda q, k, v: local_attention(q, k, v, first, head_count - first), (queries, keys, values)),
        (query_and_gate, (queries, gates, gain)),
    )
    prefix, (local_a, local_b, (query_act, scale)) = exclusive_prefix(own_state, "ctx", fillers, own_sent)
    mixed_rows = mix(local_a, local_b, query_act, scale, prefix)
    return project_and_reduce(mixed_rows, out_weight)


def solution(mesh):
    ctx_size, tp_size = mesh.devices.shape
    split = Mesh(
        np.asarray(mesh.devices).reshape(ctx_size, tp_size // 2, 2), ("ctx", "ty", "tc")
    )
    tp = ("ty", "tc")
    return jax.shard_map(
        on_device,
        mesh=split,
        in_specs=(
            P("ctx", tp),
            P("ctx", tp),
            P("ctx", tp),
            P("ctx", tp),
            P(tp),
            P(tp, None),
        ),
        out_specs=P(("ctx",) + tp, None),
        check_vma=False,
    )
```

```python
import jax
import jax.numpy as jnp
import numpy as np
from jax import lax
from jax.experimental import pallas as pl
from jax.experimental.pallas import tpu as pltpu
from jax.sharding import Mesh
from jax.sharding import PartitionSpec as P

HD = 128
COLUMN_CHUNKS = 3
QUERY_TILE = 128
ROW_TILE = 256


epsilon = 1e-05


def silu(x):
    x = x.astype(jnp.float32)
    return (x / (1.0 + jnp.exp(-x))).astype(jnp.bfloat16)


def head_block(tokens):
    return pl.BlockSpec((tokens, HD), lambda h: (0, h))


def state_kernel(k_ref, v_ref, state_ref, sent_ref):
    @pl.when(pl.program_id(0) == 0)
    def _():
        state_ref[...] = jnp.zeros_like(state_ref)

    key_act = silu(k_ref[...])
    value_rows = v_ref[...]
    for h in range(state_ref.shape[0]):
        heads = slice(h * HD, (h + 1) * HD)
        state_ref[h] += lax.dot_general(
            key_act[:, heads], value_rows[:, heads], (((0,), (0,)), ((), ())),
            preferred_element_type=jnp.float32,
        )

    @pl.when(pl.program_id(0) == pl.num_programs(0) - 1)
    def _():
        sent_ref[...] = state_ref[...].astype(sent_ref.dtype)


def row_block(columns):
    return pl.BlockSpec((ROW_TILE, columns), lambda i: (i, 0))


def key_value_states(keys, values):
    tokens, columns = keys.shape
    heads = columns // HD
    return pl.pallas_call(
        state_kernel,
        grid=(tokens // ROW_TILE,),
        in_specs=[row_block(columns), row_block(columns)],
        out_specs=[pl.BlockSpec((heads, HD, HD), lambda i: (0, 0, 0))] * 2,
        out_shape=[
            jax.ShapeDtypeStruct((heads, HD, HD), jnp.float32),
            jax.ShapeDtypeStruct((heads, HD, HD), jnp.bfloat16),
        ],
        cost_estimate=pl.CostEstimate(
            flops=2 * tokens * HD * HD * heads,
            transcendentals=tokens * columns,
            bytes_accessed=4 * tokens * columns + 4 * heads * HD * HD,
        ),
    )(keys, values)


def local_kernel(q_ref, k_ref, v_ref, out_ref):
    tokens = q_ref.shape[0]
    query_act = silu(q_ref[...])
    key_act = silu(k_ref[...])
    value_rows = v_ref[...]
    for tile in range(tokens // QUERY_TILE):
        seen = (tile + 1) * QUERY_TILE
        scores = lax.dot_general(
            query_act[tile * QUERY_TILE:seen],
            key_act[:seen],
            (((1,), (1,)), ((), ())),
            preferred_element_type=jnp.float32,
        )
        row = lax.broadcasted_iota(jnp.int32, scores.shape, 0) + tile * QUERY_TILE
        col = lax.broadcasted_iota(jnp.int32, scores.shape, 1)
        scores = jnp.where(row >= col, scores, 0.0).astype(jnp.bfloat16)
        out_ref[tile * QUERY_TILE:seen, :] = jnp.dot(
            scores, value_rows[:seen], preferred_element_type=jnp.float32
        ).astype(out_ref.dtype)


def local_attention(queries, keys, values, first_head, heads):
    tokens, columns = queries.shape
    tiles = tokens // QUERY_TILE
    pairs = QUERY_TILE * QUERY_TILE * tiles * (tiles + 1) // 2
    picked = pl.BlockSpec((tokens, HD), lambda h: (0, h + first_head))
    return pl.pallas_call(
        local_kernel,
        grid=(heads,),
        in_specs=[picked] * 3,
        out_specs=head_block(tokens),
        out_shape=jax.ShapeDtypeStruct((tokens, heads * HD), jnp.bfloat16),
        cost_estimate=pl.CostEstimate(
            flops=4 * pairs * HD * heads,
            transcendentals=2 * tokens * heads * HD,
            bytes_accessed=10 * tokens * heads * HD,
        ),
    )(queries, keys, values)


def gate_kernel(q_ref, g_ref, gain_ref, query_act_ref, scale_ref):
    query_act_ref[...] = silu(q_ref[...])
    gates = g_ref[...].astype(jnp.float32)
    scale_ref[...] = (gain_ref[...] * (1.0 / (1.0 + jnp.exp(-gates)))).astype(scale_ref.dtype)


def query_and_gate(queries, gates, gain):
    tokens, columns = queries.shape
    return pl.pallas_call(
        gate_kernel,
        grid=(tokens // ROW_TILE,),
        in_specs=[row_block(columns), row_block(columns), pl.BlockSpec((1, columns), lambda i: (0, 0))],
        out_specs=[row_block(columns), row_block(columns)],
        out_shape=[
            jax.ShapeDtypeStruct((tokens, columns), jnp.bfloat16),
            jax.ShapeDtypeStruct((tokens, columns), jnp.bfloat16),
        ],
        cost_estimate=pl.CostEstimate(
            flops=8 * tokens * columns,
            transcendentals=2 * tokens * columns,
            bytes_accessed=10 * tokens * columns,
        ),
    )(queries, gates, gain.reshape(1, columns))


def mix_kernel(local_a_ref, local_b_ref, q_ref, scale_ref, prefix_ref, out_ref):
    query_act = q_ref[...]
    first = local_a_ref.shape[1] // HD
    for h in range(prefix_ref.shape[0]):
        heads = slice(h * HD, (h + 1) * HD)
        prefix_hi, prefix_lo = split_bf16(prefix_ref[h])
        if h < first:
            local = local_a_ref[:, heads]
        else:
            local = local_b_ref[:, (h - first) * HD:(h - first + 1) * HD]
        local = local.astype(jnp.float32)
        remote = jnp.dot(query_act[:, heads], prefix_hi, preferred_element_type=jnp.float32) + jnp.dot(
            query_act[:, heads], prefix_lo, preferred_element_type=jnp.float32
        )
        attention = local + remote
        mean_sq = jnp.mean(attention * attention, axis=-1, keepdims=True)
        scale = scale_ref[:, heads].astype(jnp.float32)
        out_ref[:, heads] = (attention * lax.rsqrt(mean_sq + epsilon) * scale).astype(
            out_ref.dtype
        )


def mix(local_a, local_b, query_act, scale, prefix):
    tokens, columns = query_act.shape
    heads = columns // HD
    whole_state = pl.BlockSpec((heads, HD, HD), lambda i: (0, 0, 0))
    return pl.pallas_call(
        mix_kernel,
        grid=(tokens // ROW_TILE,),
        in_specs=[
            row_block(local_a.shape[1]),
            row_block(local_b.shape[1]),
            row_block(columns),
            row_block(columns),
            whole_state,
        ],
        out_specs=row_block(columns),
        out_shape=jax.ShapeDtypeStruct((tokens, columns), jnp.bfloat16),
        cost_estimate=pl.CostEstimate(
            flops=4 * tokens * HD * HD * heads,
            transcendentals=tokens * heads,
            bytes_accessed=12 * tokens * columns,
        ),
    )(local_a, local_b, query_act, scale, prefix)


def split_bf16(x):
    hi = x.astype(jnp.bfloat16)
    lo = (x - hi.astype(jnp.float32)).astype(jnp.bfloat16)
    return hi, lo


def shift(block, axis, distance):
    size = lax.axis_size(axis)
    return lax.ppermute(block, axis, [(i, i + distance) for i in range(size) if i + distance < size])


def swap(block, axis):
    return lax.ppermute(block, axis, [(0, 1), (1, 0)])


def exclusive_prefix(state, axis, fillers=(), sent_first=None):
    inclusive = state
    exclusive = jnp.zeros_like(state)
    distance = 1
    results = []
    while distance < lax.axis_size(axis):
        sent = inclusive.astype(jnp.bfloat16) if distance > 1 or sent_first is None else sent_first
        arrived = shift(sent, axis, distance)
        if len(results) < len(fillers):
            function, operands = fillers[len(results)]
            _, operands = lax.optimization_barrier((sent, operands))
            result = function(*operands)
            arrived, result = lax.optimization_barrier((arrived, result))
            results.append(result)
        arrived = arrived.astype(jnp.float32)
        exclusive = exclusive + arrived
        inclusive = inclusive + arrived
        distance *= 2
    for function, operands in fillers[len(results):]:
        results.append(function(*operands))
    return exclusive, results


def project_and_reduce(mixed_rows, out_weight):
    tokens, columns = mixed_rows.shape
    ty_size = lax.axis_size("ty")
    tc_size = lax.axis_size("tc")
    block = tokens // (ty_size * tc_size)
    width = out_weight.shape[1]

    def product(rows):
        return jnp.dot(rows, out_weight, preferred_element_type=jnp.float32).astype(jnp.bfloat16)

    if ty_size != 2 or tc_size != 2:
        ordered = (
            mixed_rows.reshape(ty_size, tc_size, block, columns)
            .transpose(1, 0, 2, 3)
            .reshape(tokens, columns)
        )
        part = product(ordered)
        part = lax.psum_scatter(part, "tc", scatter_dimension=0, tiled=True)
        return lax.psum_scatter(part, "ty", scatter_dimension=0, tiled=True)

    ty = lax.axis_index("ty")
    tc = lax.axis_index("tc")
    pair = tc_size * block
    far_rows = lax.dynamic_slice_in_dim(mixed_rows, (1 - ty) * pair, pair, axis=0)
    near_rows = lax.dynamic_slice_in_dim(mixed_rows, ty * pair, pair, axis=0)

    def block_of(part, owner_tc):
        return lax.dynamic_slice_in_dim(part, owner_tc * block, block, axis=0)

    chunk = width // COLUMN_CHUNKS
    chip_sums = []
    for c in range(COLUMN_CHUNKS):
        far_part = jnp.dot(
            far_rows, out_weight[:, c * chunk:(c + 1) * chunk], preferred_element_type=jnp.float32
        ).astype(jnp.bfloat16)
        from_partner = swap(block_of(far_part, 1 - tc), "tc")
        chip_sum = block_of(far_part, tc).astype(jnp.float32) + from_partner.astype(jnp.float32)
        chip_sums.append(chip_sum.astype(jnp.bfloat16))
    chip_sums, near_rows = lax.optimization_barrier((chip_sums, near_rows))
    across = [swap(chip_sum, "ty") for chip_sum in chip_sums]
    near = swap(product(block_of(near_rows, 1 - tc)), "tc")
    mine = lax.optimization_barrier(product(block_of(near_rows, tc)))
    far = jnp.concatenate(across, axis=1)
    total = mine.astype(jnp.float32) + near.astype(jnp.float32) + far.astype(jnp.float32)
    return total.astype(jnp.bfloat16)


def on_device(queries, keys, values, gates, gain, out_weight):
    own_state, own_sent = key_value_states(keys, values)
    head_count = queries.shape[1] // HD
    first = (head_count + 1) // 2
    fillers = (
        (lambda q, k, v: local_attention(q, k, v, 0, first), (queries, keys, values)),
        (lambda q, k, v: local_attention(q, k, v, first, head_count - first), (queries, keys, values)),
        (query_and_gate, (queries, gates, gain)),
    )
    prefix, (local_a, local_b, (query_act, scale)) = exclusive_prefix(own_state, "ctx", fillers, own_sent)
    mixed_rows = mix(local_a, local_b, query_act, scale, prefix)
    return project_and_reduce(mixed_rows, out_weight)


def solution(mesh):
    ctx_size, tp_size = mesh.devices.shape
    split = Mesh(
        np.asarray(mesh.devices).reshape(ctx_size, tp_size // 2, 2), ("ctx", "ty", "tc")
    )
    tp = ("ty", "tc")
    return jax.shard_map(
        on_device,
        mesh=split,
        in_specs=(
            P("ctx", tp),
            P("ctx", tp),
            P("ctx", tp),
            P("ctx", tp),
            P(tp),
            P(tp, None),
        ),
        out_specs=P(("ctx",) + tp, None),
        check_vma=False,
    )
```

```python
import jax
import jax.numpy as jnp
import numpy as np
from jax import lax
from jax.experimental import pallas as pl
from jax.experimental.pallas import tpu as pltpu
from jax.sharding import Mesh
from jax.sharding import PartitionSpec as P

HD = 128
COLUMN_CHUNKS = 3
QUERY_TILE = 256
ROW_TILE = 256


epsilon = 1e-05


def silu(x):
    x = x.astype(jnp.float32)
    return (x / (1.0 + jnp.exp(-x))).astype(jnp.bfloat16)


def head_block(tokens):
    return pl.BlockSpec((tokens, HD), lambda h: (0, h))


def state_kernel(k_ref, v_ref, state_ref, sent_ref):
    @pl.when(pl.program_id(0) == 0)
    def _():
        state_ref[...] = jnp.zeros_like(state_ref)

    key_act = silu(k_ref[...])
    value_rows = v_ref[...]
    for h in range(state_ref.shape[0]):
        heads = slice(h * HD, (h + 1) * HD)
        state_ref[h] += lax.dot_general(
            key_act[:, heads], value_rows[:, heads], (((0,), (0,)), ((), ())),
            preferred_element_type=jnp.float32,
        )

    @pl.when(pl.program_id(0) == pl.num_programs(0) - 1)
    def _():
        sent_ref[...] = state_ref[...].astype(sent_ref.dtype)


def row_block(columns):
    return pl.BlockSpec((ROW_TILE, columns), lambda i: (i, 0))


def key_value_states(keys, values):
    tokens, columns = keys.shape
    heads = columns // HD
    return pl.pallas_call(
        state_kernel,
        grid=(tokens // ROW_TILE,),
        in_specs=[row_block(columns), row_block(columns)],
        out_specs=[pl.BlockSpec((heads, HD, HD), lambda i: (0, 0, 0))] * 2,
        out_shape=[
            jax.ShapeDtypeStruct((heads, HD, HD), jnp.float32),
            jax.ShapeDtypeStruct((heads, HD, HD), jnp.bfloat16),
        ],
        cost_estimate=pl.CostEstimate(
            flops=2 * tokens * HD * HD * heads,
            transcendentals=tokens * columns,
            bytes_accessed=4 * tokens * columns + 4 * heads * HD * HD,
        ),
    )(keys, values)


def local_kernel(q_ref, k_ref, v_ref, out_ref):
    tokens = q_ref.shape[0]
    query_act = silu(q_ref[...])
    key_act = silu(k_ref[...])
    value_rows = v_ref[...]
    for tile in range(tokens // QUERY_TILE):
        seen = (tile + 1) * QUERY_TILE
        scores = lax.dot_general(
            query_act[tile * QUERY_TILE:seen],
            key_act[:seen],
            (((1,), (1,)), ((), ())),
            preferred_element_type=jnp.float32,
        )
        row = lax.broadcasted_iota(jnp.int32, scores.shape, 0) + tile * QUERY_TILE
        col = lax.broadcasted_iota(jnp.int32, scores.shape, 1)
        scores = jnp.where(row >= col, scores, 0.0).astype(jnp.bfloat16)
        out_ref[tile * QUERY_TILE:seen, :] = jnp.dot(
            scores, value_rows[:seen], preferred_element_type=jnp.float32
        ).astype(out_ref.dtype)


def local_attention(queries, keys, values, first_head, heads):
    tokens, columns = queries.shape
    tiles = tokens // QUERY_TILE
    pairs = QUERY_TILE * QUERY_TILE * tiles * (tiles + 1) // 2
    picked = pl.BlockSpec((tokens, HD), lambda h: (0, h + first_head))
    return pl.pallas_call(
        local_kernel,
        grid=(heads,),
        in_specs=[picked] * 3,
        out_specs=head_block(tokens),
        out_shape=jax.ShapeDtypeStruct((tokens, heads * HD), jnp.bfloat16),
        cost_estimate=pl.CostEstimate(
            flops=4 * pairs * HD * heads,
            transcendentals=2 * tokens * heads * HD,
            bytes_accessed=10 * tokens * heads * HD,
        ),
    )(queries, keys, values)


def gate_kernel(q_ref, g_ref, gain_ref, query_act_ref, scale_ref):
    query_act_ref[...] = silu(q_ref[...])
    gates = g_ref[...].astype(jnp.float32)
    scale_ref[...] = (gain_ref[...] * (1.0 / (1.0 + jnp.exp(-gates)))).astype(scale_ref.dtype)


def query_and_gate(queries, gates, gain):
    tokens, columns = queries.shape
    return pl.pallas_call(
        gate_kernel,
        grid=(tokens // ROW_TILE,),
        in_specs=[row_block(columns), row_block(columns), pl.BlockSpec((1, columns), lambda i: (0, 0))],
        out_specs=[row_block(columns), row_block(columns)],
        out_shape=[
            jax.ShapeDtypeStruct((tokens, columns), jnp.bfloat16),
            jax.ShapeDtypeStruct((tokens, columns), jnp.bfloat16),
        ],
        cost_estimate=pl.CostEstimate(
            flops=8 * tokens * columns,
            transcendentals=2 * tokens * columns,
            bytes_accessed=10 * tokens * columns,
        ),
    )(queries, gates, gain.reshape(1, columns))


def mix_kernel(local_a_ref, local_b_ref, q_ref, scale_ref, prefix_ref, out_ref):
    query_act = q_ref[...]
    first = local_a_ref.shape[1] // HD
    for h in range(prefix_ref.shape[0]):
        heads = slice(h * HD, (h + 1) * HD)
        prefix_hi, prefix_lo = split_bf16(prefix_ref[h])
        if h < first:
            local = local_a_ref[:, heads]
        else:
            local = local_b_ref[:, (h - first) * HD:(h - first + 1) * HD]
        local = local.astype(jnp.float32)
        remote = jnp.dot(query_act[:, heads], prefix_hi, preferred_element_type=jnp.float32) + jnp.dot(
            query_act[:, heads], prefix_lo, preferred_element_type=jnp.float32
        )
        attention = local + remote
        mean_sq = jnp.mean(attention * attention, axis=-1, keepdims=True)
        scale = scale_ref[:, heads].astype(jnp.float32)
        out_ref[:, heads] = (attention * lax.rsqrt(mean_sq + epsilon) * scale).astype(
            out_ref.dtype
        )


def mix(local_a, local_b, query_act, scale, prefix):
    tokens, columns = query_act.shape
    heads = columns // HD
    whole_state = pl.BlockSpec((heads, HD, HD), lambda i: (0, 0, 0))
    return pl.pallas_call(
        mix_kernel,
        grid=(tokens // ROW_TILE,),
        in_specs=[
            row_block(local_a.shape[1]),
            row_block(local_b.shape[1]),
            row_block(columns),
            row_block(columns),
            whole_state,
        ],
        out_specs=row_block(columns),
        out_shape=jax.ShapeDtypeStruct((tokens, columns), jnp.bfloat16),
        cost_estimate=pl.CostEstimate(
            flops=4 * tokens * HD * HD * heads,
            transcendentals=tokens * heads,
            bytes_accessed=12 * tokens * columns,
        ),
    )(local_a, local_b, query_act, scale, prefix)


def split_bf16(x):
    hi = x.astype(jnp.bfloat16)
    lo = (x - hi.astype(jnp.float32)).astype(jnp.bfloat16)
    return hi, lo


def shift(block, axis, distance):
    size = lax.axis_size(axis)
    return lax.ppermute(block, axis, [(i, i + distance) for i in range(size) if i + distance < size])


def swap(block, axis):
    return lax.ppermute(block, axis, [(0, 1), (1, 0)])


def exclusive_prefix(state, axis, fillers=(), sent_first=None):
    inclusive = state
    exclusive = jnp.zeros_like(state)
    distance = 1
    results = []
    while distance < lax.axis_size(axis):
        sent = inclusive.astype(jnp.bfloat16) if distance > 1 or sent_first is None else sent_first
        arrived = shift(sent, axis, distance)
        if len(results) < len(fillers):
            function, operands = fillers[len(results)]
            _, operands = lax.optimization_barrier((sent, operands))
            result = function(*operands)
            arrived, result = lax.optimization_barrier((arrived, result))
            results.append(result)
        arrived = arrived.astype(jnp.float32)
        exclusive = exclusive + arrived
        inclusive = inclusive + arrived
        distance *= 2
    for function, operands in fillers[len(results):]:
        results.append(function(*operands))
    return exclusive, results


def project_and_reduce(mixed_rows, out_weight):
    tokens, columns = mixed_rows.shape
    ty_size = lax.axis_size("ty")
    tc_size = lax.axis_size("tc")
    block = tokens // (ty_size * tc_size)
    width = out_weight.shape[1]

    def product(rows):
        return jnp.dot(rows, out_weight, preferred_element_type=jnp.float32).astype(jnp.bfloat16)

    if ty_size != 2 or tc_size != 2:
        ordered = (
            mixed_rows.reshape(ty_size, tc_size, block, columns)
            .transpose(1, 0, 2, 3)
            .reshape(tokens, columns)
        )
        part = product(ordered)
        part = lax.psum_scatter(part, "tc", scatter_dimension=0, tiled=True)
        return lax.psum_scatter(part, "ty", scatter_dimension=0, tiled=True)

    ty = lax.axis_index("ty")
    tc = lax.axis_index("tc")
    pair = tc_size * block
    far_rows = lax.dynamic_slice_in_dim(mixed_rows, (1 - ty) * pair, pair, axis=0)
    near_rows = lax.dynamic_slice_in_dim(mixed_rows, ty * pair, pair, axis=0)

    def block_of(part, owner_tc):
        return lax.dynamic_slice_in_dim(part, owner_tc * block, block, axis=0)

    partner_part = product(block_of(near_rows, 1 - tc))
    partner_part, far_rows = lax.optimization_barrier((partner_part, far_rows))
    near = swap(partner_part, "tc")
    chunk = width // COLUMN_CHUNKS
    chip_sums = []
    for c in range(COLUMN_CHUNKS):
        far_part = jnp.dot(
            far_rows, out_weight[:, c * chunk:(c + 1) * chunk], preferred_element_type=jnp.float32
        ).astype(jnp.bfloat16)
        from_partner = swap(block_of(far_part, 1 - tc), "tc")
        chip_sum = block_of(far_part, tc).astype(jnp.float32) + from_partner.astype(jnp.float32)
        chip_sums.append(chip_sum.astype(jnp.bfloat16))
    chip_sums, near_rows = lax.optimization_barrier((chip_sums, near_rows))
    across = [swap(chip_sum, "ty") for chip_sum in chip_sums]
    mine = lax.optimization_barrier(product(block_of(near_rows, tc)))
    far = jnp.concatenate(across, axis=1)
    total = mine.astype(jnp.float32) + near.astype(jnp.float32) + far.astype(jnp.float32)
    return total.astype(jnp.bfloat16)


def on_device(queries, keys, values, gates, gain, out_weight):
    own_state, own_sent = key_value_states(keys, values)
    head_count = queries.shape[1] // HD
    first = (head_count + 1) // 2
    fillers = (
        (lambda q, k, v: local_attention(q, k, v, 0, first), (queries, keys, values)),
        (lambda q, k, v: local_attention(q, k, v, first, head_count - first), (queries, keys, values)),
        (query_and_gate, (queries, gates, gain)),
    )
    prefix, (local_a, local_b, (query_act, scale)) = exclusive_prefix(own_state, "ctx", fillers, own_sent)
    mixed_rows = mix(local_a, local_b, query_act, scale, prefix)
    return project_and_reduce(mixed_rows, out_weight)


def solution(mesh):
    ctx_size, tp_size = mesh.devices.shape
    split = Mesh(
        np.asarray(mesh.devices).reshape(ctx_size, tp_size // 2, 2), ("ctx", "ty", "tc")
    )
    tp = ("ty", "tc")
    return jax.shard_map(
        on_device,
        mesh=split,
        in_specs=(
            P("ctx", tp),
            P("ctx", tp),
            P("ctx", tp),
            P("ctx", tp),
            P(tp),
            P(tp, None),
        ),
        out_specs=P(("ctx",) + tp, None),
        check_vma=False,
    )
```

```python
import jax
import jax.numpy as jnp
import numpy as np
from jax import lax
from jax.experimental import pallas as pl
from jax.experimental.pallas import tpu as pltpu
from jax.sharding import Mesh
from jax.sharding import PartitionSpec as P

HD = 128
COLUMN_CHUNKS = 3
QUERY_TILE = 256
ROW_TILE = 256


epsilon = 1e-05


def silu(x):
    x = x.astype(jnp.float32)
    return (x / (1.0 + jnp.exp(-x))).astype(jnp.bfloat16)


def head_block(tokens):
    return pl.BlockSpec((tokens, HD), lambda h: (0, h))


def state_kernel(k_ref, v_ref, state_ref, sent_ref):
    @pl.when(pl.program_id(0) == 0)
    def _():
        state_ref[...] = jnp.zeros_like(state_ref)

    key_act = silu(k_ref[...])
    value_rows = v_ref[...]
    for h in range(state_ref.shape[0]):
        heads = slice(h * HD, (h + 1) * HD)
        state_ref[h] += lax.dot_general(
            key_act[:, heads], value_rows[:, heads], (((0,), (0,)), ((), ())),
            preferred_element_type=jnp.float32,
        )

    @pl.when(pl.program_id(0) == pl.num_programs(0) - 1)
    def _():
        sent_ref[...] = state_ref[...].astype(sent_ref.dtype)


def row_block(columns):
    return pl.BlockSpec((ROW_TILE, columns), lambda i: (i, 0))


def key_value_states(keys, values):
    tokens, columns = keys.shape
    heads = columns // HD
    return pl.pallas_call(
        state_kernel,
        grid=(tokens // ROW_TILE,),
        in_specs=[row_block(columns), row_block(columns)],
        out_specs=[pl.BlockSpec((heads, HD, HD), lambda i: (0, 0, 0))] * 2,
        out_shape=[
            jax.ShapeDtypeStruct((heads, HD, HD), jnp.float32),
            jax.ShapeDtypeStruct((heads, HD, HD), jnp.bfloat16),
        ],
        cost_estimate=pl.CostEstimate(
            flops=2 * tokens * HD * HD * heads,
            transcendentals=tokens * columns,
            bytes_accessed=4 * tokens * columns + 4 * heads * HD * HD,
        ),
    )(keys, values)


def local_kernel(q_ref, k_ref, v_ref, out_ref):
    tokens = q_ref.shape[0]
    query_act = silu(q_ref[...])
    key_act = silu(k_ref[...])
    value_rows = v_ref[...]
    for tile in range(tokens // QUERY_TILE):
        seen = (tile + 1) * QUERY_TILE
        scores = lax.dot_general(
            query_act[tile * QUERY_TILE:seen],
            key_act[:seen],
            (((1,), (1,)), ((), ())),
            preferred_element_type=jnp.float32,
        )
        row = lax.broadcasted_iota(jnp.int32, scores.shape, 0) + tile * QUERY_TILE
        col = lax.broadcasted_iota(jnp.int32, scores.shape, 1)
        scores = jnp.where(row >= col, scores, 0.0).astype(jnp.bfloat16)
        out_ref[tile * QUERY_TILE:seen, :] = jnp.dot(
            scores, value_rows[:seen], preferred_element_type=jnp.float32
        ).astype(out_ref.dtype)


def local_attention(queries, keys, values, first_head, heads):
    tokens, columns = queries.shape
    tiles = tokens // QUERY_TILE
    pairs = QUERY_TILE * QUERY_TILE * tiles * (tiles + 1) // 2
    picked = pl.BlockSpec((tokens, HD), lambda h: (0, h + first_head))
    return pl.pallas_call(
        local_kernel,
        grid=(heads,),
        in_specs=[picked] * 3,
        out_specs=head_block(tokens),
        out_shape=jax.ShapeDtypeStruct((tokens, heads * HD), jnp.bfloat16),
        cost_estimate=pl.CostEstimate(
            flops=4 * pairs * HD * heads,
            transcendentals=2 * tokens * heads * HD,
            bytes_accessed=10 * tokens * heads * HD,
        ),
    )(queries, keys, values)


def gate_kernel(q_ref, g_ref, gain_ref, query_act_ref, scale_ref):
    query_act_ref[...] = silu(q_ref[...])
    gates = g_ref[...].astype(jnp.float32)
    scale_ref[...] = (gain_ref[...] * (1.0 / (1.0 + jnp.exp(-gates)))).astype(scale_ref.dtype)


def query_and_gate(queries, gates, gain):
    tokens, columns = queries.shape
    return pl.pallas_call(
        gate_kernel,
        grid=(tokens // ROW_TILE,),
        in_specs=[row_block(columns), row_block(columns), pl.BlockSpec((1, columns), lambda i: (0, 0))],
        out_specs=[row_block(columns), row_block(columns)],
        out_shape=[
            jax.ShapeDtypeStruct((tokens, columns), jnp.bfloat16),
            jax.ShapeDtypeStruct((tokens, columns), jnp.bfloat16),
        ],
        cost_estimate=pl.CostEstimate(
            flops=8 * tokens * columns,
            transcendentals=2 * tokens * columns,
            bytes_accessed=10 * tokens * columns,
        ),
    )(queries, gates, gain.reshape(1, columns))


def mix_kernel(local_a_ref, local_b_ref, q_ref, scale_ref, prefix_ref, out_ref):
    query_act = q_ref[...]
    first = local_a_ref.shape[1] // HD
    for h in range(prefix_ref.shape[0]):
        heads = slice(h * HD, (h + 1) * HD)
        prefix_hi, prefix_lo = split_bf16(prefix_ref[h])
        if h < first:
            local = local_a_ref[:, heads]
        else:
            local = local_b_ref[:, (h - first) * HD:(h - first + 1) * HD]
        local = local.astype(jnp.float32)
        remote = jnp.dot(query_act[:, heads], prefix_hi, preferred_element_type=jnp.float32) + jnp.dot(
            query_act[:, heads], prefix_lo, preferred_element_type=jnp.float32
        )
        attention = local + remote
        mean_sq = jnp.mean(attention * attention, axis=-1, keepdims=True)
        scale = scale_ref[:, heads].astype(jnp.float32)
        out_ref[:, heads] = (attention * lax.rsqrt(mean_sq + epsilon) * scale).astype(
            out_ref.dtype
        )


def mix(local_a, local_b, query_act, scale, prefix):
    tokens, columns = query_act.shape
    heads = columns // HD
    whole_state = pl.BlockSpec((heads, HD, HD), lambda i: (0, 0, 0))
    return pl.pallas_call(
        mix_kernel,
        grid=(tokens // ROW_TILE,),
        in_specs=[
            row_block(local_a.shape[1]),
            row_block(local_b.shape[1]),
            row_block(columns),
            row_block(columns),
            whole_state,
        ],
        out_specs=row_block(columns),
        out_shape=jax.ShapeDtypeStruct((tokens, columns), jnp.bfloat16),
        cost_estimate=pl.CostEstimate(
            flops=4 * tokens * HD * HD * heads,
            transcendentals=tokens * heads,
            bytes_accessed=12 * tokens * columns,
        ),
    )(local_a, local_b, query_act, scale, prefix)


def split_bf16(x):
    hi = x.astype(jnp.bfloat16)
    lo = (x - hi.astype(jnp.float32)).astype(jnp.bfloat16)
    return hi, lo


def shift(block, axis, distance):
    size = lax.axis_size(axis)
    return lax.ppermute(block, axis, [(i, i + distance) for i in range(size) if i + distance < size])


def swap(block, axis):
    return lax.ppermute(block, axis, [(0, 1), (1, 0)])


def exclusive_prefix(state, axis, fillers=(), sent_first=None):
    inclusive = state
    exclusive = jnp.zeros_like(state)
    distance = 1
    results = []
    while distance < lax.axis_size(axis):
        sent = inclusive.astype(jnp.bfloat16) if distance > 1 or sent_first is None else sent_first
        size = lax.axis_size(axis)
        arrived = lax.ppermute(sent, axis, [(i, (i + distance) % size) for i in range(size)])
        arrived = jnp.where(lax.axis_index(axis) >= distance, arrived, jnp.zeros_like(arrived))
        if len(results) < len(fillers):
            function, operands = fillers[len(results)]
            _, operands = lax.optimization_barrier((sent, operands))
            result = function(*operands)
            arrived, result = lax.optimization_barrier((arrived, result))
            results.append(result)
        arrived = arrived.astype(jnp.float32)
        exclusive = exclusive + arrived
        inclusive = inclusive + arrived
        distance *= 2
    for function, operands in fillers[len(results):]:
        results.append(function(*operands))
    return exclusive, results


def project_and_reduce(mixed_rows, out_weight):
    tokens, columns = mixed_rows.shape
    ty_size = lax.axis_size("ty")
    tc_size = lax.axis_size("tc")
    block = tokens // (ty_size * tc_size)
    width = out_weight.shape[1]

    def product(rows):
        return jnp.dot(rows, out_weight, preferred_element_type=jnp.float32).astype(jnp.bfloat16)

    if ty_size != 2 or tc_size != 2:
        ordered = (
            mixed_rows.reshape(ty_size, tc_size, block, columns)
            .transpose(1, 0, 2, 3)
            .reshape(tokens, columns)
        )
        part = product(ordered)
        part = lax.psum_scatter(part, "tc", scatter_dimension=0, tiled=True)
        return lax.psum_scatter(part, "ty", scatter_dimension=0, tiled=True)

    ty = lax.axis_index("ty")
    tc = lax.axis_index("tc")
    pair = tc_size * block
    far_rows = lax.dynamic_slice_in_dim(mixed_rows, (1 - ty) * pair, pair, axis=0)
    near_rows = lax.dynamic_slice_in_dim(mixed_rows, ty * pair, pair, axis=0)

    def block_of(part, owner_tc):
        return lax.dynamic_slice_in_dim(part, owner_tc * block, block, axis=0)

    chunk = width // COLUMN_CHUNKS
    chip_sums = []
    for c in range(COLUMN_CHUNKS):
        far_part = jnp.dot(
            far_rows, out_weight[:, c * chunk:(c + 1) * chunk], preferred_element_type=jnp.float32
        ).astype(jnp.bfloat16)
        from_partner = swap(block_of(far_part, 1 - tc), "tc")
        chip_sum = block_of(far_part, tc).astype(jnp.float32) + from_partner.astype(jnp.float32)
        chip_sums.append(chip_sum.astype(jnp.bfloat16))
    chip_sums, near_rows = lax.optimization_barrier((chip_sums, near_rows))
    across = [swap(chip_sum, "ty") for chip_sum in chip_sums]
    near = swap(product(block_of(near_rows, 1 - tc)), "tc")
    mine = lax.optimization_barrier(product(block_of(near_rows, tc)))
    far = jnp.concatenate(across, axis=1)
    total = mine.astype(jnp.float32) + near.astype(jnp.float32) + far.astype(jnp.float32)
    return total.astype(jnp.bfloat16)


def on_device(queries, keys, values, gates, gain, out_weight):
    own_state, own_sent = key_value_states(keys, values)
    head_count = queries.shape[1] // HD
    first = (head_count + 1) // 2
    fillers = (
        (lambda q, k, v: local_attention(q, k, v, 0, first), (queries, keys, values)),
        (lambda q, k, v: local_attention(q, k, v, first, head_count - first), (queries, keys, values)),
        (query_and_gate, (queries, gates, gain)),
    )
    prefix, (local_a, local_b, (query_act, scale)) = exclusive_prefix(own_state, "ctx", fillers, own_sent)
    mixed_rows = mix(local_a, local_b, query_act, scale, prefix)
    return project_and_reduce(mixed_rows, out_weight)


def solution(mesh):
    ctx_size, tp_size = mesh.devices.shape
    split = Mesh(
        np.asarray(mesh.devices).reshape(ctx_size, tp_size // 2, 2), ("ctx", "ty", "tc")
    )
    tp = ("ty", "tc")
    return jax.shard_map(
        on_device,
        mesh=split,
        in_specs=(
            P("ctx", tp),
            P("ctx", tp),
            P("ctx", tp),
            P("ctx", tp),
            P(tp),
            P(tp, None),
        ),
        out_specs=P(("ctx",) + tp, None),
        check_vma=False,
    )
```

```python
import jax
import jax.numpy as jnp
import numpy as np
from jax import lax
from jax.experimental import pallas as pl
from jax.experimental.pallas import tpu as pltpu
from jax.sharding import Mesh
from jax.sharding import PartitionSpec as P

HD = 128
COLUMN_CHUNKS = 3
QUERY_TILE = 256
ROW_TILE = 256


epsilon = 1e-05


def silu(x):
    x = x.astype(jnp.float32)
    return (x / (1.0 + jnp.exp(-x))).astype(jnp.bfloat16)


def head_block(tokens):
    return pl.BlockSpec((tokens, HD), lambda h: (0, h))


def state_kernel(k_ref, v_ref, state_ref, sent_ref):
    @pl.when(pl.program_id(0) == 0)
    def _():
        state_ref[...] = jnp.zeros_like(state_ref)

    key_act = silu(k_ref[...])
    value_rows = v_ref[...]
    for h in range(state_ref.shape[0]):
        heads = slice(h * HD, (h + 1) * HD)
        state_ref[h] += lax.dot_general(
            key_act[:, heads], value_rows[:, heads], (((0,), (0,)), ((), ())),
            preferred_element_type=jnp.float32,
        )

    @pl.when(pl.program_id(0) == pl.num_programs(0) - 1)
    def _():
        sent_ref[...] = state_ref[...].astype(sent_ref.dtype)


def row_block(columns):
    return pl.BlockSpec((ROW_TILE, columns), lambda i: (i, 0))


def key_value_states(keys, values):
    tokens, columns = keys.shape
    heads = columns // HD
    return pl.pallas_call(
        state_kernel,
        grid=(tokens // ROW_TILE,),
        in_specs=[row_block(columns), row_block(columns)],
        out_specs=[pl.BlockSpec((heads, HD, HD), lambda i: (0, 0, 0))] * 2,
        out_shape=[
            jax.ShapeDtypeStruct((heads, HD, HD), jnp.float32),
            jax.ShapeDtypeStruct((heads, HD, HD), jnp.bfloat16),
        ],
        cost_estimate=pl.CostEstimate(
            flops=2 * tokens * HD * HD * heads,
            transcendentals=tokens * columns,
            bytes_accessed=4 * tokens * columns + 4 * heads * HD * HD,
        ),
    )(keys, values)


def local_kernel(q_ref, k_ref, v_ref, out_ref, query_act_ref):
    tokens = q_ref.shape[0]
    query_act = silu(q_ref[...])
    query_act_ref[...] = query_act
    key_act = silu(k_ref[...])
    value_rows = v_ref[...]
    for tile in range(tokens // QUERY_TILE):
        seen = (tile + 1) * QUERY_TILE
        scores = lax.dot_general(
            query_act[tile * QUERY_TILE:seen],
            key_act[:seen],
            (((1,), (1,)), ((), ())),
            preferred_element_type=jnp.float32,
        )
        row = lax.broadcasted_iota(jnp.int32, scores.shape, 0) + tile * QUERY_TILE
        col = lax.broadcasted_iota(jnp.int32, scores.shape, 1)
        scores = jnp.where(row >= col, scores, 0.0).astype(jnp.bfloat16)
        out_ref[tile * QUERY_TILE:seen, :] = jnp.dot(
            scores, value_rows[:seen], preferred_element_type=jnp.float32
        ).astype(out_ref.dtype)


def local_attention(queries, keys, values, first_head, heads):
    tokens, columns = queries.shape
    tiles = tokens // QUERY_TILE
    pairs = QUERY_TILE * QUERY_TILE * tiles * (tiles + 1) // 2
    picked = pl.BlockSpec((tokens, HD), lambda h: (0, h + first_head))
    return pl.pallas_call(
        local_kernel,
        grid=(heads,),
        in_specs=[picked] * 3,
        out_specs=[head_block(tokens), head_block(tokens)],
        out_shape=[jax.ShapeDtypeStruct((tokens, heads * HD), jnp.bfloat16)] * 2,
        cost_estimate=pl.CostEstimate(
            flops=4 * pairs * HD * heads,
            transcendentals=2 * tokens * heads * HD,
            bytes_accessed=10 * tokens * heads * HD,
        ),
    )(queries, keys, values)


def gate_kernel(g_ref, gain_ref, scale_ref):
    gates = g_ref[...].astype(jnp.float32)
    scale_ref[...] = (gain_ref[...] * (1.0 / (1.0 + jnp.exp(-gates)))).astype(scale_ref.dtype)


def gate_scale(gates, gain):
    tokens, columns = gates.shape
    return pl.pallas_call(
        gate_kernel,
        grid=(tokens // ROW_TILE,),
        in_specs=[row_block(columns), pl.BlockSpec((1, columns), lambda i: (0, 0))],
        out_specs=row_block(columns),
        out_shape=jax.ShapeDtypeStruct((tokens, columns), jnp.bfloat16),
        cost_estimate=pl.CostEstimate(
            flops=4 * tokens * columns,
            transcendentals=tokens * columns,
            bytes_accessed=4 * tokens * columns,
        ),
    )(gates, gain.reshape(1, columns))


def mix_kernel(local_a_ref, local_b_ref, qa_a_ref, qa_b_ref, scale_ref, prefix_ref, out_ref):
    first = local_a_ref.shape[1] // HD
    for h in range(prefix_ref.shape[0]):
        heads = slice(h * HD, (h + 1) * HD)
        prefix_hi, prefix_lo = split_bf16(prefix_ref[h])
        if h < first:
            local = local_a_ref[:, heads]
            query_act = qa_a_ref[:, heads]
        else:
            local = local_b_ref[:, (h - first) * HD:(h - first + 1) * HD]
            query_act = qa_b_ref[:, (h - first) * HD:(h - first + 1) * HD]
        local = local.astype(jnp.float32)
        remote = jnp.dot(query_act, prefix_hi, preferred_element_type=jnp.float32) + jnp.dot(
            query_act, prefix_lo, preferred_element_type=jnp.float32
        )
        attention = local + remote
        mean_sq = jnp.mean(attention * attention, axis=-1, keepdims=True)
        scale = scale_ref[:, heads].astype(jnp.float32)
        out_ref[:, heads] = (attention * lax.rsqrt(mean_sq + epsilon) * scale).astype(
            out_ref.dtype
        )


def mix(local_a, local_b, qa_a, qa_b, scale, prefix):
    tokens, columns = scale.shape
    heads = columns // HD
    whole_state = pl.BlockSpec((heads, HD, HD), lambda i: (0, 0, 0))
    return pl.pallas_call(
        mix_kernel,
        grid=(tokens // ROW_TILE,),
        in_specs=[
            row_block(local_a.shape[1]),
            row_block(local_b.shape[1]),
            row_block(qa_a.shape[1]),
            row_block(qa_b.shape[1]),
            row_block(columns),
            whole_state,
        ],
        out_specs=row_block(columns),
        out_shape=jax.ShapeDtypeStruct((tokens, columns), jnp.bfloat16),
        cost_estimate=pl.CostEstimate(
            flops=4 * tokens * HD * HD * heads,
            transcendentals=tokens * heads,
            bytes_accessed=12 * tokens * columns,
        ),
    )(local_a, local_b, qa_a, qa_b, scale, prefix)


def split_bf16(x):
    hi = x.astype(jnp.bfloat16)
    lo = (x - hi.astype(jnp.float32)).astype(jnp.bfloat16)
    return hi, lo


def shift(block, axis, distance):
    size = lax.axis_size(axis)
    return lax.ppermute(block, axis, [(i, i + distance) for i in range(size) if i + distance < size])


def swap(block, axis):
    return lax.ppermute(block, axis, [(0, 1), (1, 0)])


def exclusive_prefix(state, axis, fillers=(), sent_first=None):
    inclusive = state
    exclusive = jnp.zeros_like(state)
    distance = 1
    results = []
    while distance < lax.axis_size(axis):
        sent = inclusive.astype(jnp.bfloat16) if distance > 1 or sent_first is None else sent_first
        size = lax.axis_size(axis)
        arrived = lax.ppermute(sent, axis, [(i, (i + distance) % size) for i in range(size)])
        arrived = jnp.where(lax.axis_index(axis) >= distance, arrived, jnp.zeros_like(arrived))
        if len(results) < len(fillers):
            function, operands = fillers[len(results)]
            _, operands = lax.optimization_barrier((sent, operands))
            result = function(*operands)
            arrived, result = lax.optimization_barrier((arrived, result))
            results.append(result)
        arrived = arrived.astype(jnp.float32)
        exclusive = exclusive + arrived
        inclusive = inclusive + arrived
        distance *= 2
    for function, operands in fillers[len(results):]:
        results.append(function(*operands))
    return exclusive, results


def project_and_reduce(mixed_rows, out_weight):
    tokens, columns = mixed_rows.shape
    ty_size = lax.axis_size("ty")
    tc_size = lax.axis_size("tc")
    block = tokens // (ty_size * tc_size)
    width = out_weight.shape[1]

    def product(rows):
        return jnp.dot(rows, out_weight, preferred_element_type=jnp.float32).astype(jnp.bfloat16)

    if ty_size != 2 or tc_size != 2:
        ordered = (
            mixed_rows.reshape(ty_size, tc_size, block, columns)
            .transpose(1, 0, 2, 3)
            .reshape(tokens, columns)
        )
        part = product(ordered)
        part = lax.psum_scatter(part, "tc", scatter_dimension=0, tiled=True)
        return lax.psum_scatter(part, "ty", scatter_dimension=0, tiled=True)

    ty = lax.axis_index("ty")
    tc = lax.axis_index("tc")
    pair = tc_size * block
    far_rows = lax.dynamic_slice_in_dim(mixed_rows, (1 - ty) * pair, pair, axis=0)
    near_rows = lax.dynamic_slice_in_dim(mixed_rows, ty * pair, pair, axis=0)

    def block_of(part, owner_tc):
        return lax.dynamic_slice_in_dim(part, owner_tc * block, block, axis=0)

    chunk = width // COLUMN_CHUNKS
    chip_sums = []
    for c in range(COLUMN_CHUNKS):
        far_part = jnp.dot(
            far_rows, out_weight[:, c * chunk:(c + 1) * chunk], preferred_element_type=jnp.float32
        ).astype(jnp.bfloat16)
        from_partner = swap(block_of(far_part, 1 - tc), "tc")
        chip_sum = block_of(far_part, tc).astype(jnp.float32) + from_partner.astype(jnp.float32)
        chip_sums.append(chip_sum.astype(jnp.bfloat16))
    chip_sums, near_rows = lax.optimization_barrier((chip_sums, near_rows))
    across = [swap(chip_sum, "ty") for chip_sum in chip_sums]
    near = swap(product(block_of(near_rows, 1 - tc)), "tc")
    mine = lax.optimization_barrier(product(block_of(near_rows, tc)))
    far = jnp.concatenate(across, axis=1)
    total = mine.astype(jnp.float32) + near.astype(jnp.float32) + far.astype(jnp.float32)
    return total.astype(jnp.bfloat16)


def on_device(queries, keys, values, gates, gain, out_weight):
    own_state, own_sent = key_value_states(keys, values)
    head_count = queries.shape[1] // HD
    first = (head_count + 1) // 2
    fillers = (
        (lambda q, k, v: local_attention(q, k, v, 0, first), (queries, keys, values)),
        (lambda q, k, v: local_attention(q, k, v, first, head_count - first), (queries, keys, values)),
        (gate_scale, (gates, gain)),
    )
    prefix, ((local_a, qa_a), (local_b, qa_b), scale) = exclusive_prefix(own_state, "ctx", fillers, own_sent)
    mixed_rows = mix(local_a, local_b, qa_a, qa_b, scale, prefix)
    return project_and_reduce(mixed_rows, out_weight)


def solution(mesh):
    ctx_size, tp_size = mesh.devices.shape
    split = Mesh(
        np.asarray(mesh.devices).reshape(ctx_size, tp_size // 2, 2), ("ctx", "ty", "tc")
    )
    tp = ("ty", "tc")
    return jax.shard_map(
        on_device,
        mesh=split,
        in_specs=(
            P("ctx", tp),
            P("ctx", tp),
            P("ctx", tp),
            P("ctx", tp),
            P(tp),
            P(tp, None),
        ),
        out_specs=P(("ctx",) + tp, None),
        check_vma=False,
    )
```

```python
import jax
import jax.numpy as jnp
import numpy as np
from jax import lax
from jax.experimental import pallas as pl
from jax.experimental.pallas import tpu as pltpu
from jax.sharding import Mesh
from jax.sharding import PartitionSpec as P

HD = 128
COLUMN_CHUNKS = 3
QUERY_TILE = 256
ROW_TILE = 512


epsilon = 1e-05


def silu(x):
    x = x.astype(jnp.float32)
    return (x / (1.0 + jnp.exp(-x))).astype(jnp.bfloat16)


def head_block(tokens):
    return pl.BlockSpec((tokens, HD), lambda h: (0, h))


def state_kernel(k_ref, v_ref, state_ref, sent_ref):
    @pl.when(pl.program_id(0) == 0)
    def _():
        state_ref[...] = jnp.zeros_like(state_ref)

    key_act = silu(k_ref[...])
    value_rows = v_ref[...]
    for h in range(state_ref.shape[0]):
        heads = slice(h * HD, (h + 1) * HD)
        state_ref[h] += lax.dot_general(
            key_act[:, heads], value_rows[:, heads], (((0,), (0,)), ((), ())),
            preferred_element_type=jnp.float32,
        )

    @pl.when(pl.program_id(0) == pl.num_programs(0) - 1)
    def _():
        sent_ref[...] = state_ref[...].astype(sent_ref.dtype)


def row_block(columns):
    return pl.BlockSpec((ROW_TILE, columns), lambda i: (i, 0))


def key_value_states(keys, values):
    tokens, columns = keys.shape
    heads = columns // HD
    return pl.pallas_call(
        state_kernel,
        grid=(tokens // ROW_TILE,),
        in_specs=[row_block(columns), row_block(columns)],
        out_specs=[pl.BlockSpec((heads, HD, HD), lambda i: (0, 0, 0))] * 2,
        out_shape=[
            jax.ShapeDtypeStruct((heads, HD, HD), jnp.float32),
            jax.ShapeDtypeStruct((heads, HD, HD), jnp.bfloat16),
        ],
        cost_estimate=pl.CostEstimate(
            flops=2 * tokens * HD * HD * heads,
            transcendentals=tokens * columns,
            bytes_accessed=4 * tokens * columns + 4 * heads * HD * HD,
        ),
    )(keys, values)


def local_kernel(q_ref, k_ref, v_ref, out_ref, query_act_ref):
    tokens = q_ref.shape[0]
    query_act = silu(q_ref[...])
    query_act_ref[...] = query_act
    key_act = silu(k_ref[...])
    value_rows = v_ref[...]
    for tile in range(tokens // QUERY_TILE):
        seen = (tile + 1) * QUERY_TILE
        scores = lax.dot_general(
            query_act[tile * QUERY_TILE:seen],
            key_act[:seen],
            (((1,), (1,)), ((), ())),
            preferred_element_type=jnp.float32,
        )
        row = lax.broadcasted_iota(jnp.int32, scores.shape, 0) + tile * QUERY_TILE
        col = lax.broadcasted_iota(jnp.int32, scores.shape, 1)
        scores = jnp.where(row >= col, scores, 0.0).astype(jnp.bfloat16)
        out_ref[tile * QUERY_TILE:seen, :] = jnp.dot(
            scores, value_rows[:seen], preferred_element_type=jnp.float32
        ).astype(out_ref.dtype)


def local_attention(queries, keys, values, first_head, heads):
    tokens, columns = queries.shape
    tiles = tokens // QUERY_TILE
    pairs = QUERY_TILE * QUERY_TILE * tiles * (tiles + 1) // 2
    picked = pl.BlockSpec((tokens, HD), lambda h: (0, h + first_head))
    return pl.pallas_call(
        local_kernel,
        grid=(heads,),
        in_specs=[picked] * 3,
        out_specs=[head_block(tokens), head_block(tokens)],
        out_shape=[jax.ShapeDtypeStruct((tokens, heads * HD), jnp.bfloat16)] * 2,
        cost_estimate=pl.CostEstimate(
            flops=4 * pairs * HD * heads,
            transcendentals=2 * tokens * heads * HD,
            bytes_accessed=10 * tokens * heads * HD,
        ),
    )(queries, keys, values)


def gate_kernel(g_ref, gain_ref, scale_ref):
    gates = g_ref[...].astype(jnp.float32)
    scale_ref[...] = (gain_ref[...] * (1.0 / (1.0 + jnp.exp(-gates)))).astype(scale_ref.dtype)


def gate_scale(gates, gain):
    tokens, columns = gates.shape
    return pl.pallas_call(
        gate_kernel,
        grid=(tokens // ROW_TILE,),
        in_specs=[row_block(columns), pl.BlockSpec((1, columns), lambda i: (0, 0))],
        out_specs=row_block(columns),
        out_shape=jax.ShapeDtypeStruct((tokens, columns), jnp.bfloat16),
        cost_estimate=pl.CostEstimate(
            flops=4 * tokens * columns,
            transcendentals=tokens * columns,
            bytes_accessed=4 * tokens * columns,
        ),
    )(gates, gain.reshape(1, columns))


def mix_kernel(local_a_ref, local_b_ref, qa_a_ref, qa_b_ref, scale_ref, prefix_ref, out_ref):
    first = local_a_ref.shape[1] // HD
    for h in range(prefix_ref.shape[0]):
        heads = slice(h * HD, (h + 1) * HD)
        prefix_hi, prefix_lo = split_bf16(prefix_ref[h])
        if h < first:
            local = local_a_ref[:, heads]
            query_act = qa_a_ref[:, heads]
        else:
            local = local_b_ref[:, (h - first) * HD:(h - first + 1) * HD]
            query_act = qa_b_ref[:, (h - first) * HD:(h - first + 1) * HD]
        local = local.astype(jnp.float32)
        remote = jnp.dot(query_act, prefix_hi, preferred_element_type=jnp.float32) + jnp.dot(
            query_act, prefix_lo, preferred_element_type=jnp.float32
        )
        attention = local + remote
        mean_sq = jnp.mean(attention * attention, axis=-1, keepdims=True)
        scale = scale_ref[:, heads].astype(jnp.float32)
        out_ref[:, heads] = (attention * lax.rsqrt(mean_sq + epsilon) * scale).astype(
            out_ref.dtype
        )


def mix(local_a, local_b, qa_a, qa_b, scale, prefix):
    tokens, columns = scale.shape
    heads = columns // HD
    whole_state = pl.BlockSpec((heads, HD, HD), lambda i: (0, 0, 0))
    return pl.pallas_call(
        mix_kernel,
        grid=(tokens // ROW_TILE,),
        in_specs=[
            row_block(local_a.shape[1]),
            row_block(local_b.shape[1]),
            row_block(qa_a.shape[1]),
            row_block(qa_b.shape[1]),
            row_block(columns),
            whole_state,
        ],
        out_specs=row_block(columns),
        out_shape=jax.ShapeDtypeStruct((tokens, columns), jnp.bfloat16),
        cost_estimate=pl.CostEstimate(
            flops=4 * tokens * HD * HD * heads,
            transcendentals=tokens * heads,
            bytes_accessed=12 * tokens * columns,
        ),
    )(local_a, local_b, qa_a, qa_b, scale, prefix)


def split_bf16(x):
    hi = x.astype(jnp.bfloat16)
    lo = (x - hi.astype(jnp.float32)).astype(jnp.bfloat16)
    return hi, lo


def shift(block, axis, distance):
    size = lax.axis_size(axis)
    return lax.ppermute(block, axis, [(i, i + distance) for i in range(size) if i + distance < size])


def swap(block, axis):
    return lax.ppermute(block, axis, [(0, 1), (1, 0)])


def exclusive_prefix(state, axis, fillers=(), sent_first=None):
    inclusive = state
    exclusive = jnp.zeros_like(state)
    distance = 1
    results = []
    while distance < lax.axis_size(axis):
        sent = inclusive.astype(jnp.bfloat16) if distance > 1 or sent_first is None else sent_first
        size = lax.axis_size(axis)
        arrived = lax.ppermute(sent, axis, [(i, (i + distance) % size) for i in range(size)])
        arrived = jnp.where(lax.axis_index(axis) >= distance, arrived, jnp.zeros_like(arrived))
        if len(results) < len(fillers):
            function, operands = fillers[len(results)]
            _, operands = lax.optimization_barrier((sent, operands))
            result = function(*operands)
            arrived, result = lax.optimization_barrier((arrived, result))
            results.append(result)
        arrived = arrived.astype(jnp.float32)
        exclusive = exclusive + arrived
        inclusive = inclusive + arrived
        distance *= 2
    for function, operands in fillers[len(results):]:
        results.append(function(*operands))
    return exclusive, results


def project_and_reduce(mixed_rows, out_weight):
    tokens, columns = mixed_rows.shape
    ty_size = lax.axis_size("ty")
    tc_size = lax.axis_size("tc")
    block = tokens // (ty_size * tc_size)
    width = out_weight.shape[1]

    def product(rows):
        return jnp.dot(rows, out_weight, preferred_element_type=jnp.float32).astype(jnp.bfloat16)

    if ty_size != 2 or tc_size != 2:
        ordered = (
            mixed_rows.reshape(ty_size, tc_size, block, columns)
            .transpose(1, 0, 2, 3)
            .reshape(tokens, columns)
        )
        part = product(ordered)
        part = lax.psum_scatter(part, "tc", scatter_dimension=0, tiled=True)
        return lax.psum_scatter(part, "ty", scatter_dimension=0, tiled=True)

    ty = lax.axis_index("ty")
    tc = lax.axis_index("tc")
    pair = tc_size * block
    far_rows = lax.dynamic_slice_in_dim(mixed_rows, (1 - ty) * pair, pair, axis=0)
    near_rows = lax.dynamic_slice_in_dim(mixed_rows, ty * pair, pair, axis=0)

    def block_of(part, owner_tc):
        return lax.dynamic_slice_in_dim(part, owner_tc * block, block, axis=0)

    chunk = width // COLUMN_CHUNKS
    chip_sums = []
    for c in range(COLUMN_CHUNKS):
        far_part = jnp.dot(
            far_rows, out_weight[:, c * chunk:(c + 1) * chunk], preferred_element_type=jnp.float32
        ).astype(jnp.bfloat16)
        from_partner = swap(block_of(far_part, 1 - tc), "tc")
        chip_sum = block_of(far_part, tc).astype(jnp.float32) + from_partner.astype(jnp.float32)
        chip_sums.append(chip_sum.astype(jnp.bfloat16))
    chip_sums, near_rows = lax.optimization_barrier((chip_sums, near_rows))
    across = [swap(chip_sum, "ty") for chip_sum in chip_sums]
    near = swap(product(block_of(near_rows, 1 - tc)), "tc")
    mine = lax.optimization_barrier(product(block_of(near_rows, tc)))
    far = jnp.concatenate(across, axis=1)
    total = mine.astype(jnp.float32) + near.astype(jnp.float32) + far.astype(jnp.float32)
    return total.astype(jnp.bfloat16)


def on_device(queries, keys, values, gates, gain, out_weight):
    own_state, own_sent = key_value_states(keys, values)
    head_count = queries.shape[1] // HD
    first = (head_count + 1) // 2
    fillers = (
        (lambda q, k, v: local_attention(q, k, v, 0, first), (queries, keys, values)),
        (lambda q, k, v: local_attention(q, k, v, first, head_count - first), (queries, keys, values)),
        (gate_scale, (gates, gain)),
    )
    prefix, ((local_a, qa_a), (local_b, qa_b), scale) = exclusive_prefix(own_state, "ctx", fillers, own_sent)
    mixed_rows = mix(local_a, local_b, qa_a, qa_b, scale, prefix)
    return project_and_reduce(mixed_rows, out_weight)


def solution(mesh):
    ctx_size, tp_size = mesh.devices.shape
    split = Mesh(
        np.asarray(mesh.devices).reshape(ctx_size, tp_size // 2, 2), ("ctx", "ty", "tc")
    )
    tp = ("ty", "tc")
    return jax.shard_map(
        on_device,
        mesh=split,
        in_specs=(
            P("ctx", tp),
            P("ctx", tp),
            P("ctx", tp),
            P("ctx", tp),
            P(tp),
            P(tp, None),
        ),
        out_specs=P(("ctx",) + tp, None),
        check_vma=False,
    )
```

```python
import jax
import jax.numpy as jnp
import numpy as np
from jax import lax
from jax.experimental import pallas as pl
from jax.experimental.pallas import tpu as pltpu
from jax.sharding import Mesh
from jax.sharding import PartitionSpec as P

HD = 128
COLUMN_CHUNKS = 3
QUERY_TILE = 256
ROW_TILE = 512


epsilon = 1e-05


def silu(x):
    x = x.astype(jnp.float32)
    return (x / (1.0 + jnp.exp(-x))).astype(jnp.bfloat16)


def head_block(tokens):
    return pl.BlockSpec((tokens, HD), lambda h: (0, h))


def state_kernel(k_ref, v_ref, state_ref, sent_ref):
    @pl.when(pl.program_id(0) == 0)
    def _():
        state_ref[...] = jnp.zeros_like(state_ref)

    key_act = silu(k_ref[...])
    value_rows = v_ref[...]
    for h in range(state_ref.shape[0]):
        heads = slice(h * HD, (h + 1) * HD)
        state_ref[h] += lax.dot_general(
            key_act[:, heads], value_rows[:, heads], (((0,), (0,)), ((), ())),
            preferred_element_type=jnp.float32,
        )

    @pl.when(pl.program_id(0) == pl.num_programs(0) - 1)
    def _():
        sent_ref[...] = state_ref[...].astype(sent_ref.dtype)


def row_block(columns):
    return pl.BlockSpec((ROW_TILE, columns), lambda i: (i, 0))


def key_value_states(keys, values):
    tokens, columns = keys.shape
    heads = columns // HD
    return pl.pallas_call(
        state_kernel,
        grid=(tokens // ROW_TILE,),
        in_specs=[row_block(columns), row_block(columns)],
        out_specs=[pl.BlockSpec((heads, HD, HD), lambda i: (0, 0, 0))] * 2,
        out_shape=[
            jax.ShapeDtypeStruct((heads, HD, HD), jnp.float32),
            jax.ShapeDtypeStruct((heads, HD, HD), jnp.bfloat16),
        ],
        cost_estimate=pl.CostEstimate(
            flops=2 * tokens * HD * HD * heads,
            transcendentals=tokens * columns,
            bytes_accessed=4 * tokens * columns + 4 * heads * HD * HD,
        ),
    )(keys, values)


def local_kernel(q_ref, k_ref, v_ref, out_ref, query_act_ref):
    tokens = q_ref.shape[0]
    query_act = silu(q_ref[...])
    query_act_ref[...] = query_act
    key_act = silu(k_ref[...])
    value_rows = v_ref[...]
    for tile in range(tokens // QUERY_TILE):
        seen = (tile + 1) * QUERY_TILE
        scores = lax.dot_general(
            query_act[tile * QUERY_TILE:seen],
            key_act[:seen],
            (((1,), (1,)), ((), ())),
            preferred_element_type=jnp.float32,
        )
        row = lax.broadcasted_iota(jnp.int32, scores.shape, 0) + tile * QUERY_TILE
        col = lax.broadcasted_iota(jnp.int32, scores.shape, 1)
        scores = jnp.where(row >= col, scores, 0.0).astype(jnp.bfloat16)
        out_ref[tile * QUERY_TILE:seen, :] = jnp.dot(
            scores, value_rows[:seen], preferred_element_type=jnp.float32
        ).astype(out_ref.dtype)


def local_attention(queries, keys, values, first_head, heads):
    tokens, columns = queries.shape
    tiles = tokens // QUERY_TILE
    pairs = QUERY_TILE * QUERY_TILE * tiles * (tiles + 1) // 2
    picked = pl.BlockSpec((tokens, HD), lambda h: (0, h + first_head))
    return pl.pallas_call(
        local_kernel,
        grid=(heads,),
        in_specs=[picked] * 3,
        out_specs=[head_block(tokens), head_block(tokens)],
        out_shape=[jax.ShapeDtypeStruct((tokens, heads * HD), jnp.bfloat16)] * 2,
        cost_estimate=pl.CostEstimate(
            flops=4 * pairs * HD * heads,
            transcendentals=2 * tokens * heads * HD,
            bytes_accessed=10 * tokens * heads * HD,
        ),
    )(queries, keys, values)


def gate_kernel(g_ref, gain_ref, scale_ref):
    gates = g_ref[...].astype(jnp.float32)
    scale_ref[...] = (gain_ref[...] * (1.0 / (1.0 + jnp.exp(-gates)))).astype(scale_ref.dtype)


def gate_scale(gates, gain):
    tokens, columns = gates.shape
    return pl.pallas_call(
        gate_kernel,
        grid=(tokens // ROW_TILE,),
        in_specs=[row_block(columns), pl.BlockSpec((1, columns), lambda i: (0, 0))],
        out_specs=row_block(columns),
        out_shape=jax.ShapeDtypeStruct((tokens, columns), jnp.bfloat16),
        cost_estimate=pl.CostEstimate(
            flops=4 * tokens * columns,
            transcendentals=tokens * columns,
            bytes_accessed=4 * tokens * columns,
        ),
    )(gates, gain.reshape(1, columns))


def mix_kernel(local_a_ref, local_b_ref, qa_a_ref, qa_b_ref, scale_ref, prefix_ref, out_ref):
    first = local_a_ref.shape[1] // HD
    for h in range(prefix_ref.shape[0]):
        heads = slice(h * HD, (h + 1) * HD)
        prefix_hi, prefix_lo = split_bf16(prefix_ref[h])
        if h < first:
            local = local_a_ref[:, heads]
            query_act = qa_a_ref[:, heads]
        else:
            local = local_b_ref[:, (h - first) * HD:(h - first + 1) * HD]
            query_act = qa_b_ref[:, (h - first) * HD:(h - first + 1) * HD]
        local = local.astype(jnp.float32)
        remote = jnp.dot(query_act, prefix_hi, preferred_element_type=jnp.float32) + jnp.dot(
            query_act, prefix_lo, preferred_element_type=jnp.float32
        )
        attention = local + remote
        mean_sq = jnp.mean(attention * attention, axis=-1, keepdims=True)
        scale = scale_ref[:, heads].astype(jnp.float32)
        out_ref[:, heads] = (attention * lax.rsqrt(mean_sq + epsilon) * scale).astype(
            out_ref.dtype
        )


def mix(local_a, local_b, qa_a, qa_b, scale, prefix):
    tokens, columns = scale.shape
    heads = columns // HD
    whole_state = pl.BlockSpec((heads, HD, HD), lambda i: (0, 0, 0))
    return pl.pallas_call(
        mix_kernel,
        grid=(tokens // ROW_TILE,),
        in_specs=[
            row_block(local_a.shape[1]),
            row_block(local_b.shape[1]),
            row_block(qa_a.shape[1]),
            row_block(qa_b.shape[1]),
            row_block(columns),
            whole_state,
        ],
        out_specs=row_block(columns),
        out_shape=jax.ShapeDtypeStruct((tokens, columns), jnp.bfloat16),
        cost_estimate=pl.CostEstimate(
            flops=4 * tokens * HD * HD * heads,
            transcendentals=tokens * heads,
            bytes_accessed=12 * tokens * columns,
        ),
    )(local_a, local_b, qa_a, qa_b, scale, prefix)


def split_bf16(x):
    hi = x.astype(jnp.bfloat16)
    lo = (x - hi.astype(jnp.float32)).astype(jnp.bfloat16)
    return hi, lo


def shift(block, axis, distance):
    size = lax.axis_size(axis)
    return lax.ppermute(block, axis, [(i, i + distance) for i in range(size) if i + distance < size])


def swap(block, axis):
    return lax.ppermute(block, axis, [(0, 1), (1, 0)])


def exclusive_prefix(state, axis, fillers=(), sent_first=None):
    inclusive = state
    exclusive = jnp.zeros_like(state)
    distance = 1
    results = []
    while distance < lax.axis_size(axis):
        sent = inclusive.astype(jnp.bfloat16) if distance > 1 or sent_first is None else sent_first
        size = lax.axis_size(axis)
        arrived = lax.ppermute(sent, axis, [(i, (i + distance) % size) for i in range(size)])
        arrived = jnp.where(lax.axis_index(axis) >= distance, arrived, jnp.zeros_like(arrived))
        if len(results) < len(fillers):
            function, operands = fillers[len(results)]
            _, operands = lax.optimization_barrier((sent, operands))
            result = function(*operands)
            arrived, result = lax.optimization_barrier((arrived, result))
            results.append(result)
        arrived = arrived.astype(jnp.float32)
        exclusive = exclusive + arrived
        inclusive = inclusive + arrived
        distance *= 2
    for function, operands in fillers[len(results):]:
        results.append(function(*operands))
    return exclusive, results


def project_and_reduce(mixed_rows, out_weight):
    tokens, columns = mixed_rows.shape
    ty_size = lax.axis_size("ty")
    tc_size = lax.axis_size("tc")
    block = tokens // (ty_size * tc_size)
    width = out_weight.shape[1]

    def product(rows):
        return jnp.dot(rows, out_weight, preferred_element_type=jnp.float32).astype(jnp.bfloat16)

    if ty_size != 2 or tc_size != 2:
        ordered = (
            mixed_rows.reshape(ty_size, tc_size, block, columns)
            .transpose(1, 0, 2, 3)
            .reshape(tokens, columns)
        )
        part = product(ordered)
        part = lax.psum_scatter(part, "tc", scatter_dimension=0, tiled=True)
        return lax.psum_scatter(part, "ty", scatter_dimension=0, tiled=True)

    ty = lax.axis_index("ty")
    tc = lax.axis_index("tc")
    pair = tc_size * block
    far_rows = lax.dynamic_slice_in_dim(mixed_rows, (1 - ty) * pair, pair, axis=0)
    near_rows = lax.dynamic_slice_in_dim(mixed_rows, ty * pair, pair, axis=0)

    def block_of(part, owner_tc):
        return lax.dynamic_slice_in_dim(part, owner_tc * block, block, axis=0)

    chunk = width // COLUMN_CHUNKS
    chip_sums = []
    for c in range(COLUMN_CHUNKS):
        far_part = jnp.dot(
            far_rows, out_weight[:, c * chunk:(c + 1) * chunk], preferred_element_type=jnp.float32
        ).astype(jnp.bfloat16)
        from_partner = swap(block_of(far_part, 1 - tc), "tc")
        chip_sum = block_of(far_part, tc).astype(jnp.float32) + from_partner.astype(jnp.float32)
        chip_sums.append(chip_sum.astype(jnp.bfloat16))
    chip_sums, near_rows = lax.optimization_barrier((chip_sums, near_rows))
    across = [swap(chip_sum, "ty") for chip_sum in chip_sums]
    near = swap(product(block_of(near_rows, 1 - tc)), "tc")
    mine = lax.optimization_barrier(product(block_of(near_rows, tc)))
    far = jnp.concatenate(across, axis=1)
    own_chip = lax.optimization_barrier(
        (mine.astype(jnp.float32) + near.astype(jnp.float32)).astype(jnp.bfloat16)
    )
    return (own_chip + far.astype(jnp.float32)).astype(jnp.bfloat16)


def on_device(queries, keys, values, gates, gain, out_weight):
    own_state, own_sent = key_value_states(keys, values)
    head_count = queries.shape[1] // HD
    first = (head_count + 1) // 2
    fillers = (
        (lambda q, k, v: local_attention(q, k, v, 0, first), (queries, keys, values)),
        (lambda q, k, v: local_attention(q, k, v, first, head_count - first), (queries, keys, values)),
        (gate_scale, (gates, gain)),
    )
    prefix, ((local_a, qa_a), (local_b, qa_b), scale) = exclusive_prefix(own_state, "ctx", fillers, own_sent)
    mixed_rows = mix(local_a, local_b, qa_a, qa_b, scale, prefix)
    return project_and_reduce(mixed_rows, out_weight)


def solution(mesh):
    ctx_size, tp_size = mesh.devices.shape
    split = Mesh(
        np.asarray(mesh.devices).reshape(ctx_size, tp_size // 2, 2), ("ctx", "ty", "tc")
    )
    tp = ("ty", "tc")
    return jax.shard_map(
        on_device,
        mesh=split,
        in_specs=(
            P("ctx", tp),
            P("ctx", tp),
            P("ctx", tp),
            P("ctx", tp),
            P(tp),
            P(tp, None),
        ),
        out_specs=P(("ctx",) + tp, None),
        check_vma=False,
    )
```

```python
import jax
import jax.numpy as jnp
import numpy as np
from jax import lax
from jax.experimental import pallas as pl
from jax.experimental.pallas import tpu as pltpu
from jax.sharding import Mesh
from jax.sharding import PartitionSpec as P

HD = 128
COLUMN_CHUNKS = 3
QUERY_TILE = 256
ROW_TILE = 1024


epsilon = 1e-05


def silu(x):
    x = x.astype(jnp.float32)
    return (x / (1.0 + jnp.exp(-x))).astype(jnp.bfloat16)


def head_block(tokens):
    return pl.BlockSpec((tokens, HD), lambda h: (0, h))


def state_kernel(k_ref, v_ref, state_ref, sent_ref):
    @pl.when(pl.program_id(0) == 0)
    def _():
        state_ref[...] = jnp.zeros_like(state_ref)

    key_act = silu(k_ref[...])
    value_rows = v_ref[...]
    for h in range(state_ref.shape[0]):
        heads = slice(h * HD, (h + 1) * HD)
        state_ref[h] += lax.dot_general(
            key_act[:, heads], value_rows[:, heads], (((0,), (0,)), ((), ())),
            preferred_element_type=jnp.float32,
        )

    @pl.when(pl.program_id(0) == pl.num_programs(0) - 1)
    def _():
        sent_ref[...] = state_ref[...].astype(sent_ref.dtype)


def row_block(columns):
    return pl.BlockSpec((ROW_TILE, columns), lambda i: (i, 0))


def key_value_states(keys, values):
    tokens, columns = keys.shape
    heads = columns // HD
    return pl.pallas_call(
        state_kernel,
        grid=(tokens // ROW_TILE,),
        in_specs=[row_block(columns), row_block(columns)],
        out_specs=[pl.BlockSpec((heads, HD, HD), lambda i: (0, 0, 0))] * 2,
        out_shape=[
            jax.ShapeDtypeStruct((heads, HD, HD), jnp.float32),
            jax.ShapeDtypeStruct((heads, HD, HD), jnp.bfloat16),
        ],
        cost_estimate=pl.CostEstimate(
            flops=2 * tokens * HD * HD * heads,
            transcendentals=tokens * columns,
            bytes_accessed=4 * tokens * columns + 4 * heads * HD * HD,
        ),
    )(keys, values)


def local_kernel(q_ref, k_ref, v_ref, out_ref, query_act_ref):
    tokens = q_ref.shape[0]
    query_act = silu(q_ref[...])
    query_act_ref[...] = query_act
    key_act = silu(k_ref[...])
    value_rows = v_ref[...]
    for tile in range(tokens // QUERY_TILE):
        seen = (tile + 1) * QUERY_TILE
        scores = lax.dot_general(
            query_act[tile * QUERY_TILE:seen],
            key_act[:seen],
            (((1,), (1,)), ((), ())),
            preferred_element_type=jnp.float32,
        )
        row = lax.broadcasted_iota(jnp.int32, scores.shape, 0) + tile * QUERY_TILE
        col = lax.broadcasted_iota(jnp.int32, scores.shape, 1)
        scores = jnp.where(row >= col, scores, 0.0).astype(jnp.bfloat16)
        out_ref[tile * QUERY_TILE:seen, :] = jnp.dot(
            scores, value_rows[:seen], preferred_element_type=jnp.float32
        ).astype(out_ref.dtype)


def local_attention(queries, keys, values, first_head, heads):
    tokens, columns = queries.shape
    tiles = tokens // QUERY_TILE
    pairs = QUERY_TILE * QUERY_TILE * tiles * (tiles + 1) // 2
    picked = pl.BlockSpec((tokens, HD), lambda h: (0, h + first_head))
    return pl.pallas_call(
        local_kernel,
        grid=(heads,),
        in_specs=[picked] * 3,
        out_specs=[head_block(tokens), head_block(tokens)],
        out_shape=[jax.ShapeDtypeStruct((tokens, heads * HD), jnp.bfloat16)] * 2,
        cost_estimate=pl.CostEstimate(
            flops=4 * pairs * HD * heads,
            transcendentals=2 * tokens * heads * HD,
            bytes_accessed=10 * tokens * heads * HD,
        ),
    )(queries, keys, values)


def gate_kernel(g_ref, gain_ref, scale_ref):
    gates = g_ref[...].astype(jnp.float32)
    scale_ref[...] = (gain_ref[...] * (1.0 / (1.0 + jnp.exp(-gates)))).astype(scale_ref.dtype)


def gate_scale(gates, gain):
    tokens, columns = gates.shape
    return pl.pallas_call(
        gate_kernel,
        grid=(tokens // ROW_TILE,),
        in_specs=[row_block(columns), pl.BlockSpec((1, columns), lambda i: (0, 0))],
        out_specs=row_block(columns),
        out_shape=jax.ShapeDtypeStruct((tokens, columns), jnp.bfloat16),
        cost_estimate=pl.CostEstimate(
            flops=4 * tokens * columns,
            transcendentals=tokens * columns,
            bytes_accessed=4 * tokens * columns,
        ),
    )(gates, gain.reshape(1, columns))


def mix_kernel(local_a_ref, local_b_ref, qa_a_ref, qa_b_ref, scale_ref, prefix_ref, out_ref):
    first = local_a_ref.shape[1] // HD
    for h in range(prefix_ref.shape[0]):
        heads = slice(h * HD, (h + 1) * HD)
        prefix_hi, prefix_lo = split_bf16(prefix_ref[h])
        if h < first:
            local = local_a_ref[:, heads]
            query_act = qa_a_ref[:, heads]
        else:
            local = local_b_ref[:, (h - first) * HD:(h - first + 1) * HD]
            query_act = qa_b_ref[:, (h - first) * HD:(h - first + 1) * HD]
        local = local.astype(jnp.float32)
        remote = jnp.dot(query_act, prefix_hi, preferred_element_type=jnp.float32) + jnp.dot(
            query_act, prefix_lo, preferred_element_type=jnp.float32
        )
        attention = local + remote
        mean_sq = jnp.mean(attention * attention, axis=-1, keepdims=True)
        scale = scale_ref[:, heads].astype(jnp.float32)
        out_ref[:, heads] = (attention * lax.rsqrt(mean_sq + epsilon) * scale).astype(
            out_ref.dtype
        )


def mix(local_a, local_b, qa_a, qa_b, scale, prefix):
    tokens, columns = scale.shape
    heads = columns // HD
    whole_state = pl.BlockSpec((heads, HD, HD), lambda i: (0, 0, 0))
    return pl.pallas_call(
        mix_kernel,
        grid=(tokens // ROW_TILE,),
        in_specs=[
            row_block(local_a.shape[1]),
            row_block(local_b.shape[1]),
            row_block(qa_a.shape[1]),
            row_block(qa_b.shape[1]),
            row_block(columns),
            whole_state,
        ],
        out_specs=row_block(columns),
        out_shape=jax.ShapeDtypeStruct((tokens, columns), jnp.bfloat16),
        cost_estimate=pl.CostEstimate(
            flops=4 * tokens * HD * HD * heads,
            transcendentals=tokens * heads,
            bytes_accessed=12 * tokens * columns,
        ),
    )(local_a, local_b, qa_a, qa_b, scale, prefix)


def split_bf16(x):
    hi = x.astype(jnp.bfloat16)
    lo = (x - hi.astype(jnp.float32)).astype(jnp.bfloat16)
    return hi, lo


def shift(block, axis, distance):
    size = lax.axis_size(axis)
    return lax.ppermute(block, axis, [(i, i + distance) for i in range(size) if i + distance < size])


def swap(block, axis):
    return lax.ppermute(block, axis, [(0, 1), (1, 0)])


def exclusive_prefix(state, axis, fillers=(), sent_first=None):
    inclusive = state
    exclusive = jnp.zeros_like(state)
    distance = 1
    results = []
    while distance < lax.axis_size(axis):
        sent = inclusive.astype(jnp.bfloat16) if distance > 1 or sent_first is None else sent_first
        size = lax.axis_size(axis)
        arrived = lax.ppermute(sent, axis, [(i, (i + distance) % size) for i in range(size)])
        arrived = jnp.where(lax.axis_index(axis) >= distance, arrived, jnp.zeros_like(arrived))
        if len(results) < len(fillers):
            function, operands = fillers[len(results)]
            _, operands = lax.optimization_barrier((sent, operands))
            result = function(*operands)
            arrived, result = lax.optimization_barrier((arrived, result))
            results.append(result)
        arrived = arrived.astype(jnp.float32)
        exclusive = exclusive + arrived
        inclusive = inclusive + arrived
        distance *= 2
    for function, operands in fillers[len(results):]:
        results.append(function(*operands))
    return exclusive, results


def project_and_reduce(mixed_rows, out_weight):
    tokens, columns = mixed_rows.shape
    ty_size = lax.axis_size("ty")
    tc_size = lax.axis_size("tc")
    block = tokens // (ty_size * tc_size)
    width = out_weight.shape[1]

    def product(rows):
        return jnp.dot(rows, out_weight, preferred_element_type=jnp.float32).astype(jnp.bfloat16)

    if ty_size != 2 or tc_size != 2:
        ordered = (
            mixed_rows.reshape(ty_size, tc_size, block, columns)
            .transpose(1, 0, 2, 3)
            .reshape(tokens, columns)
        )
        part = product(ordered)
        part = lax.psum_scatter(part, "tc", scatter_dimension=0, tiled=True)
        return lax.psum_scatter(part, "ty", scatter_dimension=0, tiled=True)

    ty = lax.axis_index("ty")
    tc = lax.axis_index("tc")
    pair = tc_size * block
    far_rows = lax.dynamic_slice_in_dim(mixed_rows, (1 - ty) * pair, pair, axis=0)
    near_rows = lax.dynamic_slice_in_dim(mixed_rows, ty * pair, pair, axis=0)

    def block_of(part, owner_tc):
        return lax.dynamic_slice_in_dim(part, owner_tc * block, block, axis=0)

    chunk = width // COLUMN_CHUNKS
    chip_sums = []
    for c in range(COLUMN_CHUNKS):
        far_part = jnp.dot(
            far_rows, out_weight[:, c * chunk:(c + 1) * chunk], preferred_element_type=jnp.float32
        ).astype(jnp.bfloat16)
        from_partner = swap(block_of(far_part, 1 - tc), "tc")
        chip_sum = block_of(far_part, tc).astype(jnp.float32) + from_partner.astype(jnp.float32)
        chip_sums.append(chip_sum.astype(jnp.bfloat16))
    chip_sums, near_rows = lax.optimization_barrier((chip_sums, near_rows))
    across = [swap(chip_sum, "ty") for chip_sum in chip_sums]
    near = swap(product(block_of(near_rows, 1 - tc)), "tc")
    mine = lax.optimization_barrier(product(block_of(near_rows, tc)))
    far = jnp.concatenate(across, axis=1)
    total = mine.astype(jnp.float32) + near.astype(jnp.float32) + far.astype(jnp.float32)
    return total.astype(jnp.bfloat16)


def on_device(queries, keys, values, gates, gain, out_weight):
    own_state, own_sent = key_value_states(keys, values)
    head_count = queries.shape[1] // HD
    first = (head_count + 1) // 2
    fillers = (
        (lambda q, k, v: local_attention(q, k, v, 0, first), (queries, keys, values)),
        (lambda q, k, v: local_attention(q, k, v, first, head_count - first), (queries, keys, values)),
        (gate_scale, (gates, gain)),
    )
    prefix, ((local_a, qa_a), (local_b, qa_b), scale) = exclusive_prefix(own_state, "ctx", fillers, own_sent)
    mixed_rows = mix(local_a, local_b, qa_a, qa_b, scale, prefix)
    return project_and_reduce(mixed_rows, out_weight)


def solution(mesh):
    ctx_size, tp_size = mesh.devices.shape
    split = Mesh(
        np.asarray(mesh.devices).reshape(ctx_size, tp_size // 2, 2), ("ctx", "ty", "tc")
    )
    tp = ("ty", "tc")
    return jax.shard_map(
        on_device,
        mesh=split,
        in_specs=(
            P("ctx", tp),
            P("ctx", tp),
            P("ctx", tp),
            P("ctx", tp),
            P(tp),
            P(tp, None),
        ),
        out_specs=P(("ctx",) + tp, None),
        check_vma=False,
    )
```

```python
import jax
import jax.numpy as jnp
import numpy as np
from jax import lax
from jax.experimental import pallas as pl
from jax.experimental.pallas import tpu as pltpu
from jax.sharding import Mesh
from jax.sharding import PartitionSpec as P

HD = 128
COLUMN_CHUNKS = 3
QUERY_TILE = 256
ROW_TILE = 512


epsilon = 1e-05


def silu(x):
    x = x.astype(jnp.float32)
    return (x / (1.0 + jnp.exp(-x))).astype(jnp.bfloat16)


def head_block(tokens):
    return pl.BlockSpec((tokens, HD), lambda h: (0, h))


def state_kernel(k_ref, v_ref, state_ref, sent_ref):
    @pl.when(pl.program_id(0) == 0)
    def _():
        state_ref[...] = jnp.zeros_like(state_ref)

    key_act = silu(k_ref[...])
    value_rows = v_ref[...]
    for h in range(state_ref.shape[0]):
        heads = slice(h * HD, (h + 1) * HD)
        state_ref[h] += lax.dot_general(
            key_act[:, heads], value_rows[:, heads], (((0,), (0,)), ((), ())),
            preferred_element_type=jnp.float32,
        )

    @pl.when(pl.program_id(0) == pl.num_programs(0) - 1)
    def _():
        sent_ref[...] = state_ref[...].astype(sent_ref.dtype)


def row_block(columns):
    return pl.BlockSpec((ROW_TILE, columns), lambda i: (i, 0))


def key_value_states(keys, values):
    tokens, columns = keys.shape
    heads = columns // HD
    return pl.pallas_call(
        state_kernel,
        grid=(1,),
        in_specs=[pl.BlockSpec((tokens, columns), lambda i: (0, 0))] * 2,
        out_specs=[pl.BlockSpec((heads, HD, HD), lambda i: (0, 0, 0))] * 2,
        out_shape=[
            jax.ShapeDtypeStruct((heads, HD, HD), jnp.float32),
            jax.ShapeDtypeStruct((heads, HD, HD), jnp.bfloat16),
        ],
        cost_estimate=pl.CostEstimate(
            flops=2 * tokens * HD * HD * heads,
            transcendentals=tokens * columns,
            bytes_accessed=4 * tokens * columns + 4 * heads * HD * HD,
        ),
    )(keys, values)


def local_kernel(q_ref, k_ref, v_ref, out_ref, query_act_ref):
    tokens = q_ref.shape[0]
    query_act = silu(q_ref[...])
    query_act_ref[...] = query_act
    key_act = silu(k_ref[...])
    value_rows = v_ref[...]
    for tile in range(tokens // QUERY_TILE):
        seen = (tile + 1) * QUERY_TILE
        scores = lax.dot_general(
            query_act[tile * QUERY_TILE:seen],
            key_act[:seen],
            (((1,), (1,)), ((), ())),
            preferred_element_type=jnp.float32,
        )
        row = lax.broadcasted_iota(jnp.int32, scores.shape, 0) + tile * QUERY_TILE
        col = lax.broadcasted_iota(jnp.int32, scores.shape, 1)
        scores = jnp.where(row >= col, scores, 0.0).astype(jnp.bfloat16)
        out_ref[tile * QUERY_TILE:seen, :] = jnp.dot(
            scores, value_rows[:seen], preferred_element_type=jnp.float32
        ).astype(out_ref.dtype)


def local_attention(queries, keys, values, first_head, heads):
    tokens, columns = queries.shape
    tiles = tokens // QUERY_TILE
    pairs = QUERY_TILE * QUERY_TILE * tiles * (tiles + 1) // 2
    picked = pl.BlockSpec((tokens, HD), lambda h: (0, h + first_head))
    return pl.pallas_call(
        local_kernel,
        grid=(heads,),
        in_specs=[picked] * 3,
        out_specs=[head_block(tokens), head_block(tokens)],
        out_shape=[jax.ShapeDtypeStruct((tokens, heads * HD), jnp.bfloat16)] * 2,
        cost_estimate=pl.CostEstimate(
            flops=4 * pairs * HD * heads,
            transcendentals=2 * tokens * heads * HD,
            bytes_accessed=10 * tokens * heads * HD,
        ),
    )(queries, keys, values)


def gate_kernel(g_ref, gain_ref, scale_ref):
    gates = g_ref[...].astype(jnp.float32)
    scale_ref[...] = (gain_ref[...] * (1.0 / (1.0 + jnp.exp(-gates)))).astype(scale_ref.dtype)


def gate_scale(gates, gain):
    tokens, columns = gates.shape
    return pl.pallas_call(
        gate_kernel,
        grid=(tokens // ROW_TILE,),
        in_specs=[row_block(columns), pl.BlockSpec((1, columns), lambda i: (0, 0))],
        out_specs=row_block(columns),
        out_shape=jax.ShapeDtypeStruct((tokens, columns), jnp.bfloat16),
        cost_estimate=pl.CostEstimate(
            flops=4 * tokens * columns,
            transcendentals=tokens * columns,
            bytes_accessed=4 * tokens * columns,
        ),
    )(gates, gain.reshape(1, columns))


def mix_kernel(local_a_ref, local_b_ref, qa_a_ref, qa_b_ref, scale_ref, prefix_ref, out_ref):
    first = local_a_ref.shape[1] // HD
    for h in range(prefix_ref.shape[0]):
        heads = slice(h * HD, (h + 1) * HD)
        prefix_hi, prefix_lo = split_bf16(prefix_ref[h])
        if h < first:
            local = local_a_ref[:, heads]
            query_act = qa_a_ref[:, heads]
        else:
            local = local_b_ref[:, (h - first) * HD:(h - first + 1) * HD]
            query_act = qa_b_ref[:, (h - first) * HD:(h - first + 1) * HD]
        local = local.astype(jnp.float32)
        remote = jnp.dot(query_act, prefix_hi, preferred_element_type=jnp.float32) + jnp.dot(
            query_act, prefix_lo, preferred_element_type=jnp.float32
        )
        attention = local + remote
        mean_sq = jnp.mean(attention * attention, axis=-1, keepdims=True)
        scale = scale_ref[:, heads].astype(jnp.float32)
        out_ref[:, heads] = (attention * lax.rsqrt(mean_sq + epsilon) * scale).astype(
            out_ref.dtype
        )


def mix(local_a, local_b, qa_a, qa_b, scale, prefix):
    tokens, columns = scale.shape
    heads = columns // HD
    whole_state = pl.BlockSpec((heads, HD, HD), lambda i: (0, 0, 0))
    return pl.pallas_call(
        mix_kernel,
        grid=(tokens // ROW_TILE,),
        in_specs=[
            row_block(local_a.shape[1]),
            row_block(local_b.shape[1]),
            row_block(qa_a.shape[1]),
            row_block(qa_b.shape[1]),
            row_block(columns),
            whole_state,
        ],
        out_specs=row_block(columns),
        out_shape=jax.ShapeDtypeStruct((tokens, columns), jnp.bfloat16),
        cost_estimate=pl.CostEstimate(
            flops=4 * tokens * HD * HD * heads,
            transcendentals=tokens * heads,
            bytes_accessed=12 * tokens * columns,
        ),
    )(local_a, local_b, qa_a, qa_b, scale, prefix)


def split_bf16(x):
    hi = x.astype(jnp.bfloat16)
    lo = (x - hi.astype(jnp.float32)).astype(jnp.bfloat16)
    return hi, lo


def shift(block, axis, distance):
    size = lax.axis_size(axis)
    return lax.ppermute(block, axis, [(i, i + distance) for i in range(size) if i + distance < size])


def swap(block, axis):
    return lax.ppermute(block, axis, [(0, 1), (1, 0)])


def exclusive_prefix(state, axis, fillers=(), sent_first=None):
    inclusive = state
    exclusive = jnp.zeros_like(state)
    distance = 1
    results = []
    while distance < lax.axis_size(axis):
        sent = inclusive.astype(jnp.bfloat16) if distance > 1 or sent_first is None else sent_first
        size = lax.axis_size(axis)
        arrived = lax.ppermute(sent, axis, [(i, (i + distance) % size) for i in range(size)])
        arrived = jnp.where(lax.axis_index(axis) >= distance, arrived, jnp.zeros_like(arrived))
        if len(results) < len(fillers):
            function, operands = fillers[len(results)]
            _, operands = lax.optimization_barrier((sent, operands))
            result = function(*operands)
            arrived, result = lax.optimization_barrier((arrived, result))
            results.append(result)
        arrived = arrived.astype(jnp.float32)
        exclusive = exclusive + arrived
        inclusive = inclusive + arrived
        distance *= 2
    for function, operands in fillers[len(results):]:
        results.append(function(*operands))
    return exclusive, results


def project_and_reduce(mixed_rows, out_weight):
    tokens, columns = mixed_rows.shape
    ty_size = lax.axis_size("ty")
    tc_size = lax.axis_size("tc")
    block = tokens // (ty_size * tc_size)
    width = out_weight.shape[1]

    def product(rows):
        return jnp.dot(rows, out_weight, preferred_element_type=jnp.float32).astype(jnp.bfloat16)

    if ty_size != 2 or tc_size != 2:
        ordered = (
            mixed_rows.reshape(ty_size, tc_size, block, columns)
            .transpose(1, 0, 2, 3)
            .reshape(tokens, columns)
        )
        part = product(ordered)
        part = lax.psum_scatter(part, "tc", scatter_dimension=0, tiled=True)
        return lax.psum_scatter(part, "ty", scatter_dimension=0, tiled=True)

    ty = lax.axis_index("ty")
    tc = lax.axis_index("tc")
    pair = tc_size * block
    far_rows = lax.dynamic_slice_in_dim(mixed_rows, (1 - ty) * pair, pair, axis=0)
    near_rows = lax.dynamic_slice_in_dim(mixed_rows, ty * pair, pair, axis=0)

    def block_of(part, owner_tc):
        return lax.dynamic_slice_in_dim(part, owner_tc * block, block, axis=0)

    chunk = width // COLUMN_CHUNKS
    chip_sums = []
    for c in range(COLUMN_CHUNKS):
        far_part = jnp.dot(
            far_rows, out_weight[:, c * chunk:(c + 1) * chunk], preferred_element_type=jnp.float32
        ).astype(jnp.bfloat16)
        from_partner = swap(block_of(far_part, 1 - tc), "tc")
        chip_sum = block_of(far_part, tc).astype(jnp.float32) + from_partner.astype(jnp.float32)
        chip_sums.append(chip_sum.astype(jnp.bfloat16))
    chip_sums, near_rows = lax.optimization_barrier((chip_sums, near_rows))
    across = [swap(chip_sum, "ty") for chip_sum in chip_sums]
    near = swap(product(block_of(near_rows, 1 - tc)), "tc")
    mine = lax.optimization_barrier(product(block_of(near_rows, tc)))
    far = jnp.concatenate(across, axis=1)
    total = mine.astype(jnp.float32) + near.astype(jnp.float32) + far.astype(jnp.float32)
    return total.astype(jnp.bfloat16)


def on_device(queries, keys, values, gates, gain, out_weight):
    own_state, own_sent = key_value_states(keys, values)
    head_count = queries.shape[1] // HD
    first = (head_count + 1) // 2
    fillers = (
        (lambda q, k, v: local_attention(q, k, v, 0, first), (queries, keys, values)),
        (lambda q, k, v: local_attention(q, k, v, first, head_count - first), (queries, keys, values)),
        (gate_scale, (gates, gain)),
    )
    prefix, ((local_a, qa_a), (local_b, qa_b), scale) = exclusive_prefix(own_state, "ctx", fillers, own_sent)
    mixed_rows = mix(local_a, local_b, qa_a, qa_b, scale, prefix)
    return project_and_reduce(mixed_rows, out_weight)


def solution(mesh):
    ctx_size, tp_size = mesh.devices.shape
    split = Mesh(
        np.asarray(mesh.devices).reshape(ctx_size, tp_size // 2, 2), ("ctx", "ty", "tc")
    )
    tp = ("ty", "tc")
    return jax.shard_map(
        on_device,
        mesh=split,
        in_specs=(
            P("ctx", tp),
            P("ctx", tp),
            P("ctx", tp),
            P("ctx", tp),
            P(tp),
            P(tp, None),
        ),
        out_specs=P(("ctx",) + tp, None),
        check_vma=False,
    )
```
